32 devices in a mesh: row: 4 (over x, core), col: 8 (over z, y).
Axes of the slice: x: 2, y: 2, z: 4, core: 2. Of those that a mesh axis runs over, the one named last changes fastest.
Arguments:
- particle_phase: float32 [128, 8, 4, 32], P(('row', 'col')), may hold values from -2 to 2
- particle_weight: bfloat16 [128, 8, 32], P(('row', 'col')), may hold values from -4 to 4
- cell_column: int32 [128, 8, 32], P(('row', 'col')), may hold values from 0 to 2047
- cell_depth: int32 [128, 8, 32], P(('row', 'col')), may hold values from 0 to 511
- slot_counts: int32 [128, 8], P(('row', 'col')), may hold values from 8 to 32, as said below
Outputs:
- kicked_momenta: float32 [128, 8, 2, 32], P(('row', 'col'))
- slice_moments: float32 [210, 64], replicated
The draws below stay inside these ranges and needn't reach their ends.
Inputs may be any that keep to these rules, and one draw needn't show every extreme that they name: `slot_counts`: in every draw some pencil receives exactly 32 live slots from every device; an eighth of the pencils receive far more than the others.
All inputs are finite; a program needn't handle non-finite values.
Results may differ from the reference program's by a relative error of at most 0.0003.
Values sent between devices are 32-bit elements; how exact they have to be, the bound alone decides.
No kernel may reach another device: no remote copies, remote signals or barrier semaphores. Data moves between devices by JAX's collectives and lax.ppermute only.
A program may use at most 64 MiB of HBM per device.

```python
import math
import jax
import jax.numpy as jnp
from jax import lax

NX = 256
NY = 256
NZ = 512
SLICES = 64
ORDER = 6
SLOT = 32
PEN_ROWS = 4
PEN_COLS = 8
BINS = 128
CXL = 64
CYL = 32
COLUMNS = 2048
MONO = 210
N_ROW = 4
N_COL = 8


def draw_slot_counts(key, part):
    sources = PEN_ROWS * PEN_COLS
    baseline = jax.random.randint(jax.random.fold_in(key, 11), (sources, sources), SLOT // 4, SLOT // 2 + 1)
    heavy = jax.random.randint(jax.random.fold_in(key, 12), (sources, sources), 3 * SLOT // 4, SLOT + 1)
    shuffled = jax.random.permutation(jax.random.fold_in(key, 13), sources)
    ranking = jnp.zeros((sources,), jnp.int32).at[shuffled].set(jnp.arange(sources, dtype=jnp.int32))
    hot_dest = ranking < max(1, sources // 8)
    full_dest = ranking == 0
    counted = jnp.where(hot_dest[None, :], heavy, baseline)
    counted = jnp.where(full_dest[None, :], SLOT, counted)
    return counted.reshape(sources * PEN_ROWS, PEN_COLS).astype(jnp.int32)


def set_ends(values, stream_key, least, top_value):
    extent = values.shape
    index_at = [jax.random.randint(jax.random.fold_in(stream_key, axis), (), 0, extent[axis]) for axis in range(len(extent))]
    values = values.at[tuple(index_at)].set(least)
    longest = extent.index(max(extent))
    index_at[longest] = (index_at[longest] + 1) % extent[longest]
    return values.at[tuple(index_at)].set(top_value)


def block_levels(stream_key, shape, pieces, least, largest):
    loudness, own = 1.0, jax.random.fold_in(stream_key, 6)
    for dim, blocks in pieces:
        draws = jnp.exp(jax.random.uniform(jax.random.fold_in(own, dim), (blocks,), jnp.float32, least / len(pieces), largest / len(pieces)))
        loudness = loudness * jnp.repeat(draws, shape[dim] // blocks).reshape([-1 if axis == dim else 1 for axis in range(len(shape))])
    return loudness


def centred(rng, dims, width, reach, cuts=(), kind=jnp.bfloat16):
    entries = jax.random.normal(rng, dims, jnp.float32) * width
    if len(cuts) > 0:
        entries = block_levels(rng, dims, cuts, -0.22, 0.18) * entries
    return jnp.clip(entries, min=-reach, max=reach).astype(kind)


def setup_inputs(seed: int = 0) -> dict:
    key_of = jax.random.split(jax.random.key(seed), 6)
    particle_phase = centred(key_of[0], (BINS, PEN_COLS, 4, SLOT), 0.5, 2.0, ((0, 32),), jnp.float32)
    particle_weight = centred(key_of[1], (BINS, PEN_COLS, SLOT), 1.0, 4.0, ((0, 32),))
    cell_column = set_ends(jax.random.randint(key_of[2], (BINS, PEN_COLS, SLOT), 0, COLUMNS), jax.random.fold_in(key_of[2], 1), 0, COLUMNS - 1).astype(jnp.int32)
    cell_depth = set_ends(jax.random.randint(key_of[3], (BINS, PEN_COLS, SLOT), 0, NZ), jax.random.fold_in(key_of[3], 1), 0, NZ - 1).astype(jnp.int32)
    slot_counts = draw_slot_counts(jax.random.fold_in(key_of[5], 71), 0)
    return dict(particle_phase=particle_phase, particle_weight=particle_weight, cell_column=cell_column, cell_depth=cell_depth, slot_counts=slot_counts)


kick_strength = 8.0
epsilon = 1e-06

def exponent_table(max_order):
    listing = []
    for power_one in range(max_order + 1):
        for power_two in range(max_order + 1):
            for power_three in range(max_order + 1):
                for power_four in range(max_order + 1):
                    if power_one + power_two + power_three + power_four <= max_order:
                        listing.append([power_one, power_two, power_three, power_four])
    return listing

def monomials(coords, max_order):
    power_lists = []
    for position in range(4):
        variable = coords[position]
        powers = [jnp.ones_like(variable)]
        for degree in range(max_order):
            powers.append(powers[-1] * variable)
        power_lists.append(powers)
    terms = []
    for entry in exponent_table(max_order):
        product = power_lists[0][entry[0]]
        for position in range(1, 4):
            product = product * power_lists[position][entry[position]]
        terms.append(product)
    return jnp.stack(terms)

def sine_along(grid_field, axis_index):
    rolled = jnp.moveaxis(grid_field, axis_index, -1)
    length = rolled.shape[-1]
    zero_edge = jnp.zeros(rolled.shape[:-1] + (1,), rolled.dtype)
    extended = jnp.concatenate([zero_edge, rolled, zero_edge, -rolled[..., ::-1]], axis=-1)
    spectrum = jnp.fft.rfft(extended, axis=-1)[..., 1:length + 1]
    result = (-jnp.imag(spectrum) * (0.5 * math.sqrt(2.0 / (length + 1)))).astype(grid_field.dtype)
    return jnp.moveaxis(result, -1, axis_index)

def eigen_line(length):
    wave_index = jnp.arange(length, dtype=jnp.float32) + 1.0
    return 2.0 - 2.0 * jnp.cos(wave_index * (math.pi / (length + 1)))

def reference(particle_phase, particle_weight, cell_column, cell_depth, slot_counts):
    slot_count = particle_weight.shape[-1]
    sources = N_ROW * N_COL
    live_slot = jnp.arange(slot_count, dtype=jnp.int32)[None, None, :] < slot_counts[:, :, None]
    live_mass = jnp.where(live_slot, particle_weight.astype(jnp.float32), jnp.float32(0.0))
    dest_row = (jnp.arange(BINS, dtype=jnp.int32) % N_ROW)[:, None, None]
    dest_col = jnp.arange(N_COL, dtype=jnp.int32)[None, :, None]
    cell_x = dest_row * CXL + cell_column // CYL
    cell_y = dest_col * CYL + cell_column % CYL
    flat_cell = ((cell_x * NY + cell_y) * NZ + cell_depth).astype(jnp.int32)
    density = jnp.zeros((NX * NY * NZ,), jnp.float32).at[flat_cell.reshape(-1)].add(live_mass.reshape(-1))
    density = density.reshape(NX, NY, NZ)
    spectrum = sine_along(sine_along(sine_along(density, 2), 1), 0)
    eigen_sum = eigen_line(NX)[:, None, None] + eigen_line(NY)[None, :, None] + eigen_line(NZ)[None, None, :]
    potential = sine_along(sine_along(sine_along(spectrum / eigen_sum, 0), 1), 2)
    padded_x = jnp.pad(potential, ((1, 1), (0, 0), (0, 0)))
    padded_y = jnp.pad(potential, ((0, 0), (1, 1), (0, 0)))
    field_x = -0.5 * (padded_x[2:] - padded_x[:-2])
    field_y = -0.5 * (padded_y[:, 2:] - padded_y[:, :-2])
    field_at_x = field_x.reshape(-1)[flat_cell]
    field_at_y = field_y.reshape(-1)[flat_cell]
    momentum_x = particle_phase[:, :, 1, :] + kick_strength * field_at_x
    momentum_y = particle_phase[:, :, 3, :] + kick_strength * field_at_y
    stacked = jnp.stack([momentum_x, momentum_y], axis=2)
    arranged = stacked.reshape(N_ROW, N_COL, N_ROW, N_COL, 2, slot_count)
    arranged = arranged.transpose(2, 3, 0, 1, 4, 5).reshape(BINS, N_COL, 2, slot_count)
    coord_blocks = (particle_phase[:, :, 0, :].reshape(sources, -1), momentum_x.reshape(sources, -1), particle_phase[:, :, 2, :].reshape(sources, -1), momentum_y.reshape(sources, -1))
    slice_blocks = (cell_depth // (NZ // SLICES)).astype(jnp.int32).reshape(sources, -1)
    mass_blocks = live_mass.reshape(sources, -1)

    def accumulate(running, element):
        coord_one, coord_two, coord_three, coord_four, segment, weight = element
        weighted = monomials([coord_one, coord_two, coord_three, coord_four], ORDER) * weight[None, :]
        segment_totals = jax.ops.segment_sum(weighted.T, segment, num_segments=SLICES)
        squares = jax.ops.segment_sum(weight * weight, segment, num_segments=SLICES)
        return ((running[0] + segment_totals.T, running[1] + squares), None)
    start_state = (jnp.zeros((MONO, SLICES), jnp.float32), jnp.zeros((SLICES,), jnp.float32))
    (moment_sum, square_sum), unused = lax.scan(accumulate, start_state, coord_blocks + (slice_blocks, mass_blocks))
    slice_moments = moment_sum / jnp.sqrt(square_sum + epsilon)[None, :]
    return (arranged, slice_moments)
```

```python
import math

import jax
import jax.numpy as jnp
from jax import lax
from jax.sharding import PartitionSpec as P

NX = 256
NY = 256
NZ = 512
SLICES = 64
ORDER = 6


kick_strength = 8.0
epsilon = 1e-06
highest = lax.Precision.HIGHEST
high = lax.Precision.HIGH


def with_halo(block, sides, width):
    for axis, dim in sides:
        count = lax.axis_size(axis)
        forward = [(i, i + 1) for i in range(count - 1)]
        backward = [(target, source) for source, target in forward]
        low = lax.ppermute(
            lax.slice_in_dim(block, block.shape[dim] - width, None, axis=dim), axis, forward
        )
        high = lax.ppermute(lax.slice_in_dim(block, 0, width, axis=dim), axis, backward)
        block = jnp.concatenate([low, block, high], axis=dim)
    return block


def exponent_table(max_order):
    listing = []
    for power_one in range(max_order + 1):
        for power_two in range(max_order + 1):
            for power_three in range(max_order + 1):
                for power_four in range(max_order + 1):
                    if power_one + power_two + power_three + power_four <= max_order:
                        listing.append([power_one, power_two, power_three, power_four])
    return listing


def monomials(coords, max_order):
    power_lists = []
    for position in range(4):
        variable = coords[position]
        powers = [jnp.ones_like(variable)]
        for degree in range(max_order):
            powers.append(powers[-1] * variable)
        power_lists.append(powers)
    terms = []
    for entry in exponent_table(max_order):
        product = power_lists[0][entry[0]]
        for position in range(1, 4):
            product = product * power_lists[position][entry[position]]
        terms.append(product)
    return jnp.stack(terms)


def wave_grid(length):
    row_wave = lax.broadcasted_iota(jnp.int32, (length, length), 0) + 1
    col_wave = lax.broadcasted_iota(jnp.int32, (length, length), 1) + 1
    reduced = row_wave * col_wave % (2 * (length + 1))
    return (reduced.astype(jnp.float32) * (math.pi / (length + 1)), col_wave)


def sine_table(length):
    angles, col_wave = wave_grid(length)
    return math.sqrt(2.0 / (length + 1)) * jnp.sin(angles)


def eigen_line(length):
    wave_index = lax.broadcasted_iota(jnp.int32, (length,), 0).astype(jnp.float32) + 1.0
    return 2.0 - 2.0 * jnp.cos(wave_index * (math.pi / (length + 1)))


def basis_count(max_order):
    return (max_order + 1) * (max_order + 2) * (max_order + 3) * (max_order + 4) // 24


def lookup_fields(field_x, field_y, column_blocks, depth_blocks):
    columns = field_x.shape[0]
    depth_total = field_x.shape[1]
    table = jnp.concatenate([field_x, field_y], axis=1)
    upper = table.astype(jnp.bfloat16)
    upper_wide = lax.optimization_barrier(upper).astype(jnp.float32)
    lower = (table - upper_wide).astype(jnp.bfloat16)
    column_ids = lax.broadcasted_iota(jnp.int32, (1, columns), 1)
    depth_ids = lax.broadcasted_iota(jnp.int32, (1, depth_total), 1)

    def pick(carry, element):
        block_column, block_depth = element
        picked = (block_column[:, None] == column_ids).astype(jnp.bfloat16)
        rows_found = jnp.dot(picked, upper, preferred_element_type=jnp.float32)
        rows_found = rows_found + jnp.dot(picked, lower, preferred_element_type=jnp.float32)
        chosen = block_depth[:, None] == depth_ids
        value_x = jnp.sum(jnp.where(chosen, rows_found[:, :depth_total], 0.0), axis=1)
        value_y = jnp.sum(jnp.where(chosen, rows_found[:, depth_total:], 0.0), axis=1)
        return (carry, (value_x, value_y))

    unused, (found_x, found_y) = lax.scan(
        pick, jnp.zeros((), jnp.float32), (column_blocks, depth_blocks)
    )
    return (found_x, found_y)


def body(particle_phase, particle_weight, cell_column, cell_depth, slot_counts):
    row_count = lax.axis_size("row")
    col_count = lax.axis_size("col")
    devices = row_count * col_count
    slot_count = particle_weight.shape[-1]
    cells_x = NX // row_count
    cells_y = NY // col_count
    columns = cells_x * cells_y
    layers = NZ // devices
    both = ("row", "col")
    live_slot = lax.broadcasted_iota(jnp.int32, particle_weight.shape, 2) < slot_counts[:, :, None]
    live_mass = jnp.where(live_slot, particle_weight.astype(jnp.float32), 0.0)
    packed = jnp.concatenate(
        [
            particle_phase,
            live_mass[:, :, None, :],
            cell_column.astype(jnp.float32)[:, :, None, :],
            cell_depth.astype(jnp.float32)[:, :, None, :],
        ],
        axis=2,
    ).reshape(devices, 7, slot_count)
    arrived = lax.all_to_all(packed, both, 0, 0, tiled=True)
    phase_in = arrived[:, 0:4, :]
    mass_in = arrived[:, 4, :]
    column_in = arrived[:, 5, :].astype(jnp.int32)
    depth_in = arrived[:, 6, :].astype(jnp.int32)
    sources = devices
    group_size = math.gcd(sources, max(1, 2048 // slot_count))
    step_count = sources // group_size
    block_rows = group_size * slot_count
    column_blocks = column_in.reshape(step_count, block_rows)
    depth_blocks = depth_in.reshape(step_count, block_rows)
    mass_blocks = mass_in.reshape(step_count, block_rows)
    column_ids = lax.broadcasted_iota(jnp.int32, (1, columns), 1)
    depth_ids = lax.broadcasted_iota(jnp.int32, (1, NZ), 1)

    def deposit(running, element):
        block_column, block_depth, block_mass = element
        picked = (block_column[:, None] == column_ids).astype(jnp.bfloat16)
        spread = jnp.where(
            block_depth[:, None] == depth_ids,
            block_mass.astype(jnp.bfloat16)[:, None],
            jnp.zeros((), jnp.bfloat16),
        )
        added = lax.dot_general(
            picked, spread, (((0,), (0,)), ((), ())), preferred_element_type=jnp.float32
        )
        return (running + added, None)

    density, unused = lax.scan(
        deposit, jnp.zeros((columns, NZ), jnp.float32), (column_blocks, depth_blocks, mass_blocks)
    )
    sine_x = sine_table(NX)
    sine_y = sine_table(NY)
    sine_z = sine_table(NZ)
    depth_spectrum = lax.dot_general(sine_z, density, (((0,), (1,)), ((), ())), precision=high)
    slabs = lax.all_to_all(depth_spectrum.reshape(devices, layers, columns), both, 0, 0, tiled=True)
    slab_field = (
        slabs.reshape(row_count, col_count, layers, cells_x, cells_y)
        .transpose(2, 0, 3, 1, 4)
        .reshape(layers, NX, NY)
    )
    mixed = jnp.einsum("zxy,yl->zxl", slab_field, sine_y, precision=high)
    mixed = jnp.einsum("zxl,xk->zkl", mixed, sine_x, precision=high)
    slab_index = lax.axis_index("row") * col_count + lax.axis_index("col")
    depth_wave = slab_index * layers + lax.broadcasted_iota(jnp.int32, (layers,), 0)
    depth_eigen = 2.0 - 2.0 * jnp.cos((depth_wave.astype(jnp.float32) + 1.0) * (math.pi / (NZ + 1)))
    eigen_sum = (
        eigen_line(NX)[None, :, None] + eigen_line(NY)[None, None, :] + depth_eigen[:, None, None]
    )
    scaled = mixed / eigen_sum
    potential = jnp.einsum("zkl,xk->zxl", scaled, sine_x, precision=high)
    potential = jnp.einsum("zxl,yl->zxy", potential, sine_y, precision=high)
    outgoing = (
        potential.reshape(layers, row_count, cells_x, col_count, cells_y)
        .transpose(1, 3, 0, 2, 4)
        .reshape(devices, layers, columns)
    )
    returned = lax.all_to_all(outgoing, both, 0, 0, tiled=True)
    line_field = lax.dot_general(
        returned.reshape(NZ, columns), sine_z, (((0,), (0,)), ((), ())), precision=high
    )
    padded = with_halo(line_field.reshape(cells_x, cells_y, NZ), (("row", 0), ("col", 1)), 1)
    field_x = (-0.5 * (padded[2:, 1:-1] - padded[:-2, 1:-1])).reshape(columns, NZ)
    field_y = (-0.5 * (padded[1:-1, 2:] - padded[1:-1, :-2])).reshape(columns, NZ)
    found_x, found_y = lookup_fields(field_x, field_y, column_blocks, depth_blocks)
    momentum_x = phase_in[:, 1, :] + kick_strength * found_x.reshape(sources, slot_count)
    momentum_y = phase_in[:, 3, :] + kick_strength * found_y.reshape(sources, slot_count)
    kicked = jnp.stack([momentum_x, momentum_y], axis=1).reshape(
        row_count, col_count, 2, slot_count
    )
    coord_blocks = (
        phase_in[:, 0, :].reshape(step_count, block_rows),
        momentum_x.reshape(step_count, block_rows),
        phase_in[:, 2, :].reshape(step_count, block_rows),
        momentum_y.reshape(step_count, block_rows),
    )
    slice_blocks = (depth_in // (NZ // SLICES)).reshape(step_count, block_rows)
    slice_ids = lax.broadcasted_iota(jnp.int32, (1, SLICES), 1)

    def gather_moments(running, element):
        coord_one, coord_two, coord_three, coord_four, block_slice, block_mass = element
        weighted_slices = jnp.where(block_slice[:, None] == slice_ids, block_mass[:, None], 0.0)
        basis = monomials([coord_one, coord_two, coord_three, coord_four], ORDER)
        moment_part = jnp.dot(
            basis, weighted_slices, precision=highest, preferred_element_type=jnp.float32
        )
        square_part = jnp.sum(weighted_slices * block_mass[:, None], axis=0)
        return ((running[0] + moment_part, running[1] + square_part), None)

    start_state = (
        jnp.zeros((basis_count(ORDER), SLICES), jnp.float32),
        jnp.zeros((SLICES,), jnp.float32),
    )
    (moment_sum, square_sum), unused_too = lax.scan(
        gather_moments, start_state, coord_blocks + (slice_blocks, mass_blocks)
    )
    totals = lax.psum(jnp.concatenate([moment_sum, square_sum[None, :]], axis=0), both)
    moment_total = totals[:-1]
    square_total = totals[-1]
    slice_moments = moment_total / jnp.sqrt(square_total + epsilon)[None, :]
    return (kicked, slice_moments)


def momentum_shape(phase_in):
    return (phase_in.shape[0], phase_in.shape[1], phase_in.shape[3])


def solution(mesh):
    placed = (
        P(("row", "col"), None, None, None),
        P(("row", "col"), None, None),
        P(("row", "col"), None, None),
        P(("row", "col"), None, None),
        P(("row", "col"), None),
    )
    return jax.shard_map(
        body,
        mesh=mesh,
        in_specs=placed,
        out_specs=(P(("row", "col"), None, None, None), P()),
        check_vma=False,
    )
```

```python
import math

import jax
import jax.numpy as jnp
from jax import lax
from jax.sharding import PartitionSpec as P

NX = 256
NY = 256
NZ = 512
SLICES = 64
ORDER = 6


kick_strength = 8.0
epsilon = 1e-06
highest = lax.Precision.HIGHEST
high = lax.Precision.HIGH


def with_halo(block, sides, width):
    for axis, dim in sides:
        count = lax.axis_size(axis)
        forward = [(i, i + 1) for i in range(count - 1)]
        backward = [(target, source) for source, target in forward]
        low = lax.ppermute(
            lax.slice_in_dim(block, block.shape[dim] - width, None, axis=dim), axis, forward
        )
        high = lax.ppermute(lax.slice_in_dim(block, 0, width, axis=dim), axis, backward)
        block = jnp.concatenate([low, block, high], axis=dim)
    return block


def exponent_table(max_order):
    listing = []
    for power_one in range(max_order + 1):
        for power_two in range(max_order + 1):
            for power_three in range(max_order + 1):
                for power_four in range(max_order + 1):
                    if power_one + power_two + power_three + power_four <= max_order:
                        listing.append([power_one, power_two, power_three, power_four])
    return listing


def monomials(coords, max_order):
    power_lists = []
    for position in range(4):
        variable = coords[position]
        powers = [jnp.ones_like(variable)]
        for degree in range(max_order):
            powers.append(powers[-1] * variable)
        power_lists.append(powers)
    terms = []
    for entry in exponent_table(max_order):
        product = power_lists[0][entry[0]]
        for position in range(1, 4):
            product = product * power_lists[position][entry[position]]
        terms.append(product)
    return jnp.stack(terms)


def wave_grid(length):
    row_wave = lax.broadcasted_iota(jnp.int32, (length, length), 0) + 1
    col_wave = lax.broadcasted_iota(jnp.int32, (length, length), 1) + 1
    reduced = row_wave * col_wave % (2 * (length + 1))
    return (reduced.astype(jnp.float32) * (math.pi / (length + 1)), col_wave)


def sine_table(length):
    angles, col_wave = wave_grid(length)
    return math.sqrt(2.0 / (length + 1)) * jnp.sin(angles)


def eigen_line(length):
    wave_index = lax.broadcasted_iota(jnp.int32, (length,), 0).astype(jnp.float32) + 1.0
    return 2.0 - 2.0 * jnp.cos(wave_index * (math.pi / (length + 1)))


def basis_count(max_order):
    return (max_order + 1) * (max_order + 2) * (max_order + 3) * (max_order + 4) // 24


def lookup_fields(field_x, field_y, column_blocks, depth_blocks):
    columns = field_x.shape[0]
    depth_total = field_x.shape[1]
    table = jnp.concatenate([field_x, field_y], axis=1)
    upper = table.astype(jnp.bfloat16)
    upper_wide = lax.optimization_barrier(upper).astype(jnp.float32)
    lower = (table - upper_wide).astype(jnp.bfloat16)
    column_ids = lax.broadcasted_iota(jnp.int32, (1, columns), 1)
    depth_ids = lax.broadcasted_iota(jnp.int32, (1, depth_total), 1)

    def pick(carry, element):
        block_column, block_depth = element
        picked = (block_column[:, None] == column_ids).astype(jnp.bfloat16)
        rows_found = jnp.dot(picked, upper, preferred_element_type=jnp.float32)
        rows_found = rows_found + jnp.dot(picked, lower, preferred_element_type=jnp.float32)
        chosen = block_depth[:, None] == depth_ids
        value_x = jnp.sum(jnp.where(chosen, rows_found[:, :depth_total], 0.0), axis=1)
        value_y = jnp.sum(jnp.where(chosen, rows_found[:, depth_total:], 0.0), axis=1)
        return (carry, (value_x, value_y))

    unused, (found_x, found_y) = lax.scan(
        pick, jnp.zeros((), jnp.float32), (column_blocks, depth_blocks)
    )
    return (found_x, found_y)


def body(particle_phase, particle_weight, cell_column, cell_depth, slot_counts):
    row_count = lax.axis_size("row")
    col_count = lax.axis_size("col")
    devices = row_count * col_count
    slot_count = particle_weight.shape[-1]
    cells_x = NX // row_count
    cells_y = NY // col_count
    columns = cells_x * cells_y
    layers = NZ // devices
    both = ("row", "col")
    live_slot = lax.broadcasted_iota(jnp.int32, particle_weight.shape, 2) < slot_counts[:, :, None]
    live_mass = jnp.where(live_slot, particle_weight.astype(jnp.float32), 0.0)
    packed = jnp.concatenate(
        [
            particle_phase,
            live_mass[:, :, None, :],
            cell_column.astype(jnp.float32)[:, :, None, :],
            cell_depth.astype(jnp.float32)[:, :, None, :],
        ],
        axis=2,
    ).reshape(devices, 7, slot_count)
    arrived = lax.all_to_all(packed, both, 0, 0, tiled=True)
    phase_in = arrived[:, 0:4, :]
    mass_in = arrived[:, 4, :]
    column_in = arrived[:, 5, :].astype(jnp.int32)
    depth_in = arrived[:, 6, :].astype(jnp.int32)
    sources = devices
    group_size = math.gcd(sources, max(1, 2048 // slot_count))
    step_count = sources // group_size
    block_rows = group_size * slot_count
    column_blocks = column_in.reshape(step_count, block_rows)
    depth_blocks = depth_in.reshape(step_count, block_rows)
    mass_blocks = mass_in.reshape(step_count, block_rows)
    column_ids = lax.broadcasted_iota(jnp.int32, (1, columns), 1)
    depth_ids = lax.broadcasted_iota(jnp.int32, (1, NZ), 1)

    def deposit(running, element):
        block_column, block_depth, block_mass = element
        picked = (block_column[:, None] == column_ids).astype(jnp.bfloat16)
        spread = jnp.where(
            block_depth[:, None] == depth_ids,
            block_mass.astype(jnp.bfloat16)[:, None],
            jnp.zeros((), jnp.bfloat16),
        )
        added = lax.dot_general(
            picked, spread, (((0,), (0,)), ((), ())), preferred_element_type=jnp.float32
        )
        return (running + added, None)

    density, unused = lax.scan(
        deposit, jnp.zeros((columns, NZ), jnp.float32), (column_blocks, depth_blocks, mass_blocks)
    )
    sine_x = sine_table(NX)
    sine_y = sine_table(NY)
    sine_z = sine_table(NZ)
    chunk_count = 2 if layers % 2 == 0 else 1
    chunk_layers = layers // chunk_count
    slab_index = lax.axis_index("row") * col_count + lax.axis_index("col")
    sine_z_slabs = sine_z.reshape(NZ, devices, layers)
    line_field = jnp.zeros((columns, NZ), jnp.float32)
    for chunk in range(chunk_count):
        lower_layer = chunk * chunk_layers
        sine_z_part = sine_z_slabs[:, :, lower_layer : lower_layer + chunk_layers]
        depth_spectrum = lax.dot_general(
            sine_z_part, density, (((0,), (1,)), ((), ())), precision=high
        )
        slabs = lax.all_to_all(depth_spectrum, both, 0, 0, tiled=True)
        slab_field = (
            slabs.reshape(row_count, col_count, chunk_layers, cells_x, cells_y)
            .transpose(2, 0, 3, 1, 4)
            .reshape(chunk_layers, NX, NY)
        )
        mixed = jnp.einsum("zxy,yl->zxl", slab_field, sine_y, precision=high)
        mixed = jnp.einsum("zxl,xk->zkl", mixed, sine_x, precision=high)
        depth_wave = (
            slab_index * layers
            + lower_layer
            + lax.broadcasted_iota(jnp.int32, (chunk_layers,), 0)
        )
        depth_eigen = 2.0 - 2.0 * jnp.cos(
            (depth_wave.astype(jnp.float32) + 1.0) * (math.pi / (NZ + 1))
        )
        eigen_sum = (
            eigen_line(NX)[None, :, None]
            + eigen_line(NY)[None, None, :]
            + depth_eigen[:, None, None]
        )
        scaled = mixed / eigen_sum
        potential = jnp.einsum("zkl,xk->zxl", scaled, sine_x, precision=high)
        potential = jnp.einsum("zxl,yl->zxy", potential, sine_y, precision=high)
        outgoing = (
            potential.reshape(chunk_layers, row_count, cells_x, col_count, cells_y)
            .transpose(1, 3, 0, 2, 4)
            .reshape(devices, chunk_layers, columns)
        )
        returned = lax.all_to_all(outgoing, both, 0, 0, tiled=True)
        line_field = line_field + lax.dot_general(
            returned, sine_z_part, (((0, 1), (1, 2)), ((), ())), precision=high
        )
    padded = with_halo(line_field.reshape(cells_x, cells_y, NZ), (("row", 0), ("col", 1)), 1)
    field_x = (-0.5 * (padded[2:, 1:-1] - padded[:-2, 1:-1])).reshape(columns, NZ)
    field_y = (-0.5 * (padded[1:-1, 2:] - padded[1:-1, :-2])).reshape(columns, NZ)
    found_x, found_y = lookup_fields(field_x, field_y, column_blocks, depth_blocks)
    momentum_x = phase_in[:, 1, :] + kick_strength * found_x.reshape(sources, slot_count)
    momentum_y = phase_in[:, 3, :] + kick_strength * found_y.reshape(sources, slot_count)
    kicked = jnp.stack([momentum_x, momentum_y], axis=1).reshape(
        row_count, col_count, 2, slot_count
    )
    coord_blocks = (
        phase_in[:, 0, :].reshape(step_count, block_rows),
        momentum_x.reshape(step_count, block_rows),
        phase_in[:, 2, :].reshape(step_count, block_rows),
        momentum_y.reshape(step_count, block_rows),
    )
    slice_blocks = (depth_in // (NZ // SLICES)).reshape(step_count, block_rows)
    slice_ids = lax.broadcasted_iota(jnp.int32, (1, SLICES), 1)

    def gather_moments(running, element):
        coord_one, coord_two, coord_three, coord_four, block_slice, block_mass = element
        weighted_slices = jnp.where(block_slice[:, None] == slice_ids, block_mass[:, None], 0.0)
        basis = monomials([coord_one, coord_two, coord_three, coord_four], ORDER)
        moment_part = jnp.dot(
            basis, weighted_slices, precision=highest, preferred_element_type=jnp.float32
        )
        square_part = jnp.sum(weighted_slices * block_mass[:, None], axis=0)
        return ((running[0] + moment_part, running[1] + square_part), None)

    start_state = (
        jnp.zeros((basis_count(ORDER), SLICES), jnp.float32),
        jnp.zeros((SLICES,), jnp.float32),
    )
    (moment_sum, square_sum), unused_too = lax.scan(
        gather_moments, start_state, coord_blocks + (slice_blocks, mass_blocks)
    )
    flat_totals = jnp.concatenate([moment_sum.reshape(-1), square_sum])
    totals = lax.psum(flat_totals, both)
    moment_total = totals[:-SLICES].reshape(moment_sum.shape)
    square_total = totals[-SLICES:]
    slice_moments = moment_total / jnp.sqrt(square_total + epsilon)[None, :]
    return (kicked, slice_moments)


def momentum_shape(phase_in):
    return (phase_in.shape[0], phase_in.shape[1], phase_in.shape[3])


def solution(mesh):
    placed = (
        P(("row", "col"), None, None, None),
        P(("row", "col"), None, None),
        P(("row", "col"), None, None),
        P(("row", "col"), None, None),
        P(("row", "col"), None),
    )
    return jax.shard_map(
        body,
        mesh=mesh,
        in_specs=placed,
        out_specs=(P(("row", "col"), None, None, None), P()),
        check_vma=False,
    )
```

```python
import math

import jax
import jax.numpy as jnp
from jax import lax
from jax.sharding import PartitionSpec as P

NX = 256
NY = 256
NZ = 512
SLICES = 64
ORDER = 6


kick_strength = 8.0
epsilon = 1e-06
highest = lax.Precision.HIGHEST
high = lax.Precision.HIGH


def with_halo(block, sides, width):
    for axis, dim in sides:
        count = lax.axis_size(axis)
        forward = [(i, i + 1) for i in range(count - 1)]
        backward = [(target, source) for source, target in forward]
        low = lax.ppermute(
            lax.slice_in_dim(block, block.shape[dim] - width, None, axis=dim), axis, forward
        )
        high = lax.ppermute(lax.slice_in_dim(block, 0, width, axis=dim), axis, backward)
        block = jnp.concatenate([low, block, high], axis=dim)
    return block


def exponent_table(max_order):
    listing = []
    for power_one in range(max_order + 1):
        for power_two in range(max_order + 1):
            for power_three in range(max_order + 1):
                for power_four in range(max_order + 1):
                    if power_one + power_two + power_three + power_four <= max_order:
                        listing.append([power_one, power_two, power_three, power_four])
    return listing


def monomials(coords, max_order):
    power_lists = []
    for position in range(4):
        variable = coords[position]
        powers = [jnp.ones_like(variable)]
        for degree in range(max_order):
            powers.append(powers[-1] * variable)
        power_lists.append(powers)
    terms = []
    for entry in exponent_table(max_order):
        product = power_lists[0][entry[0]]
        for position in range(1, 4):
            product = product * power_lists[position][entry[position]]
        terms.append(product)
    return jnp.stack(terms)


def wave_grid(length):
    row_wave = lax.broadcasted_iota(jnp.int32, (length, length), 0) + 1
    col_wave = lax.broadcasted_iota(jnp.int32, (length, length), 1) + 1
    reduced = row_wave * col_wave % (2 * (length + 1))
    return (reduced.astype(jnp.float32) * (math.pi / (length + 1)), col_wave)


def sine_table(length):
    angles, col_wave = wave_grid(length)
    return math.sqrt(2.0 / (length + 1)) * jnp.sin(angles)


def eigen_line(length):
    wave_index = lax.broadcasted_iota(jnp.int32, (length,), 0).astype(jnp.float32) + 1.0
    return 2.0 - 2.0 * jnp.cos(wave_index * (math.pi / (length + 1)))


def basis_count(max_order):
    return (max_order + 1) * (max_order + 2) * (max_order + 3) * (max_order + 4) // 24


def lookup_fields(field_x, field_y, column_blocks, depth_blocks):
    columns = field_x.shape[0]
    depth_total = field_x.shape[1]
    table = jnp.concatenate([field_x, field_y], axis=1)
    upper = table.astype(jnp.bfloat16)
    upper_wide = lax.optimization_barrier(upper).astype(jnp.float32)
    lower = (table - upper_wide).astype(jnp.bfloat16)
    column_ids = lax.broadcasted_iota(jnp.int32, (1, columns), 1)
    depth_ids = lax.broadcasted_iota(jnp.int32, (1, depth_total), 1)

    def pick(carry, element):
        block_column, block_depth = element
        picked = (block_column[:, None] == column_ids).astype(jnp.bfloat16)
        rows_found = jnp.dot(picked, upper, preferred_element_type=jnp.float32)
        rows_found = rows_found + jnp.dot(picked, lower, preferred_element_type=jnp.float32)
        chosen = block_depth[:, None] == depth_ids
        value_x = jnp.sum(jnp.where(chosen, rows_found[:, :depth_total], 0.0), axis=1)
        value_y = jnp.sum(jnp.where(chosen, rows_found[:, depth_total:], 0.0), axis=1)
        return (carry, (value_x, value_y))

    unused, (found_x, found_y) = lax.scan(
        pick, jnp.zeros((), jnp.float32), (column_blocks, depth_blocks)
    )
    return (found_x, found_y)


def body(particle_phase, particle_weight, cell_column, cell_depth, slot_counts):
    row_count = lax.axis_size("row")
    col_count = lax.axis_size("col")
    devices = row_count * col_count
    slot_count = particle_weight.shape[-1]
    cells_x = NX // row_count
    cells_y = NY // col_count
    columns = cells_x * cells_y
    layers = NZ // devices
    both = ("row", "col")
    live_slot = lax.broadcasted_iota(jnp.int32, particle_weight.shape, 2) < slot_counts[:, :, None]
    live_mass = jnp.where(live_slot, particle_weight.astype(jnp.float32), 0.0)
    packed = jnp.concatenate(
        [
            particle_phase,
            live_mass[:, :, None, :],
            cell_column.astype(jnp.float32)[:, :, None, :],
            cell_depth.astype(jnp.float32)[:, :, None, :],
        ],
        axis=2,
    ).reshape(devices, 7, slot_count)
    arrived = lax.all_to_all(packed, both, 0, 0, tiled=True)
    phase_in = arrived[:, 0:4, :]
    mass_in = arrived[:, 4, :]
    column_in = arrived[:, 5, :].astype(jnp.int32)
    depth_in = arrived[:, 6, :].astype(jnp.int32)
    sources = devices
    group_size = math.gcd(sources, max(1, 2048 // slot_count))
    step_count = sources // group_size
    block_rows = group_size * slot_count
    column_blocks = column_in.reshape(step_count, block_rows)
    depth_blocks = depth_in.reshape(step_count, block_rows)
    mass_blocks = mass_in.reshape(step_count, block_rows)
    column_ids = lax.broadcasted_iota(jnp.int32, (1, columns), 1)
    depth_ids = lax.broadcasted_iota(jnp.int32, (1, NZ), 1)

    def deposit(running, element):
        block_column, block_depth, block_mass = element
        picked = (block_column[:, None] == column_ids).astype(jnp.bfloat16)
        spread = jnp.where(
            block_depth[:, None] == depth_ids,
            block_mass.astype(jnp.bfloat16)[:, None],
            jnp.zeros((), jnp.bfloat16),
        )
        added = lax.dot_general(
            picked, spread, (((0,), (0,)), ((), ())), preferred_element_type=jnp.float32
        )
        return (running + added, None)

    density, unused = lax.scan(
        deposit, jnp.zeros((columns, NZ), jnp.float32), (column_blocks, depth_blocks, mass_blocks)
    )
    sine_x = sine_table(NX)
    sine_y = sine_table(NY)
    sine_z = sine_table(NZ)
    chunk_count = 4 if layers % 4 == 0 else 1
    chunk_layers = layers // chunk_count
    slab_index = lax.axis_index("row") * col_count + lax.axis_index("col")
    sine_z_slabs = sine_z.reshape(NZ, devices, layers)
    line_field = jnp.zeros((columns, NZ), jnp.float32)
    for chunk in range(chunk_count):
        lower_layer = chunk * chunk_layers
        sine_z_part = sine_z_slabs[:, :, lower_layer : lower_layer + chunk_layers]
        depth_spectrum = lax.dot_general(
            sine_z_part, density, (((0,), (1,)), ((), ())), precision=high
        )
        slabs = lax.all_to_all(depth_spectrum, both, 0, 0, tiled=True)
        slab_field = (
            slabs.reshape(row_count, col_count, chunk_layers, cells_x, cells_y)
            .transpose(2, 0, 3, 1, 4)
            .reshape(chunk_layers, NX, NY)
        )
        mixed = jnp.einsum("zxy,yl->zxl", slab_field, sine_y, precision=high)
        mixed = jnp.einsum("zxl,xk->zkl", mixed, sine_x, precision=high)
        depth_wave = (
            slab_index * layers
            + lower_layer
            + lax.broadcasted_iota(jnp.int32, (chunk_layers,), 0)
        )
        depth_eigen = 2.0 - 2.0 * jnp.cos(
            (depth_wave.astype(jnp.float32) + 1.0) * (math.pi / (NZ + 1))
        )
        eigen_sum = (
            eigen_line(NX)[None, :, None]
            + eigen_line(NY)[None, None, :]
            + depth_eigen[:, None, None]
        )
        scaled = mixed / eigen_sum
        potential = jnp.einsum("zkl,xk->zxl", scaled, sine_x, precision=high)
        potential = jnp.einsum("zxl,yl->zxy", potential, sine_y, precision=high)
        outgoing = (
            potential.reshape(chunk_layers, row_count, cells_x, col_count, cells_y)
            .transpose(1, 3, 0, 2, 4)
            .reshape(devices, chunk_layers, columns)
        )
        returned = lax.all_to_all(outgoing, both, 0, 0, tiled=True)
        line_field = line_field + lax.dot_general(
            returned, sine_z_part, (((0, 1), (1, 2)), ((), ())), precision=high
        )
    padded = with_halo(line_field.reshape(cells_x, cells_y, NZ), (("row", 0), ("col", 1)), 1)
    field_x = (-0.5 * (padded[2:, 1:-1] - padded[:-2, 1:-1])).reshape(columns, NZ)
    field_y = (-0.5 * (padded[1:-1, 2:] - padded[1:-1, :-2])).reshape(columns, NZ)
    found_x, found_y = lookup_fields(field_x, field_y, column_blocks, depth_blocks)
    momentum_x = phase_in[:, 1, :] + kick_strength * found_x.reshape(sources, slot_count)
    momentum_y = phase_in[:, 3, :] + kick_strength * found_y.reshape(sources, slot_count)
    kicked = jnp.stack([momentum_x, momentum_y], axis=1).reshape(
        row_count, col_count, 2, slot_count
    )
    coord_blocks = (
        phase_in[:, 0, :].reshape(step_count, block_rows),
        momentum_x.reshape(step_count, block_rows),
        phase_in[:, 2, :].reshape(step_count, block_rows),
        momentum_y.reshape(step_count, block_rows),
    )
    slice_blocks = (depth_in // (NZ // SLICES)).reshape(step_count, block_rows)
    slice_ids = lax.broadcasted_iota(jnp.int32, (1, SLICES), 1)

    def gather_moments(running, element):
        coord_one, coord_two, coord_three, coord_four, block_slice, block_mass = element
        weighted_slices = jnp.where(block_slice[:, None] == slice_ids, block_mass[:, None], 0.0)
        basis = monomials([coord_one, coord_two, coord_three, coord_four], ORDER)
        moment_part = jnp.dot(
            basis, weighted_slices, precision=highest, preferred_element_type=jnp.float32
        )
        square_part = jnp.sum(weighted_slices * block_mass[:, None], axis=0)
        return ((running[0] + moment_part, running[1] + square_part), None)

    start_state = (
        jnp.zeros((basis_count(ORDER), SLICES), jnp.float32),
        jnp.zeros((SLICES,), jnp.float32),
    )
    (moment_sum, square_sum), unused_too = lax.scan(
        gather_moments, start_state, coord_blocks + (slice_blocks, mass_blocks)
    )
    flat_totals = jnp.concatenate([moment_sum.reshape(-1), square_sum])
    piece = -(-flat_totals.shape[0] // devices)
    flat_totals = jnp.pad(flat_totals, (0, piece * devices - flat_totals.shape[0]))
    own_piece = jnp.sum(
        lax.all_to_all(flat_totals.reshape(devices, piece), both, 0, 0, tiled=True), axis=0
    )
    totals = lax.all_to_all(
        jnp.broadcast_to(own_piece[None, :], (devices, piece)), both, 0, 0, tiled=True
    ).reshape(-1)
    moment_count = moment_sum.shape[0] * SLICES
    moment_total = totals[:moment_count].reshape(moment_sum.shape)
    square_total = totals[moment_count : moment_count + SLICES]
    slice_moments = moment_total / jnp.sqrt(square_total + epsilon)[None, :]
    return (kicked, slice_moments)


def momentum_shape(phase_in):
    return (phase_in.shape[0], phase_in.shape[1], phase_in.shape[3])


def solution(mesh):
    placed = (
        P(("row", "col"), None, None, None),
        P(("row", "col"), None, None),
        P(("row", "col"), None, None),
        P(("row", "col"), None, None),
        P(("row", "col"), None),
    )
    return jax.shard_map(
        body,
        mesh=mesh,
        in_specs=placed,
        out_specs=(P(("row", "col"), None, None, None), P()),
        check_vma=False,
    )
```

```python
import math

import jax
import jax.numpy as jnp
from jax import lax
from jax.sharding import PartitionSpec as P

NX = 256
NY = 256
NZ = 512
SLICES = 64
ORDER = 6


kick_strength = 8.0
epsilon = 1e-06
highest = lax.Precision.HIGHEST
high = lax.Precision.HIGH


def with_halo(block, sides, width):
    for axis, dim in sides:
        count = lax.axis_size(axis)
        forward = [(i, i + 1) for i in range(count - 1)]
        backward = [(target, source) for source, target in forward]
        low = lax.ppermute(
            lax.slice_in_dim(block, block.shape[dim] - width, None, axis=dim), axis, forward
        )
        high = lax.ppermute(lax.slice_in_dim(block, 0, width, axis=dim), axis, backward)
        block = jnp.concatenate([low, block, high], axis=dim)
    return block


def exponent_table(max_order):
    listing = []
    for power_one in range(max_order + 1):
        for power_two in range(max_order + 1):
            for power_three in range(max_order + 1):
                for power_four in range(max_order + 1):
                    if power_one + power_two + power_three + power_four <= max_order:
                        listing.append([power_one, power_two, power_three, power_four])
    return listing


def monomials(coords, max_order):
    power_lists = []
    for position in range(4):
        variable = coords[position]
        powers = [jnp.ones_like(variable)]
        for degree in range(max_order):
            powers.append(powers[-1] * variable)
        power_lists.append(powers)
    terms = []
    for entry in exponent_table(max_order):
        product = power_lists[0][entry[0]]
        for position in range(1, 4):
            product = product * power_lists[position][entry[position]]
        terms.append(product)
    return jnp.stack(terms)


def wave_grid(length):
    row_wave = lax.broadcasted_iota(jnp.int32, (length, length), 0) + 1
    col_wave = lax.broadcasted_iota(jnp.int32, (length, length), 1) + 1
    reduced = row_wave * col_wave % (2 * (length + 1))
    return (reduced.astype(jnp.float32) * (math.pi / (length + 1)), col_wave)


def sine_table(length):
    angles, col_wave = wave_grid(length)
    return math.sqrt(2.0 / (length + 1)) * jnp.sin(angles)


def eigen_line(length):
    wave_index = lax.broadcasted_iota(jnp.int32, (length,), 0).astype(jnp.float32) + 1.0
    return 2.0 - 2.0 * jnp.cos(wave_index * (math.pi / (length + 1)))


def basis_count(max_order):
    return (max_order + 1) * (max_order + 2) * (max_order + 3) * (max_order + 4) // 24


def lookup_fields(field_x, field_y, column_blocks, depth_blocks):
    columns = field_x.shape[0]
    depth_total = field_x.shape[1]
    table = jnp.concatenate([field_x, field_y], axis=1)
    upper = table.astype(jnp.bfloat16)
    upper_wide = lax.optimization_barrier(upper).astype(jnp.float32)
    lower = (table - upper_wide).astype(jnp.bfloat16)
    column_ids = lax.broadcasted_iota(jnp.int32, (1, columns), 1)
    depth_ids = lax.broadcasted_iota(jnp.int32, (1, depth_total), 1)

    def pick(carry, element):
        block_column, block_depth = element
        picked = (block_column[:, None] == column_ids).astype(jnp.bfloat16)
        rows_found = jnp.dot(picked, upper, preferred_element_type=jnp.float32)
        rows_found = rows_found + jnp.dot(picked, lower, preferred_element_type=jnp.float32)
        chosen = block_depth[:, None] == depth_ids
        value_x = jnp.sum(jnp.where(chosen, rows_found[:, :depth_total], 0.0), axis=1)
        value_y = jnp.sum(jnp.where(chosen, rows_found[:, depth_total:], 0.0), axis=1)
        return (carry, (value_x, value_y))

    unused, (found_x, found_y) = lax.scan(
        pick, jnp.zeros((), jnp.float32), (column_blocks, depth_blocks)
    )
    return (found_x, found_y)


def body(particle_phase, particle_weight, cell_column, cell_depth, slot_counts):
    row_count = lax.axis_size("row")
    col_count = lax.axis_size("col")
    devices = row_count * col_count
    slot_count = particle_weight.shape[-1]
    cells_x = NX // row_count
    cells_y = NY // col_count
    columns = cells_x * cells_y
    layers = NZ // devices
    both = ("row", "col")
    live_slot = lax.broadcasted_iota(jnp.int32, particle_weight.shape, 2) < slot_counts[:, :, None]
    live_mass = jnp.where(live_slot, particle_weight.astype(jnp.float32), 0.0)
    packed = jnp.concatenate(
        [
            particle_phase,
            live_mass[:, :, None, :],
            cell_column.astype(jnp.float32)[:, :, None, :],
            cell_depth.astype(jnp.float32)[:, :, None, :],
        ],
        axis=2,
    ).reshape(devices, 7, slot_count)
    arrived = lax.all_to_all(packed, both, 0, 0, tiled=True)
    phase_in = arrived[:, 0:4, :]
    mass_in = arrived[:, 4, :]
    column_in = arrived[:, 5, :].astype(jnp.int32)
    depth_in = arrived[:, 6, :].astype(jnp.int32)
    sources = devices
    group_size = math.gcd(sources, max(1, 2048 // slot_count))
    step_count = sources // group_size
    block_rows = group_size * slot_count
    column_blocks = column_in.reshape(step_count, block_rows)
    depth_blocks = depth_in.reshape(step_count, block_rows)
    mass_blocks = mass_in.reshape(step_count, block_rows)
    column_ids = lax.broadcasted_iota(jnp.int32, (1, columns), 1)
    depth_ids = lax.broadcasted_iota(jnp.int32, (1, NZ), 1)

    def deposit(running, element):
        block_column, block_depth, block_mass = element
        picked = (block_column[:, None] == column_ids).astype(jnp.bfloat16)
        spread = jnp.where(
            block_depth[:, None] == depth_ids,
            block_mass.astype(jnp.bfloat16)[:, None],
            jnp.zeros((), jnp.bfloat16),
        )
        added = lax.dot_general(
            picked, spread, (((0,), (0,)), ((), ())), preferred_element_type=jnp.float32
        )
        return (running + added, None)

    density, unused = lax.scan(
        deposit, jnp.zeros((columns, NZ), jnp.float32), (column_blocks, depth_blocks, mass_blocks)
    )
    sine_x = sine_table(NX)
    sine_y = sine_table(NY)
    sine_z = sine_table(NZ)
    chunk_count = 4 if layers % 4 == 0 else 1
    chunk_layers = layers // chunk_count
    slab_index = lax.axis_index("row") * col_count + lax.axis_index("col")
    sine_z_slabs = sine_z.reshape(NZ, devices, layers)
    line_field = jnp.zeros((columns, NZ), jnp.float32)
    sine_z_parts = []
    sends = []
    for chunk in range(chunk_count):
        lower_layer = chunk * chunk_layers
        sine_z_part = sine_z_slabs[:, :, lower_layer : lower_layer + chunk_layers]
        sine_z_parts.append(sine_z_part)
        sends.append(
            lax.dot_general(sine_z_part, density, (((0,), (1,)), ((), ())), precision=high)
        )
    arrivals = [lax.all_to_all(sends[0], both, 0, 0, tiled=True)]
    if chunk_count > 1:
        arrivals.append(lax.all_to_all(sends[1], both, 0, 0, tiled=True))
    for chunk in range(chunk_count):
        lower_layer = chunk * chunk_layers
        slab_field = (
            arrivals[chunk]
            .reshape(row_count, col_count, chunk_layers, cells_x, cells_y)
            .transpose(2, 0, 3, 1, 4)
            .reshape(chunk_layers, NX, NY)
        )
        mixed = jnp.einsum("zxy,yl->zxl", slab_field, sine_y, precision=high)
        mixed = jnp.einsum("zxl,xk->zkl", mixed, sine_x, precision=high)
        depth_wave = (
            slab_index * layers
            + lower_layer
            + lax.broadcasted_iota(jnp.int32, (chunk_layers,), 0)
        )
        depth_eigen = 2.0 - 2.0 * jnp.cos(
            (depth_wave.astype(jnp.float32) + 1.0) * (math.pi / (NZ + 1))
        )
        eigen_sum = (
            eigen_line(NX)[None, :, None]
            + eigen_line(NY)[None, None, :]
            + depth_eigen[:, None, None]
        )
        scaled = mixed / eigen_sum
        potential = jnp.einsum("zkl,xk->zxl", scaled, sine_x, precision=high)
        potential = jnp.einsum("zxl,yl->zxy", potential, sine_y, precision=high)
        outgoing = (
            potential.reshape(chunk_layers, row_count, cells_x, col_count, cells_y)
            .transpose(1, 3, 0, 2, 4)
            .reshape(devices, chunk_layers, columns)
        )
        returned = lax.all_to_all(outgoing, both, 0, 0, tiled=True)
        if chunk + 2 < chunk_count:
            upcoming, returned = lax.optimization_barrier((sends[chunk + 2], returned))
            arrivals.append(lax.all_to_all(upcoming, both, 0, 0, tiled=True))
        line_field = line_field + lax.dot_general(
            returned, sine_z_parts[chunk], (((0, 1), (1, 2)), ((), ())), precision=high
        )
    padded = with_halo(line_field.reshape(cells_x, cells_y, NZ), (("row", 0), ("col", 1)), 1)
    field_x = (-0.5 * (padded[2:, 1:-1] - padded[:-2, 1:-1])).reshape(columns, NZ)
    field_y = (-0.5 * (padded[1:-1, 2:] - padded[1:-1, :-2])).reshape(columns, NZ)
    found_x, found_y = lookup_fields(field_x, field_y, column_blocks, depth_blocks)
    momentum_x = phase_in[:, 1, :] + kick_strength * found_x.reshape(sources, slot_count)
    momentum_y = phase_in[:, 3, :] + kick_strength * found_y.reshape(sources, slot_count)
    kicked = jnp.stack([momentum_x, momentum_y], axis=1).reshape(
        row_count, col_count, 2, slot_count
    )
    coord_blocks = (
        phase_in[:, 0, :].reshape(step_count, block_rows),
        momentum_x.reshape(step_count, block_rows),
        phase_in[:, 2, :].reshape(step_count, block_rows),
        momentum_y.reshape(step_count, block_rows),
    )
    slice_blocks = (depth_in // (NZ // SLICES)).reshape(step_count, block_rows)
    slice_ids = lax.broadcasted_iota(jnp.int32, (1, SLICES), 1)

    def gather_moments(running, element):
        coord_one, coord_two, coord_three, coord_four, block_slice, block_mass = element
        weighted_slices = jnp.where(block_slice[:, None] == slice_ids, block_mass[:, None], 0.0)
        basis = monomials([coord_one, coord_two, coord_three, coord_four], ORDER)
        moment_part = jnp.dot(
            basis, weighted_slices, precision=highest, preferred_element_type=jnp.float32
        )
        square_part = jnp.sum(weighted_slices * block_mass[:, None], axis=0)
        return ((running[0] + moment_part, running[1] + square_part), None)

    start_state = (
        jnp.zeros((basis_count(ORDER), SLICES), jnp.float32),
        jnp.zeros((SLICES,), jnp.float32),
    )
    (moment_sum, square_sum), unused_too = lax.scan(
        gather_moments, start_state, coord_blocks + (slice_blocks, mass_blocks)
    )
    flat_totals = jnp.concatenate([moment_sum.reshape(-1), square_sum])
    piece = -(-flat_totals.shape[0] // devices)
    flat_totals = jnp.pad(flat_totals, (0, piece * devices - flat_totals.shape[0]))
    own_piece = jnp.sum(
        lax.all_to_all(flat_totals.reshape(devices, piece), both, 0, 0, tiled=True), axis=0
    )
    totals = lax.all_to_all(
        jnp.broadcast_to(own_piece[None, :], (devices, piece)), both, 0, 0, tiled=True
    ).reshape(-1)
    moment_count = moment_sum.shape[0] * SLICES
    moment_total = totals[:moment_count].reshape(moment_sum.shape)
    square_total = totals[moment_count : moment_count + SLICES]
    slice_moments = moment_total / jnp.sqrt(square_total + epsilon)[None, :]
    return (kicked, slice_moments)


def momentum_shape(phase_in):
    return (phase_in.shape[0], phase_in.shape[1], phase_in.shape[3])


def solution(mesh):
    placed = (
        P(("row", "col"), None, None, None),
        P(("row", "col"), None, None),
        P(("row", "col"), None, None),
        P(("row", "col"), None, None),
        P(("row", "col"), None),
    )
    return jax.shard_map(
        body,
        mesh=mesh,
        in_specs=placed,
        out_specs=(P(("row", "col"), None, None, None), P()),
        check_vma=False,
    )
```

```python
import math

import jax
import jax.numpy as jnp
from jax import lax
from jax.sharding import PartitionSpec as P

NX = 256
NY = 256
NZ = 512
SLICES = 64
ORDER = 6


kick_strength = 8.0
epsilon = 1e-06
highest = lax.Precision.HIGHEST
high = lax.Precision.HIGH


def with_halo(block, sides, width):
    for axis, dim in sides:
        count = lax.axis_size(axis)
        forward = [(i, i + 1) for i in range(count - 1)]
        backward = [(target, source) for source, target in forward]
        low = lax.ppermute(
            lax.slice_in_dim(block, block.shape[dim] - width, None, axis=dim), axis, forward
        )
        high = lax.ppermute(lax.slice_in_dim(block, 0, width, axis=dim), axis, backward)
        block = jnp.concatenate([low, block, high], axis=dim)
    return block


def exponent_table(max_order):
    listing = []
    for power_one in range(max_order + 1):
        for power_two in range(max_order + 1):
            for power_three in range(max_order + 1):
                for power_four in range(max_order + 1):
                    if power_one + power_two + power_three + power_four <= max_order:
                        listing.append([power_one, power_two, power_three, power_four])
    return listing


def monomials(coords, max_order):
    power_lists = []
    for position in range(4):
        variable = coords[position]
        powers = [jnp.ones_like(variable)]
        for degree in range(max_order):
            powers.append(powers[-1] * variable)
        power_lists.append(powers)
    terms = []
    for entry in exponent_table(max_order):
        product = power_lists[0][entry[0]]
        for position in range(1, 4):
            product = product * power_lists[position][entry[position]]
        terms.append(product)
    return jnp.stack(terms)


def wave_grid(length):
    row_wave = lax.broadcasted_iota(jnp.int32, (length, length), 0) + 1
    col_wave = lax.broadcasted_iota(jnp.int32, (length, length), 1) + 1
    reduced = row_wave * col_wave % (2 * (length + 1))
    return (reduced.astype(jnp.float32) * (math.pi / (length + 1)), col_wave)


def sine_table(length):
    angles, col_wave = wave_grid(length)
    return math.sqrt(2.0 / (length + 1)) * jnp.sin(angles)


def eigen_line(length):
    wave_index = lax.broadcasted_iota(jnp.int32, (length,), 0).astype(jnp.float32) + 1.0
    return 2.0 - 2.0 * jnp.cos(wave_index * (math.pi / (length + 1)))


def basis_count(max_order):
    return (max_order + 1) * (max_order + 2) * (max_order + 3) * (max_order + 4) // 24


def lookup_fields(field_x, field_y, column_blocks, depth_blocks):
    columns = field_x.shape[0]
    depth_total = field_x.shape[1]
    table = jnp.concatenate([field_x, field_y], axis=1)
    upper = table.astype(jnp.bfloat16)
    upper_wide = lax.optimization_barrier(upper).astype(jnp.float32)
    lower = (table - upper_wide).astype(jnp.bfloat16)
    column_ids = lax.broadcasted_iota(jnp.int32, (1, columns), 1)
    depth_ids = lax.broadcasted_iota(jnp.int32, (1, depth_total), 1)

    def pick(carry, element):
        block_column, block_depth = element
        picked = (block_column[:, None] == column_ids).astype(jnp.bfloat16)
        rows_found = jnp.dot(picked, upper, preferred_element_type=jnp.float32)
        rows_found = rows_found + jnp.dot(picked, lower, preferred_element_type=jnp.float32)
        chosen = block_depth[:, None] == depth_ids
        value_x = jnp.sum(jnp.where(chosen, rows_found[:, :depth_total], 0.0), axis=1)
        value_y = jnp.sum(jnp.where(chosen, rows_found[:, depth_total:], 0.0), axis=1)
        return (carry, (value_x, value_y))

    unused, (found_x, found_y) = lax.scan(
        pick, jnp.zeros((), jnp.float32), (column_blocks, depth_blocks)
    )
    return (found_x, found_y)


def body(particle_phase, particle_weight, cell_column, cell_depth, slot_counts):
    row_count = lax.axis_size("row")
    col_count = lax.axis_size("col")
    devices = row_count * col_count
    slot_count = particle_weight.shape[-1]
    cells_x = NX // row_count
    cells_y = NY // col_count
    columns = cells_x * cells_y
    layers = NZ // devices
    both = ("row", "col")
    live_slot = lax.broadcasted_iota(jnp.int32, particle_weight.shape, 2) < slot_counts[:, :, None]
    live_mass = jnp.where(live_slot, particle_weight.astype(jnp.float32), 0.0)
    packed = jnp.concatenate(
        [
            particle_phase,
            live_mass[:, :, None, :],
            cell_column.astype(jnp.float32)[:, :, None, :],
            cell_depth.astype(jnp.float32)[:, :, None, :],
        ],
        axis=2,
    ).reshape(devices, 7, slot_count)
    arrived = lax.all_to_all(packed, both, 0, 0, tiled=True)
    phase_in = arrived[:, 0:4, :]
    mass_in = arrived[:, 4, :]
    column_in = arrived[:, 5, :].astype(jnp.int32)
    depth_in = arrived[:, 6, :].astype(jnp.int32)
    sources = devices
    group_size = math.gcd(sources, max(1, 2048 // slot_count))
    step_count = sources // group_size
    block_rows = group_size * slot_count
    column_blocks = column_in.reshape(step_count, block_rows)
    depth_blocks = depth_in.reshape(step_count, block_rows)
    mass_blocks = mass_in.reshape(step_count, block_rows)
    column_ids = lax.broadcasted_iota(jnp.int32, (1, columns), 1)
    depth_ids = lax.broadcasted_iota(jnp.int32, (1, NZ), 1)

    def deposit(running, element):
        block_column, block_depth, block_mass = element
        picked = (block_column[:, None] == column_ids).astype(jnp.bfloat16)
        spread = jnp.where(
            block_depth[:, None] == depth_ids,
            block_mass.astype(jnp.bfloat16)[:, None],
            jnp.zeros((), jnp.bfloat16),
        )
        added = lax.dot_general(
            picked, spread, (((0,), (0,)), ((), ())), preferred_element_type=jnp.float32
        )
        return (running + added, None)

    density, unused = lax.scan(
        deposit, jnp.zeros((columns, NZ), jnp.float32), (column_blocks, depth_blocks, mass_blocks)
    )
    sine_x = sine_table(NX)
    sine_y = sine_table(NY)
    sine_z = sine_table(NZ)
    chunk_count = 2 if layers % 2 == 0 else 1
    chunk_layers = layers // chunk_count
    slab_index = lax.axis_index("row") * col_count + lax.axis_index("col")
    sine_z_slabs = sine_z.reshape(NZ, devices, layers)
    line_field = jnp.zeros((columns, NZ), jnp.float32)
    sine_z_parts = []
    sends = []
    for chunk in range(chunk_count):
        lower_layer = chunk * chunk_layers
        sine_z_part = sine_z_slabs[:, :, lower_layer : lower_layer + chunk_layers]
        sine_z_parts.append(sine_z_part)
        sends.append(
            lax.dot_general(sine_z_part, density, (((0,), (1,)), ((), ())), precision=high)
        )
    arrivals = [lax.all_to_all(sends[0], both, 0, 0, tiled=True)]
    if chunk_count > 1:
        arrivals.append(lax.all_to_all(sends[1], both, 0, 0, tiled=True))
    for chunk in range(chunk_count):
        lower_layer = chunk * chunk_layers
        slab_field = (
            arrivals[chunk]
            .reshape(row_count, col_count, chunk_layers, cells_x, cells_y)
            .transpose(2, 0, 3, 1, 4)
            .reshape(chunk_layers, NX, NY)
        )
        mixed = jnp.einsum("zxy,yl->zxl", slab_field, sine_y, precision=high)
        mixed = jnp.einsum("zxl,xk->zkl", mixed, sine_x, precision=high)
        depth_wave = (
            slab_index * layers
            + lower_layer
            + lax.broadcasted_iota(jnp.int32, (chunk_layers,), 0)
        )
        depth_eigen = 2.0 - 2.0 * jnp.cos(
            (depth_wave.astype(jnp.float32) + 1.0) * (math.pi / (NZ + 1))
        )
        eigen_sum = (
            eigen_line(NX)[None, :, None]
            + eigen_line(NY)[None, None, :]
            + depth_eigen[:, None, None]
        )
        scaled = mixed / eigen_sum
        potential = jnp.einsum("zkl,xk->zxl", scaled, sine_x, precision=high)
        potential = jnp.einsum("zxl,yl->zxy", potential, sine_y, precision=high)
        outgoing = (
            potential.reshape(chunk_layers, row_count, cells_x, col_count, cells_y)
            .transpose(1, 3, 0, 2, 4)
            .reshape(devices, chunk_layers, columns)
        )
        returned = lax.all_to_all(outgoing, both, 0, 0, tiled=True)
        if chunk + 2 < chunk_count:
            upcoming, returned = lax.optimization_barrier((sends[chunk + 2], returned))
            arrivals.append(lax.all_to_all(upcoming, both, 0, 0, tiled=True))
        line_field = line_field + lax.dot_general(
            returned, sine_z_parts[chunk], (((0, 1), (1, 2)), ((), ())), precision=high
        )
    padded = with_halo(line_field.reshape(cells_x, cells_y, NZ), (("row", 0), ("col", 1)), 1)
    field_x = (-0.5 * (padded[2:, 1:-1] - padded[:-2, 1:-1])).reshape(columns, NZ)
    field_y = (-0.5 * (padded[1:-1, 2:] - padded[1:-1, :-2])).reshape(columns, NZ)
    found_x, found_y = lookup_fields(field_x, field_y, column_blocks, depth_blocks)
    momentum_x = phase_in[:, 1, :] + kick_strength * found_x.reshape(sources, slot_count)
    momentum_y = phase_in[:, 3, :] + kick_strength * found_y.reshape(sources, slot_count)
    kicked = jnp.stack([momentum_x, momentum_y], axis=1).reshape(
        row_count, col_count, 2, slot_count
    )
    coord_blocks = (
        phase_in[:, 0, :].reshape(step_count, block_rows),
        momentum_x.reshape(step_count, block_rows),
        phase_in[:, 2, :].reshape(step_count, block_rows),
        momentum_y.reshape(step_count, block_rows),
    )
    slice_blocks = (depth_in // (NZ // SLICES)).reshape(step_count, block_rows)
    slice_ids = lax.broadcasted_iota(jnp.int32, (1, SLICES), 1)

    def gather_moments(running, element):
        coord_one, coord_two, coord_three, coord_four, block_slice, block_mass = element
        weighted_slices = jnp.where(block_slice[:, None] == slice_ids, block_mass[:, None], 0.0)
        basis = monomials([coord_one, coord_two, coord_three, coord_four], ORDER)
        moment_part = jnp.dot(
            basis, weighted_slices, precision=highest, preferred_element_type=jnp.float32
        )
        square_part = jnp.sum(weighted_slices * block_mass[:, None], axis=0)
        return ((running[0] + moment_part, running[1] + square_part), None)

    start_state = (
        jnp.zeros((basis_count(ORDER), SLICES), jnp.float32),
        jnp.zeros((SLICES,), jnp.float32),
    )
    (moment_sum, square_sum), unused_too = lax.scan(
        gather_moments, start_state, coord_blocks + (slice_blocks, mass_blocks)
    )
    flat_totals = jnp.concatenate([moment_sum.reshape(-1), square_sum])
    piece = -(-flat_totals.shape[0] // devices)
    flat_totals = jnp.pad(flat_totals, (0, piece * devices - flat_totals.shape[0]))
    own_piece = jnp.sum(
        lax.all_to_all(flat_totals.reshape(devices, piece), both, 0, 0, tiled=True), axis=0
    )
    totals = lax.all_to_all(
        jnp.broadcast_to(own_piece[None, :], (devices, piece)), both, 0, 0, tiled=True
    ).reshape(-1)
    moment_count = moment_sum.shape[0] * SLICES
    moment_total = totals[:moment_count].reshape(moment_sum.shape)
    square_total = totals[moment_count : moment_count + SLICES]
    slice_moments = moment_total / jnp.sqrt(square_total + epsilon)[None, :]
    return (kicked, slice_moments)


def momentum_shape(phase_in):
    return (phase_in.shape[0], phase_in.shape[1], phase_in.shape[3])


def solution(mesh):
    placed = (
        P(("row", "col"), None, None, None),
        P(("row", "col"), None, None),
        P(("row", "col"), None, None),
        P(("row", "col"), None, None),
        P(("row", "col"), None),
    )
    return jax.shard_map(
        body,
        mesh=mesh,
        in_specs=placed,
        out_specs=(P(("row", "col"), None, None, None), P()),
        check_vma=False,
    )
```

```python
import math

import jax
import jax.numpy as jnp
from jax import lax
from jax.sharding import PartitionSpec as P

NX = 256
NY = 256
NZ = 512
SLICES = 64
ORDER = 6


kick_strength = 8.0
epsilon = 1e-06
highest = lax.Precision.HIGHEST
high = lax.Precision.HIGH


def with_halo(block, sides, width):
    for axis, dim in sides:
        count = lax.axis_size(axis)
        forward = [(i, i + 1) for i in range(count - 1)]
        backward = [(target, source) for source, target in forward]
        low = lax.ppermute(
            lax.slice_in_dim(block, block.shape[dim] - width, None, axis=dim), axis, forward
        )
        high = lax.ppermute(lax.slice_in_dim(block, 0, width, axis=dim), axis, backward)
        block = jnp.concatenate([low, block, high], axis=dim)
    return block


def exponent_table(max_order):
    listing = []
    for power_one in range(max_order + 1):
        for power_two in range(max_order + 1):
            for power_three in range(max_order + 1):
                for power_four in range(max_order + 1):
                    if power_one + power_two + power_three + power_four <= max_order:
                        listing.append([power_one, power_two, power_three, power_four])
    return listing


def monomials(coords, max_order):
    power_lists = []
    for position in range(4):
        variable = coords[position]
        powers = [jnp.ones_like(variable)]
        for degree in range(max_order):
            powers.append(powers[-1] * variable)
        power_lists.append(powers)
    terms = []
    for entry in exponent_table(max_order):
        product = power_lists[0][entry[0]]
        for position in range(1, 4):
            product = product * power_lists[position][entry[position]]
        terms.append(product)
    return jnp.stack(terms)


def wave_grid(length):
    row_wave = lax.broadcasted_iota(jnp.int32, (length, length), 0) + 1
    col_wave = lax.broadcasted_iota(jnp.int32, (length, length), 1) + 1
    reduced = row_wave * col_wave % (2 * (length + 1))
    return (reduced.astype(jnp.float32) * (math.pi / (length + 1)), col_wave)


def sine_table(length):
    angles, col_wave = wave_grid(length)
    return math.sqrt(2.0 / (length + 1)) * jnp.sin(angles)


def eigen_line(length):
    wave_index = lax.broadcasted_iota(jnp.int32, (length,), 0).astype(jnp.float32) + 1.0
    return 2.0 - 2.0 * jnp.cos(wave_index * (math.pi / (length + 1)))


def basis_count(max_order):
    return (max_order + 1) * (max_order + 2) * (max_order + 3) * (max_order + 4) // 24


def lookup_fields(field_x, field_y, column_blocks, depth_blocks):
    columns = field_x.shape[0]
    depth_total = field_x.shape[1]
    table = jnp.concatenate([field_x, field_y], axis=1)
    upper = table.astype(jnp.bfloat16)
    upper_wide = lax.optimization_barrier(upper).astype(jnp.float32)
    lower = (table - upper_wide).astype(jnp.bfloat16)
    column_ids = lax.broadcasted_iota(jnp.int32, (1, columns), 1)
    depth_ids = lax.broadcasted_iota(jnp.int32, (1, depth_total), 1)

    def pick(carry, element):
        block_column, block_depth = element
        picked = (block_column[:, None] == column_ids).astype(jnp.bfloat16)
        rows_found = jnp.dot(picked, upper, preferred_element_type=jnp.float32)
        rows_found = rows_found + jnp.dot(picked, lower, preferred_element_type=jnp.float32)
        chosen = block_depth[:, None] == depth_ids
        value_x = jnp.sum(jnp.where(chosen, rows_found[:, :depth_total], 0.0), axis=1)
        value_y = jnp.sum(jnp.where(chosen, rows_found[:, depth_total:], 0.0), axis=1)
        return (carry, (value_x, value_y))

    unused, (found_x, found_y) = lax.scan(
        pick, jnp.zeros((), jnp.float32), (column_blocks, depth_blocks)
    )
    return (found_x, found_y)


def neighbour_pickers(column, cells_x, cells_y):
    columns = cells_x * cells_y
    cx = column // cells_y
    cy = column % cells_y
    missing = jnp.full_like(column, -1)
    ahead = jnp.stack(
        [
            jnp.where(cx + 1 < cells_x, (cx + 1) * cells_y + cy, missing),
            jnp.where(cy + 1 < cells_y, cx * cells_y + cy + 1, missing),
        ]
    )
    behind = jnp.stack(
        [
            jnp.where(cx >= 1, (cx - 1) * cells_y + cy, missing),
            jnp.where(cy >= 1, cx * cells_y + cy - 1, missing),
        ]
    )
    halo_ahead = jnp.stack(
        [
            jnp.where(cx == cells_x - 1, cells_y + cy, missing),
            jnp.where(cy == cells_y - 1, 2 * cells_y + cells_x + cx, missing),
        ]
    )
    halo_behind = jnp.stack(
        [
            jnp.where(cx == 0, cy, missing),
            jnp.where(cy == 0, 2 * cells_y + cx, missing),
        ]
    )
    half = jnp.asarray(0.5, jnp.bfloat16)
    zero = jnp.zeros((), jnp.bfloat16)

    def picker(plus, minus, width):
        ids = lax.broadcasted_iota(jnp.int32, (1, 1, width), 2)
        chosen = jnp.where(ids == plus[:, :, None], -half, zero) + jnp.where(
            ids == minus[:, :, None], half, zero
        )
        return chosen.reshape(2 * column.shape[0], width)

    halo_width = 2 * cells_y + 2 * cells_x
    return (picker(ahead, behind, columns), picker(halo_ahead, halo_behind, halo_width))


def shift_along(block, axis, forward):
    count = lax.axis_size(axis)
    pairs = [(i, i + 1) for i in range(count - 1)]
    if not forward:
        pairs = [(target, source) for source, target in pairs]
    return lax.ppermute(block, axis, pairs)


def split_dot(pick, table):
    upper = table.astype(jnp.bfloat16)
    upper_wide = lax.optimization_barrier(upper).astype(jnp.float32)
    lower = (table - upper_wide).astype(jnp.bfloat16)
    dims = (((1,), (1,)), ((), ()))
    return lax.dot_general(pick, upper, dims, preferred_element_type=jnp.float32) + lax.dot_general(
        pick, lower, dims, preferred_element_type=jnp.float32
    )


def kz_lookup(wave_table, sine_part, pick_main, pick_halo, depth_pick, cells_x, cells_y):
    waves = wave_table.shape[0]
    grid = wave_table.reshape(waves, cells_x, cells_y)
    halo = jnp.concatenate(
        [
            shift_along(grid[:, cells_x - 1, :], "row", True),
            shift_along(grid[:, 0, :], "row", False),
            shift_along(grid[:, :, cells_y - 1], "col", True),
            shift_along(grid[:, :, 0], "col", False),
        ],
        axis=1,
    )

    def pick(carry, element):
        block_main, block_halo, block_depth = element
        pulled = split_dot(block_main, wave_table) + split_dot(block_halo, halo)
        depth_wave = jnp.dot(
            block_depth,
            sine_part,
            precision=lax.Precision.HIGHEST,
            preferred_element_type=jnp.float32,
        )
        count = block_depth.shape[0]
        return (carry, jnp.sum(pulled.reshape(2, count, waves) * depth_wave[None], axis=2))

    unused, found = lax.scan(pick, jnp.zeros((), jnp.float32), (pick_main, pick_halo, depth_pick))
    return found


def body(particle_phase, particle_weight, cell_column, cell_depth, slot_counts):
    row_count = lax.axis_size("row")
    col_count = lax.axis_size("col")
    devices = row_count * col_count
    slot_count = particle_weight.shape[-1]
    cells_x = NX // row_count
    cells_y = NY // col_count
    columns = cells_x * cells_y
    layers = NZ // devices
    both = ("row", "col")
    live_slot = lax.broadcasted_iota(jnp.int32, particle_weight.shape, 2) < slot_counts[:, :, None]
    live_mass = jnp.where(live_slot, particle_weight.astype(jnp.float32), 0.0)
    packed = jnp.concatenate(
        [
            particle_phase,
            live_mass[:, :, None, :],
            cell_column.astype(jnp.float32)[:, :, None, :],
            cell_depth.astype(jnp.float32)[:, :, None, :],
        ],
        axis=2,
    ).reshape(devices, 7, slot_count)
    arrived = lax.all_to_all(packed, both, 0, 0, tiled=True)
    phase_in = arrived[:, 0:4, :]
    mass_in = arrived[:, 4, :]
    column_in = arrived[:, 5, :].astype(jnp.int32)
    depth_in = arrived[:, 6, :].astype(jnp.int32)
    sources = devices
    group_size = math.gcd(sources, max(1, 2048 // slot_count))
    step_count = sources // group_size
    block_rows = group_size * slot_count
    column_blocks = column_in.reshape(step_count, block_rows)
    depth_blocks = depth_in.reshape(step_count, block_rows)
    mass_blocks = mass_in.reshape(step_count, block_rows)
    column_ids = lax.broadcasted_iota(jnp.int32, (1, columns), 1)
    depth_ids = lax.broadcasted_iota(jnp.int32, (1, NZ), 1)

    def deposit(running, element):
        block_column, block_depth, block_mass = element
        picked = (block_column[:, None] == column_ids).astype(jnp.bfloat16)
        spread = jnp.where(
            block_depth[:, None] == depth_ids,
            block_mass.astype(jnp.bfloat16)[:, None],
            jnp.zeros((), jnp.bfloat16),
        )
        added = lax.dot_general(
            picked, spread, (((0,), (0,)), ((), ())), preferred_element_type=jnp.float32
        )
        return (running + added, None)

    density, unused = lax.scan(
        deposit, jnp.zeros((columns, NZ), jnp.float32), (column_blocks, depth_blocks, mass_blocks)
    )
    sine_x = sine_table(NX)
    sine_y = sine_table(NY)
    sine_z = sine_table(NZ)
    chunk_count = 2 if layers % 2 == 0 else 1
    chunk_layers = layers // chunk_count
    slab_index = lax.axis_index("row") * col_count + lax.axis_index("col")
    sine_z_slabs = sine_z.reshape(NZ, devices, layers)
    pick_main, pick_halo = jax.vmap(lambda block: neighbour_pickers(block, cells_x, cells_y))(
        column_blocks
    )
    depth_pick = (depth_blocks[:, :, None] == depth_ids[None]).astype(jnp.bfloat16)
    found = jnp.zeros((step_count, 2, block_rows), jnp.float32)
    sine_z_parts = []
    sends = []
    for chunk in range(chunk_count):
        lower_layer = chunk * chunk_layers
        sine_z_part = sine_z_slabs[:, :, lower_layer : lower_layer + chunk_layers]
        sine_z_parts.append(sine_z_part)
        sends.append(
            lax.dot_general(sine_z_part, density, (((0,), (1,)), ((), ())), precision=high)
        )
    arrivals = [lax.all_to_all(sends[0], both, 0, 0, tiled=True)]
    if chunk_count > 1:
        arrivals.append(lax.all_to_all(sends[1], both, 0, 0, tiled=True))
    for chunk in range(chunk_count):
        lower_layer = chunk * chunk_layers
        slab_field = (
            arrivals[chunk]
            .reshape(row_count, col_count, chunk_layers, cells_x, cells_y)
            .transpose(2, 0, 3, 1, 4)
            .reshape(chunk_layers, NX, NY)
        )
        mixed = jnp.einsum("zxy,yl->zxl", slab_field, sine_y, precision=high)
        mixed = jnp.einsum("zxl,xk->zkl", mixed, sine_x, precision=high)
        depth_wave = (
            slab_index * layers
            + lower_layer
            + lax.broadcasted_iota(jnp.int32, (chunk_layers,), 0)
        )
        depth_eigen = 2.0 - 2.0 * jnp.cos(
            (depth_wave.astype(jnp.float32) + 1.0) * (math.pi / (NZ + 1))
        )
        eigen_sum = (
            eigen_line(NX)[None, :, None]
            + eigen_line(NY)[None, None, :]
            + depth_eigen[:, None, None]
        )
        scaled = mixed / eigen_sum
        potential = jnp.einsum("zkl,xk->zxl", scaled, sine_x, precision=high)
        potential = jnp.einsum("zxl,yl->zxy", potential, sine_y, precision=high)
        outgoing = (
            potential.reshape(chunk_layers, row_count, cells_x, col_count, cells_y)
            .transpose(1, 3, 0, 2, 4)
            .reshape(devices, chunk_layers, columns)
        )
        returned = lax.all_to_all(outgoing, both, 0, 0, tiled=True)
        if chunk + 2 < chunk_count:
            upcoming, returned = lax.optimization_barrier((sends[chunk + 2], returned))
            arrivals.append(lax.all_to_all(upcoming, both, 0, 0, tiled=True))
        found = found + kz_lookup(
            returned.reshape(devices * chunk_layers, columns),
            sine_z_parts[chunk].reshape(NZ, devices * chunk_layers),
            pick_main,
            pick_halo,
            depth_pick,
            cells_x,
            cells_y,
        )
    found_x = found[:, 0, :]
    found_y = found[:, 1, :]
    momentum_x = phase_in[:, 1, :] + kick_strength * found_x.reshape(sources, slot_count)
    momentum_y = phase_in[:, 3, :] + kick_strength * found_y.reshape(sources, slot_count)
    kicked = jnp.stack([momentum_x, momentum_y], axis=1).reshape(
        row_count, col_count, 2, slot_count
    )
    coord_blocks = (
        phase_in[:, 0, :].reshape(step_count, block_rows),
        momentum_x.reshape(step_count, block_rows),
        phase_in[:, 2, :].reshape(step_count, block_rows),
        momentum_y.reshape(step_count, block_rows),
    )
    slice_blocks = (depth_in // (NZ // SLICES)).reshape(step_count, block_rows)
    slice_ids = lax.broadcasted_iota(jnp.int32, (1, SLICES), 1)

    def gather_moments(running, element):
        coord_one, coord_two, coord_three, coord_four, block_slice, block_mass = element
        weighted_slices = jnp.where(block_slice[:, None] == slice_ids, block_mass[:, None], 0.0)
        basis = monomials([coord_one, coord_two, coord_three, coord_four], ORDER)
        moment_part = jnp.dot(
            basis, weighted_slices, precision=highest, preferred_element_type=jnp.float32
        )
        square_part = jnp.sum(weighted_slices * block_mass[:, None], axis=0)
        return ((running[0] + moment_part, running[1] + square_part), None)

    start_state = (
        jnp.zeros((basis_count(ORDER), SLICES), jnp.float32),
        jnp.zeros((SLICES,), jnp.float32),
    )
    (moment_sum, square_sum), unused_too = lax.scan(
        gather_moments, start_state, coord_blocks + (slice_blocks, mass_blocks)
    )
    flat_totals = jnp.concatenate([moment_sum.reshape(-1), square_sum])
    piece = -(-flat_totals.shape[0] // devices)
    flat_totals = jnp.pad(flat_totals, (0, piece * devices - flat_totals.shape[0]))
    own_piece = jnp.sum(
        lax.all_to_all(flat_totals.reshape(devices, piece), both, 0, 0, tiled=True), axis=0
    )
    totals = lax.all_to_all(
        jnp.broadcast_to(own_piece[None, :], (devices, piece)), both, 0, 0, tiled=True
    ).reshape(-1)
    moment_count = moment_sum.shape[0] * SLICES
    moment_total = totals[:moment_count].reshape(moment_sum.shape)
    square_total = totals[moment_count : moment_count + SLICES]
    slice_moments = moment_total / jnp.sqrt(square_total + epsilon)[None, :]
    return (kicked, slice_moments)


def momentum_shape(phase_in):
    return (phase_in.shape[0], phase_in.shape[1], phase_in.shape[3])


def solution(mesh):
    placed = (
        P(("row", "col"), None, None, None),
        P(("row", "col"), None, None),
        P(("row", "col"), None, None),
        P(("row", "col"), None, None),
        P(("row", "col"), None),
    )
    return jax.shard_map(
        body,
        mesh=mesh,
        in_specs=placed,
        out_specs=(P(("row", "col"), None, None, None), P()),
        check_vma=False,
    )
```

```python
import math

import jax
import jax.numpy as jnp
from jax import lax
from jax.sharding import PartitionSpec as P

NX = 256
NY = 256
NZ = 512
SLICES = 64
ORDER = 6


kick_strength = 8.0
epsilon = 1e-06
highest = lax.Precision.HIGHEST
high = lax.Precision.HIGH


def with_halo(block, sides, width):
    for axis, dim in sides:
        count = lax.axis_size(axis)
        forward = [(i, i + 1) for i in range(count - 1)]
        backward = [(target, source) for source, target in forward]
        low = lax.ppermute(
            lax.slice_in_dim(block, block.shape[dim] - width, None, axis=dim), axis, forward
        )
        high = lax.ppermute(lax.slice_in_dim(block, 0, width, axis=dim), axis, backward)
        block = jnp.concatenate([low, block, high], axis=dim)
    return block


def exponent_table(max_order):
    listing = []
    for power_one in range(max_order + 1):
        for power_two in range(max_order + 1):
            for power_three in range(max_order + 1):
                for power_four in range(max_order + 1):
                    if power_one + power_two + power_three + power_four <= max_order:
                        listing.append([power_one, power_two, power_three, power_four])
    return listing


def monomials(coords, max_order):
    power_lists = []
    for position in range(4):
        variable = coords[position]
        powers = [jnp.ones_like(variable)]
        for degree in range(max_order):
            powers.append(powers[-1] * variable)
        power_lists.append(powers)
    terms = []
    for entry in exponent_table(max_order):
        product = power_lists[0][entry[0]]
        for position in range(1, 4):
            product = product * power_lists[position][entry[position]]
        terms.append(product)
    return jnp.stack(terms)


def wave_grid(length):
    row_wave = lax.broadcasted_iota(jnp.int32, (length, length), 0) + 1
    col_wave = lax.broadcasted_iota(jnp.int32, (length, length), 1) + 1
    reduced = row_wave * col_wave % (2 * (length + 1))
    return (reduced.astype(jnp.float32) * (math.pi / (length + 1)), col_wave)


def sine_table(length):
    angles, col_wave = wave_grid(length)
    return math.sqrt(2.0 / (length + 1)) * jnp.sin(angles)


def eigen_line(length):
    wave_index = lax.broadcasted_iota(jnp.int32, (length,), 0).astype(jnp.float32) + 1.0
    return 2.0 - 2.0 * jnp.cos(wave_index * (math.pi / (length + 1)))


def basis_count(max_order):
    return (max_order + 1) * (max_order + 2) * (max_order + 3) * (max_order + 4) // 24


def lookup_fields(field_x, field_y, column_blocks, depth_blocks):
    columns = field_x.shape[0]
    depth_total = field_x.shape[1]
    table = jnp.concatenate([field_x, field_y], axis=1)
    upper = table.astype(jnp.bfloat16)
    upper_wide = lax.optimization_barrier(upper).astype(jnp.float32)
    lower = (table - upper_wide).astype(jnp.bfloat16)
    column_ids = lax.broadcasted_iota(jnp.int32, (1, columns), 1)
    depth_ids = lax.broadcasted_iota(jnp.int32, (1, depth_total), 1)

    def pick(carry, element):
        block_column, block_depth = element
        picked = (block_column[:, None] == column_ids).astype(jnp.bfloat16)
        rows_found = jnp.dot(picked, upper, preferred_element_type=jnp.float32)
        rows_found = rows_found + jnp.dot(picked, lower, preferred_element_type=jnp.float32)
        chosen = block_depth[:, None] == depth_ids
        value_x = jnp.sum(jnp.where(chosen, rows_found[:, :depth_total], 0.0), axis=1)
        value_y = jnp.sum(jnp.where(chosen, rows_found[:, depth_total:], 0.0), axis=1)
        return (carry, (value_x, value_y))

    unused, (found_x, found_y) = lax.scan(
        pick, jnp.zeros((), jnp.float32), (column_blocks, depth_blocks)
    )
    return (found_x, found_y)


def body(particle_phase, particle_weight, cell_column, cell_depth, slot_counts):
    row_count = lax.axis_size("row")
    col_count = lax.axis_size("col")
    devices = row_count * col_count
    slot_count = particle_weight.shape[-1]
    cells_x = NX // row_count
    cells_y = NY // col_count
    columns = cells_x * cells_y
    layers = NZ // devices
    both = ("row", "col")
    live_slot = lax.broadcasted_iota(jnp.int32, particle_weight.shape, 2) < slot_counts[:, :, None]
    live_mass = jnp.where(live_slot, particle_weight.astype(jnp.float32), 0.0)
    packed = jnp.concatenate(
        [
            particle_phase,
            live_mass[:, :, None, :],
            cell_column.astype(jnp.float32)[:, :, None, :],
            cell_depth.astype(jnp.float32)[:, :, None, :],
        ],
        axis=2,
    ).reshape(devices, 7, slot_count)
    arrived = lax.all_to_all(packed, both, 0, 0, tiled=True)
    phase_in = arrived[:, 0:4, :]
    mass_in = arrived[:, 4, :]
    column_in = arrived[:, 5, :].astype(jnp.int32)
    depth_in = arrived[:, 6, :].astype(jnp.int32)
    sources = devices
    group_size = math.gcd(sources, max(1, 2048 // slot_count))
    step_count = sources // group_size
    block_rows = group_size * slot_count
    column_blocks = column_in.reshape(step_count, block_rows)
    depth_blocks = depth_in.reshape(step_count, block_rows)
    mass_blocks = mass_in.reshape(step_count, block_rows)
    column_ids = lax.broadcasted_iota(jnp.int32, (1, columns), 1)
    depth_ids = lax.broadcasted_iota(jnp.int32, (1, NZ), 1)

    def deposit(running, element):
        block_column, block_depth, block_mass = element
        picked = (block_column[:, None] == column_ids).astype(jnp.bfloat16)
        spread = jnp.where(
            block_depth[:, None] == depth_ids,
            block_mass.astype(jnp.bfloat16)[:, None],
            jnp.zeros((), jnp.bfloat16),
        )
        added = lax.dot_general(
            picked, spread, (((0,), (0,)), ((), ())), preferred_element_type=jnp.float32
        )
        return (running + added, None)

    density, unused = lax.scan(
        deposit, jnp.zeros((columns, NZ), jnp.float32), (column_blocks, depth_blocks, mass_blocks)
    )
    sine_x = sine_table(NX)
    sine_y = sine_table(NY)
    sine_z = sine_table(NZ)
    chunk_count = 2 if layers % 2 == 0 else 1
    chunk_layers = layers // chunk_count
    slab_index = lax.axis_index("row") * col_count + lax.axis_index("col")
    sine_z_slabs = sine_z.reshape(NZ, devices, layers)
    line_field = jnp.zeros((columns, NZ), jnp.float32)
    sine_z_parts = []
    sends = []
    for chunk in range(chunk_count):
        lower_layer = chunk * chunk_layers
        sine_z_part = sine_z_slabs[:, :, lower_layer : lower_layer + chunk_layers]
        sine_z_parts.append(sine_z_part)
        sends.append(
            lax.dot_general(sine_z_part, density, (((0,), (1,)), ((), ())), precision=high)
        )
    arrivals = [lax.all_to_all(sends[0], both, 0, 0, tiled=True)]
    if chunk_count > 1:
        arrivals.append(lax.all_to_all(sends[1], both, 0, 0, tiled=True))
    for chunk in range(chunk_count):
        lower_layer = chunk * chunk_layers
        slab_field = arrivals[chunk].reshape(row_count, col_count, chunk_layers, cells_x, cells_y)
        sine_y_blocks = sine_y.reshape(col_count, cells_y, NY)
        sine_x_blocks = sine_x.reshape(row_count, cells_x, NX)
        mixed = jnp.einsum("rczxy,cyl->zrxl", slab_field, sine_y_blocks, precision=high)
        mixed = jnp.einsum("zrxl,rxk->zkl", mixed, sine_x_blocks, precision=high)
        depth_wave = (
            slab_index * layers
            + lower_layer
            + lax.broadcasted_iota(jnp.int32, (chunk_layers,), 0)
        )
        depth_eigen = 2.0 - 2.0 * jnp.cos(
            (depth_wave.astype(jnp.float32) + 1.0) * (math.pi / (NZ + 1))
        )
        eigen_sum = (
            eigen_line(NX)[None, :, None]
            + eigen_line(NY)[None, None, :]
            + depth_eigen[:, None, None]
        )
        scaled = mixed / eigen_sum
        potential = jnp.einsum("zkl,rxk->zrxl", scaled, sine_x_blocks, precision=high)
        potential = jnp.einsum("zrxl,cyl->rczxy", potential, sine_y_blocks, precision=high)
        outgoing = potential.reshape(devices, chunk_layers, columns)
        returned = lax.all_to_all(outgoing, both, 0, 0, tiled=True)
        if chunk + 2 < chunk_count:
            upcoming, returned = lax.optimization_barrier((sends[chunk + 2], returned))
            arrivals.append(lax.all_to_all(upcoming, both, 0, 0, tiled=True))
        line_field = line_field + lax.dot_general(
            returned, sine_z_parts[chunk], (((0, 1), (1, 2)), ((), ())), precision=high
        )
    padded = with_halo(line_field.reshape(cells_x, cells_y, NZ), (("row", 0), ("col", 1)), 1)
    field_x = (-0.5 * (padded[2:, 1:-1] - padded[:-2, 1:-1])).reshape(columns, NZ)
    field_y = (-0.5 * (padded[1:-1, 2:] - padded[1:-1, :-2])).reshape(columns, NZ)
    found_x, found_y = lookup_fields(field_x, field_y, column_blocks, depth_blocks)
    momentum_x = phase_in[:, 1, :] + kick_strength * found_x.reshape(sources, slot_count)
    momentum_y = phase_in[:, 3, :] + kick_strength * found_y.reshape(sources, slot_count)
    kicked = jnp.stack([momentum_x, momentum_y], axis=1).reshape(
        row_count, col_count, 2, slot_count
    )
    coord_blocks = (
        phase_in[:, 0, :].reshape(step_count, block_rows),
        momentum_x.reshape(step_count, block_rows),
        phase_in[:, 2, :].reshape(step_count, block_rows),
        momentum_y.reshape(step_count, block_rows),
    )
    slice_blocks = (depth_in // (NZ // SLICES)).reshape(step_count, block_rows)
    slice_ids = lax.broadcasted_iota(jnp.int32, (1, SLICES), 1)

    def gather_moments(running, element):
        coord_one, coord_two, coord_three, coord_four, block_slice, block_mass = element
        weighted_slices = jnp.where(block_slice[:, None] == slice_ids, block_mass[:, None], 0.0)
        basis = monomials([coord_one, coord_two, coord_three, coord_four], ORDER)
        moment_part = jnp.dot(
            basis, weighted_slices, precision=highest, preferred_element_type=jnp.float32
        )
        square_part = jnp.sum(weighted_slices * block_mass[:, None], axis=0)
        return ((running[0] + moment_part, running[1] + square_part), None)

    start_state = (
        jnp.zeros((basis_count(ORDER), SLICES), jnp.float32),
        jnp.zeros((SLICES,), jnp.float32),
    )
    (moment_sum, square_sum), unused_too = lax.scan(
        gather_moments, start_state, coord_blocks + (slice_blocks, mass_blocks)
    )
    flat_totals = jnp.concatenate([moment_sum.reshape(-1), square_sum])
    piece = -(-flat_totals.shape[0] // devices)
    flat_totals = jnp.pad(flat_totals, (0, piece * devices - flat_totals.shape[0]))
    own_piece = jnp.sum(
        lax.all_to_all(flat_totals.reshape(devices, piece), both, 0, 0, tiled=True), axis=0
    )
    totals = lax.all_to_all(
        jnp.broadcast_to(own_piece[None, :], (devices, piece)), both, 0, 0, tiled=True
    ).reshape(-1)
    moment_count = moment_sum.shape[0] * SLICES
    moment_total = totals[:moment_count].reshape(moment_sum.shape)
    square_total = totals[moment_count : moment_count + SLICES]
    slice_moments = moment_total / jnp.sqrt(square_total + epsilon)[None, :]
    return (kicked, slice_moments)


def momentum_shape(phase_in):
    return (phase_in.shape[0], phase_in.shape[1], phase_in.shape[3])


def solution(mesh):
    placed = (
        P(("row", "col"), None, None, None),
        P(("row", "col"), None, None),
        P(("row", "col"), None, None),
        P(("row", "col"), None, None),
        P(("row", "col"), None),
    )
    return jax.shard_map(
        body,
        mesh=mesh,
        in_specs=placed,
        out_specs=(P(("row", "col"), None, None, None), P()),
        check_vma=False,
    )
```

```python
import math

import jax
import jax.numpy as jnp
from jax import lax
from jax.sharding import PartitionSpec as P

NX = 256
NY = 256
NZ = 512
SLICES = 64
ORDER = 6


kick_strength = 8.0
epsilon = 1e-06
highest = lax.Precision.HIGHEST
high = lax.Precision.HIGH


def with_halo(block, sides, width):
    for axis, dim in sides:
        count = lax.axis_size(axis)
        forward = [(i, i + 1) for i in range(count - 1)]
        backward = [(target, source) for source, target in forward]
        low = lax.ppermute(
            lax.slice_in_dim(block, block.shape[dim] - width, None, axis=dim), axis, forward
        )
        high = lax.ppermute(lax.slice_in_dim(block, 0, width, axis=dim), axis, backward)
        block = jnp.concatenate([low, block, high], axis=dim)
    return block


def exponent_table(max_order):
    listing = []
    for power_one in range(max_order + 1):
        for power_two in range(max_order + 1):
            for power_three in range(max_order + 1):
                for power_four in range(max_order + 1):
                    if power_one + power_two + power_three + power_four <= max_order:
                        listing.append([power_one, power_two, power_three, power_four])
    return listing


def monomials(coords, max_order):
    power_lists = []
    for position in range(4):
        variable = coords[position]
        powers = [jnp.ones_like(variable)]
        for degree in range(max_order):
            powers.append(powers[-1] * variable)
        power_lists.append(powers)
    terms = []
    for entry in exponent_table(max_order):
        product = power_lists[0][entry[0]]
        for position in range(1, 4):
            product = product * power_lists[position][entry[position]]
        terms.append(product)
    return jnp.stack(terms)


def wave_grid(length):
    row_wave = lax.broadcasted_iota(jnp.int32, (length, length), 0) + 1
    col_wave = lax.broadcasted_iota(jnp.int32, (length, length), 1) + 1
    reduced = row_wave * col_wave % (2 * (length + 1))
    return (reduced.astype(jnp.float32) * (math.pi / (length + 1)), col_wave)


def sine_table(length):
    angles, col_wave = wave_grid(length)
    return math.sqrt(2.0 / (length + 1)) * jnp.sin(angles)


def eigen_line(length):
    wave_index = lax.broadcasted_iota(jnp.int32, (length,), 0).astype(jnp.float32) + 1.0
    return 2.0 - 2.0 * jnp.cos(wave_index * (math.pi / (length + 1)))


def basis_count(max_order):
    return (max_order + 1) * (max_order + 2) * (max_order + 3) * (max_order + 4) // 24


def lookup_fields(field_x, field_y, column_blocks, depth_blocks):
    columns = field_x.shape[0]
    depth_total = field_x.shape[1]
    table = jnp.concatenate([field_x, field_y], axis=1)
    upper = table.astype(jnp.bfloat16)
    upper_wide = lax.optimization_barrier(upper).astype(jnp.float32)
    lower = (table - upper_wide).astype(jnp.bfloat16)
    column_ids = lax.broadcasted_iota(jnp.int32, (1, columns), 1)
    depth_ids = lax.broadcasted_iota(jnp.int32, (1, depth_total), 1)

    def pick(carry, element):
        block_column, block_depth = element
        picked = (block_column[:, None] == column_ids).astype(jnp.bfloat16)
        rows_found = jnp.dot(picked, upper, preferred_element_type=jnp.float32)
        rows_found = rows_found + jnp.dot(picked, lower, preferred_element_type=jnp.float32)
        chosen = block_depth[:, None] == depth_ids
        value_x = jnp.sum(jnp.where(chosen, rows_found[:, :depth_total], 0.0), axis=1)
        value_y = jnp.sum(jnp.where(chosen, rows_found[:, depth_total:], 0.0), axis=1)
        return (carry, (value_x, value_y))

    unused, (found_x, found_y) = lax.scan(
        pick, jnp.zeros((), jnp.float32), (column_blocks, depth_blocks)
    )
    return (found_x, found_y)


def body(particle_phase, particle_weight, cell_column, cell_depth, slot_counts):
    row_count = lax.axis_size("row")
    col_count = lax.axis_size("col")
    devices = row_count * col_count
    slot_count = particle_weight.shape[-1]
    cells_x = NX // row_count
    cells_y = NY // col_count
    columns = cells_x * cells_y
    layers = NZ // devices
    both = ("row", "col")
    live_slot = lax.broadcasted_iota(jnp.int32, particle_weight.shape, 2) < slot_counts[:, :, None]
    live_mass = jnp.where(live_slot, particle_weight.astype(jnp.float32), 0.0)
    packed = jnp.concatenate(
        [
            particle_phase,
            live_mass[:, :, None, :],
            cell_column.astype(jnp.float32)[:, :, None, :],
            cell_depth.astype(jnp.float32)[:, :, None, :],
        ],
        axis=2,
    ).reshape(devices, 7, slot_count)
    arrived = lax.all_to_all(packed, both, 0, 0, tiled=True)
    phase_in = arrived[:, 0:4, :]
    mass_in = arrived[:, 4, :]
    column_in = arrived[:, 5, :].astype(jnp.int32)
    depth_in = arrived[:, 6, :].astype(jnp.int32)
    sources = devices
    group_size = math.gcd(sources, max(1, 2048 // slot_count))
    step_count = sources // group_size
    block_rows = group_size * slot_count
    column_blocks = column_in.reshape(step_count, block_rows)
    depth_blocks = depth_in.reshape(step_count, block_rows)
    mass_blocks = mass_in.reshape(step_count, block_rows)
    column_ids = lax.broadcasted_iota(jnp.int32, (1, columns), 1)
    depth_ids = lax.broadcasted_iota(jnp.int32, (1, NZ), 1)

    def deposit(running, element):
        block_column, block_depth, block_mass = element
        picked = (block_column[:, None] == column_ids).astype(jnp.bfloat16)
        spread = jnp.where(
            block_depth[:, None] == depth_ids,
            block_mass.astype(jnp.bfloat16)[:, None],
            jnp.zeros((), jnp.bfloat16),
        )
        added = lax.dot_general(
            picked, spread, (((0,), (0,)), ((), ())), preferred_element_type=jnp.float32
        )
        return (running + added, None)

    density, unused = lax.scan(
        deposit, jnp.zeros((columns, NZ), jnp.float32), (column_blocks, depth_blocks, mass_blocks)
    )
    sine_x = sine_table(NX)
    sine_y = sine_table(NY)
    sine_z = sine_table(NZ)
    chunk_count = 2 if layers % 2 == 0 else 1
    chunk_layers = layers // chunk_count
    slab_index = lax.axis_index("row") * col_count + lax.axis_index("col")
    sine_z_slabs = sine_z.reshape(NZ, devices, layers)
    line_field = jnp.zeros((columns, NZ), jnp.float32)
    sine_z_parts = []
    sends = []
    for chunk in range(chunk_count):
        lower_layer = chunk * chunk_layers
        sine_z_part = sine_z_slabs[:, :, lower_layer : lower_layer + chunk_layers]
        sine_z_parts.append(sine_z_part)
        sends.append(
            lax.dot_general(sine_z_part, density, (((0,), (1,)), ((), ())), precision=high)
        )
    arrivals = [lax.all_to_all(sends[0], both, 0, 0, tiled=True)]
    if chunk_count > 1:
        arrivals.append(lax.all_to_all(sends[1], both, 0, 0, tiled=True))
    for chunk in range(chunk_count):
        lower_layer = chunk * chunk_layers
        slab_field = arrivals[chunk].reshape(row_count, col_count, chunk_layers, cells_x, cells_y)
        sine_y_blocks = sine_y.reshape(col_count, cells_y, NY)
        sine_x_blocks = sine_x.reshape(row_count, cells_x, NX)
        mixed = jnp.einsum("rczxy,cyl->zrxl", slab_field, sine_y_blocks, precision=high)
        mixed = jnp.einsum("zrxl,rxk->zkl", mixed, sine_x_blocks, precision=high)
        depth_wave = (
            slab_index * layers
            + lower_layer
            + lax.broadcasted_iota(jnp.int32, (chunk_layers,), 0)
        )
        depth_eigen = 2.0 - 2.0 * jnp.cos(
            (depth_wave.astype(jnp.float32) + 1.0) * (math.pi / (NZ + 1))
        )
        eigen_sum = (
            eigen_line(NX)[None, :, None]
            + eigen_line(NY)[None, None, :]
            + depth_eigen[:, None, None]
        )
        scaled = mixed / eigen_sum
        potential = jnp.einsum("zkl,rxk->zrxl", scaled, sine_x_blocks, precision=high)
        potential = jnp.einsum("zrxl,cyl->rczxy", potential, sine_y_blocks, precision=high)
        outgoing = potential.reshape(devices, chunk_layers, columns)
        returned = lax.all_to_all(outgoing, both, 0, 0, tiled=True)
        if chunk + 2 < chunk_count:
            upcoming, returned = lax.optimization_barrier((sends[chunk + 2], returned))
            arrivals.append(lax.all_to_all(upcoming, both, 0, 0, tiled=True))
        line_field = line_field + lax.dot_general(
            returned, sine_z_parts[chunk], (((0, 1), (1, 2)), ((), ())), precision=high
        )
    padded = with_halo(line_field.reshape(cells_x, cells_y, NZ), (("row", 0), ("col", 1)), 1)
    flat_field = padded.reshape(-1)
    padded_y = cells_y + 2
    column_flat = column_in.reshape(-1)
    depth_flat = depth_in.reshape(-1)
    cell_row = column_flat // cells_y
    cell_col = column_flat % cells_y

    def field_at(row_step, col_step):
        index = ((cell_row + 1 + row_step) * padded_y + cell_col + 1 + col_step) * NZ + depth_flat
        return flat_field[index]

    found_x = -0.5 * (field_at(1, 0) - field_at(-1, 0))
    found_y = -0.5 * (field_at(0, 1) - field_at(0, -1))
    momentum_x = phase_in[:, 1, :] + kick_strength * found_x.reshape(sources, slot_count)
    momentum_y = phase_in[:, 3, :] + kick_strength * found_y.reshape(sources, slot_count)
    kicked = jnp.stack([momentum_x, momentum_y], axis=1).reshape(
        row_count, col_count, 2, slot_count
    )
    coord_blocks = (
        phase_in[:, 0, :].reshape(step_count, block_rows),
        momentum_x.reshape(step_count, block_rows),
        phase_in[:, 2, :].reshape(step_count, block_rows),
        momentum_y.reshape(step_count, block_rows),
    )
    slice_blocks = (depth_in // (NZ // SLICES)).reshape(step_count, block_rows)
    slice_ids = lax.broadcasted_iota(jnp.int32, (1, SLICES), 1)

    def gather_moments(running, element):
        coord_one, coord_two, coord_three, coord_four, block_slice, block_mass = element
        weighted_slices = jnp.where(block_slice[:, None] == slice_ids, block_mass[:, None], 0.0)
        basis = monomials([coord_one, coord_two, coord_three, coord_four], ORDER)
        moment_part = jnp.dot(
            basis, weighted_slices, precision=highest, preferred_element_type=jnp.float32
        )
        square_part = jnp.sum(weighted_slices * block_mass[:, None], axis=0)
        return ((running[0] + moment_part, running[1] + square_part), None)

    start_state = (
        jnp.zeros((basis_count(ORDER), SLICES), jnp.float32),
        jnp.zeros((SLICES,), jnp.float32),
    )
    (moment_sum, square_sum), unused_too = lax.scan(
        gather_moments, start_state, coord_blocks + (slice_blocks, mass_blocks)
    )
    flat_totals = jnp.concatenate([moment_sum.reshape(-1), square_sum])
    piece = -(-flat_totals.shape[0] // devices)
    flat_totals = jnp.pad(flat_totals, (0, piece * devices - flat_totals.shape[0]))
    own_piece = jnp.sum(
        lax.all_to_all(flat_totals.reshape(devices, piece), both, 0, 0, tiled=True), axis=0
    )
    totals = lax.all_to_all(
        jnp.broadcast_to(own_piece[None, :], (devices, piece)), both, 0, 0, tiled=True
    ).reshape(-1)
    moment_count = moment_sum.shape[0] * SLICES
    moment_total = totals[:moment_count].reshape(moment_sum.shape)
    square_total = totals[moment_count : moment_count + SLICES]
    slice_moments = moment_total / jnp.sqrt(square_total + epsilon)[None, :]
    return (kicked, slice_moments)


def momentum_shape(phase_in):
    return (phase_in.shape[0], phase_in.shape[1], phase_in.shape[3])


def solution(mesh):
    placed = (
        P(("row", "col"), None, None, None),
        P(("row", "col"), None, None),
        P(("row", "col"), None, None),
        P(("row", "col"), None, None),
        P(("row", "col"), None),
    )
    return jax.shard_map(
        body,
        mesh=mesh,
        in_specs=placed,
        out_specs=(P(("row", "col"), None, None, None), P()),
        check_vma=False,
    )
```

```python
import math

import jax
import jax.numpy as jnp
from jax import lax
from jax.sharding import PartitionSpec as P

NX = 256
NY = 256
NZ = 512
SLICES = 64
ORDER = 6


kick_strength = 8.0
epsilon = 1e-06
highest = lax.Precision.HIGHEST
high = lax.Precision.HIGH


def with_halo(block, sides, width):
    for axis, dim in sides:
        count = lax.axis_size(axis)
        forward = [(i, i + 1) for i in range(count - 1)]
        backward = [(target, source) for source, target in forward]
        low = lax.ppermute(
            lax.slice_in_dim(block, block.shape[dim] - width, None, axis=dim), axis, forward
        )
        high = lax.ppermute(lax.slice_in_dim(block, 0, width, axis=dim), axis, backward)
        block = jnp.concatenate([low, block, high], axis=dim)
    return block


def exponent_table(max_order):
    listing = []
    for power_one in range(max_order + 1):
        for power_two in range(max_order + 1):
            for power_three in range(max_order + 1):
                for power_four in range(max_order + 1):
                    if power_one + power_two + power_three + power_four <= max_order:
                        listing.append([power_one, power_two, power_three, power_four])
    return listing


def monomials(coords, max_order):
    power_lists = []
    for position in range(4):
        variable = coords[position]
        powers = [jnp.ones_like(variable)]
        for degree in range(max_order):
            powers.append(powers[-1] * variable)
        power_lists.append(powers)
    terms = []
    for entry in exponent_table(max_order):
        product = power_lists[0][entry[0]]
        for position in range(1, 4):
            product = product * power_lists[position][entry[position]]
        terms.append(product)
    return jnp.stack(terms)


def wave_grid(length):
    row_wave = lax.broadcasted_iota(jnp.int32, (length, length), 0) + 1
    col_wave = lax.broadcasted_iota(jnp.int32, (length, length), 1) + 1
    reduced = row_wave * col_wave % (2 * (length + 1))
    return (reduced.astype(jnp.float32) * (math.pi / (length + 1)), col_wave)


def sine_table(length):
    angles, col_wave = wave_grid(length)
    return math.sqrt(2.0 / (length + 1)) * jnp.sin(angles)


def sine_windows(length, blocks):
    block_length = length // blocks
    window = block_length + 2
    position = (
        lax.broadcasted_iota(jnp.int32, (blocks, window, length), 0) * block_length
        + lax.broadcasted_iota(jnp.int32, (blocks, window, length), 1)
        - 1
    )
    col_wave = lax.broadcasted_iota(jnp.int32, (blocks, window, length), 2) + 1
    reduced = (position + 1) * col_wave % (2 * (length + 1))
    angles = reduced.astype(jnp.float32) * (math.pi / (length + 1))
    values = math.sqrt(2.0 / (length + 1)) * jnp.sin(angles)
    inside = (position >= 0) & (position < length)
    return jnp.where(inside, values, 0.0)


def eigen_line(length):
    wave_index = lax.broadcasted_iota(jnp.int32, (length,), 0).astype(jnp.float32) + 1.0
    return 2.0 - 2.0 * jnp.cos(wave_index * (math.pi / (length + 1)))


def basis_count(max_order):
    return (max_order + 1) * (max_order + 2) * (max_order + 3) * (max_order + 4) // 24


def lookup_fields(field_x, field_y, column_blocks, depth_blocks):
    columns = field_x.shape[0]
    depth_total = field_x.shape[1]
    table = jnp.concatenate([field_x, field_y], axis=1)
    upper = table.astype(jnp.bfloat16)
    upper_wide = lax.optimization_barrier(upper).astype(jnp.float32)
    lower = (table - upper_wide).astype(jnp.bfloat16)
    column_ids = lax.broadcasted_iota(jnp.int32, (1, columns), 1)
    depth_ids = lax.broadcasted_iota(jnp.int32, (1, depth_total), 1)

    def pick(carry, element):
        block_column, block_depth = element
        picked = (block_column[:, None] == column_ids).astype(jnp.bfloat16)
        rows_found = jnp.dot(picked, upper, preferred_element_type=jnp.float32)
        rows_found = rows_found + jnp.dot(picked, lower, preferred_element_type=jnp.float32)
        chosen = block_depth[:, None] == depth_ids
        value_x = jnp.sum(jnp.where(chosen, rows_found[:, :depth_total], 0.0), axis=1)
        value_y = jnp.sum(jnp.where(chosen, rows_found[:, depth_total:], 0.0), axis=1)
        return (carry, (value_x, value_y))

    unused, (found_x, found_y) = lax.scan(
        pick, jnp.zeros((), jnp.float32), (column_blocks, depth_blocks)
    )
    return (found_x, found_y)


def body(particle_phase, particle_weight, cell_column, cell_depth, slot_counts):
    row_count = lax.axis_size("row")
    col_count = lax.axis_size("col")
    devices = row_count * col_count
    slot_count = particle_weight.shape[-1]
    cells_x = NX // row_count
    cells_y = NY // col_count
    columns = cells_x * cells_y
    layers = NZ // devices
    both = ("row", "col")
    live_slot = lax.broadcasted_iota(jnp.int32, particle_weight.shape, 2) < slot_counts[:, :, None]
    live_mass = jnp.where(live_slot, particle_weight.astype(jnp.float32), 0.0)
    packed = jnp.concatenate(
        [
            particle_phase,
            live_mass[:, :, None, :],
            cell_column.astype(jnp.float32)[:, :, None, :],
            cell_depth.astype(jnp.float32)[:, :, None, :],
        ],
        axis=2,
    ).reshape(devices, 7, slot_count)
    arrived = lax.all_to_all(packed, both, 0, 0, tiled=True)
    phase_in = arrived[:, 0:4, :]
    mass_in = arrived[:, 4, :]
    column_in = arrived[:, 5, :].astype(jnp.int32)
    depth_in = arrived[:, 6, :].astype(jnp.int32)
    sources = devices
    group_size = math.gcd(sources, max(1, 2048 // slot_count))
    step_count = sources // group_size
    block_rows = group_size * slot_count
    column_blocks = column_in.reshape(step_count, block_rows)
    depth_blocks = depth_in.reshape(step_count, block_rows)
    mass_blocks = mass_in.reshape(step_count, block_rows)
    column_ids = lax.broadcasted_iota(jnp.int32, (1, columns), 1)
    depth_ids = lax.broadcasted_iota(jnp.int32, (1, NZ), 1)

    def deposit(running, element):
        block_column, block_depth, block_mass = element
        picked = (block_column[:, None] == column_ids).astype(jnp.bfloat16)
        spread = jnp.where(
            block_depth[:, None] == depth_ids,
            block_mass.astype(jnp.bfloat16)[:, None],
            jnp.zeros((), jnp.bfloat16),
        )
        added = lax.dot_general(
            picked, spread, (((0,), (0,)), ((), ())), preferred_element_type=jnp.float32
        )
        return (running + added, None)

    density, unused = lax.scan(
        deposit, jnp.zeros((columns, NZ), jnp.float32), (column_blocks, depth_blocks, mass_blocks)
    )
    sine_x = sine_table(NX)
    sine_y = sine_table(NY)
    sine_z = sine_table(NZ)
    chunk_count = 2 if layers % 2 == 0 else 1
    chunk_layers = layers // chunk_count
    slab_index = lax.axis_index("row") * col_count + lax.axis_index("col")
    sine_z_slabs = sine_z.reshape(NZ, devices, layers)
    sine_x_windows = sine_windows(NX, row_count)
    sine_y_windows = sine_windows(NY, col_count)
    padded_columns = (cells_x + 2) * (cells_y + 2)
    line_field = jnp.zeros((padded_columns, NZ), jnp.float32)
    sine_z_parts = []
    sends = []
    for chunk in range(chunk_count):
        lower_layer = chunk * chunk_layers
        sine_z_part = sine_z_slabs[:, :, lower_layer : lower_layer + chunk_layers]
        sine_z_parts.append(sine_z_part)
        sends.append(
            lax.dot_general(sine_z_part, density, (((0,), (1,)), ((), ())), precision=high)
        )
    arrivals = [lax.all_to_all(sends[0], both, 0, 0, tiled=True)]
    if chunk_count > 1:
        arrivals.append(lax.all_to_all(sends[1], both, 0, 0, tiled=True))
    for chunk in range(chunk_count):
        lower_layer = chunk * chunk_layers
        slab_field = arrivals[chunk].reshape(row_count, col_count, chunk_layers, cells_x, cells_y)
        sine_y_blocks = sine_y.reshape(col_count, cells_y, NY)
        sine_x_blocks = sine_x.reshape(row_count, cells_x, NX)
        mixed = jnp.einsum("rczxy,cyl->zrxl", slab_field, sine_y_blocks, precision=high)
        mixed = jnp.einsum("zrxl,rxk->zkl", mixed, sine_x_blocks, precision=high)
        depth_wave = (
            slab_index * layers
            + lower_layer
            + lax.broadcasted_iota(jnp.int32, (chunk_layers,), 0)
        )
        depth_eigen = 2.0 - 2.0 * jnp.cos(
            (depth_wave.astype(jnp.float32) + 1.0) * (math.pi / (NZ + 1))
        )
        eigen_sum = (
            eigen_line(NX)[None, :, None]
            + eigen_line(NY)[None, None, :]
            + depth_eigen[:, None, None]
        )
        scaled = mixed / eigen_sum
        potential = jnp.einsum("zkl,rxk->zrxl", scaled, sine_x_windows, precision=high)
        potential = jnp.einsum("zrxl,cyl->rczxy", potential, sine_y_windows, precision=high)
        outgoing = potential.reshape(devices, chunk_layers, padded_columns)
        returned = lax.all_to_all(outgoing, both, 0, 0, tiled=True)
        if chunk + 2 < chunk_count:
            upcoming, returned = lax.optimization_barrier((sends[chunk + 2], returned))
            arrivals.append(lax.all_to_all(upcoming, both, 0, 0, tiled=True))
        line_field = line_field + lax.dot_general(
            returned, sine_z_parts[chunk], (((0, 1), (1, 2)), ((), ())), precision=high
        )
    padded = line_field.reshape(cells_x + 2, cells_y + 2, NZ)
    field_x = (-0.5 * (padded[2:, 1:-1] - padded[:-2, 1:-1])).reshape(columns, NZ)
    field_y = (-0.5 * (padded[1:-1, 2:] - padded[1:-1, :-2])).reshape(columns, NZ)
    found_x, found_y = lookup_fields(field_x, field_y, column_blocks, depth_blocks)
    momentum_x = phase_in[:, 1, :] + kick_strength * found_x.reshape(sources, slot_count)
    momentum_y = phase_in[:, 3, :] + kick_strength * found_y.reshape(sources, slot_count)
    kicked = jnp.stack([momentum_x, momentum_y], axis=1).reshape(
        row_count, col_count, 2, slot_count
    )
    coord_blocks = (
        phase_in[:, 0, :].reshape(step_count, block_rows),
        momentum_x.reshape(step_count, block_rows),
        phase_in[:, 2, :].reshape(step_count, block_rows),
        momentum_y.reshape(step_count, block_rows),
    )
    slice_blocks = (depth_in // (NZ // SLICES)).reshape(step_count, block_rows)
    slice_ids = lax.broadcasted_iota(jnp.int32, (1, SLICES), 1)

    def gather_moments(running, element):
        coord_one, coord_two, coord_three, coord_four, block_slice, block_mass = element
        weighted_slices = jnp.where(block_slice[:, None] == slice_ids, block_mass[:, None], 0.0)
        basis = monomials([coord_one, coord_two, coord_three, coord_four], ORDER)
        moment_part = jnp.dot(
            basis, weighted_slices, precision=highest, preferred_element_type=jnp.float32
        )
        square_part = jnp.sum(weighted_slices * block_mass[:, None], axis=0)
        return ((running[0] + moment_part, running[1] + square_part), None)

    start_state = (
        jnp.zeros((basis_count(ORDER), SLICES), jnp.float32),
        jnp.zeros((SLICES,), jnp.float32),
    )
    (moment_sum, square_sum), unused_too = lax.scan(
        gather_moments, start_state, coord_blocks + (slice_blocks, mass_blocks)
    )
    flat_totals = jnp.concatenate([moment_sum.reshape(-1), square_sum])
    piece = -(-flat_totals.shape[0] // devices)
    flat_totals = jnp.pad(flat_totals, (0, piece * devices - flat_totals.shape[0]))
    own_piece = jnp.sum(
        lax.all_to_all(flat_totals.reshape(devices, piece), both, 0, 0, tiled=True), axis=0
    )
    totals = lax.all_to_all(
        jnp.broadcast_to(own_piece[None, :], (devices, piece)), both, 0, 0, tiled=True
    ).reshape(-1)
    moment_count = moment_sum.shape[0] * SLICES
    moment_total = totals[:moment_count].reshape(moment_sum.shape)
    square_total = totals[moment_count : moment_count + SLICES]
    slice_moments = moment_total / jnp.sqrt(square_total + epsilon)[None, :]
    return (kicked, slice_moments)


def momentum_shape(phase_in):
    return (phase_in.shape[0], phase_in.shape[1], phase_in.shape[3])


def solution(mesh):
    placed = (
        P(("row", "col"), None, None, None),
        P(("row", "col"), None, None),
        P(("row", "col"), None, None),
        P(("row", "col"), None, None),
        P(("row", "col"), None),
    )
    return jax.shard_map(
        body,
        mesh=mesh,
        in_specs=placed,
        out_specs=(P(("row", "col"), None, None, None), P()),
        check_vma=False,
    )
```

```python
import math

import jax
import jax.numpy as jnp
from jax import lax
from jax.sharding import PartitionSpec as P

NX = 256
NY = 256
NZ = 512
SLICES = 64
ORDER = 6


kick_strength = 8.0
epsilon = 1e-06
highest = lax.Precision.HIGHEST
high = lax.Precision.HIGH


def with_halo(block, sides, width):
    for axis, dim in sides:
        count = lax.axis_size(axis)
        forward = [(i, i + 1) for i in range(count - 1)]
        backward = [(target, source) for source, target in forward]
        low = lax.ppermute(
            lax.slice_in_dim(block, block.shape[dim] - width, None, axis=dim), axis, forward
        )
        high = lax.ppermute(lax.slice_in_dim(block, 0, width, axis=dim), axis, backward)
        block = jnp.concatenate([low, block, high], axis=dim)
    return block


def exponent_table(max_order):
    listing = []
    for power_one in range(max_order + 1):
        for power_two in range(max_order + 1):
            for power_three in range(max_order + 1):
                for power_four in range(max_order + 1):
                    if power_one + power_two + power_three + power_four <= max_order:
                        listing.append([power_one, power_two, power_three, power_four])
    return listing


def monomials(coords, max_order):
    power_lists = []
    for position in range(4):
        variable = coords[position]
        powers = [jnp.ones_like(variable)]
        for degree in range(max_order):
            powers.append(powers[-1] * variable)
        power_lists.append(powers)
    terms = []
    for entry in exponent_table(max_order):
        product = power_lists[0][entry[0]]
        for position in range(1, 4):
            product = product * power_lists[position][entry[position]]
        terms.append(product)
    return jnp.stack(terms)


def wave_grid(length):
    row_wave = lax.broadcasted_iota(jnp.int32, (length, length), 0) + 1
    col_wave = lax.broadcasted_iota(jnp.int32, (length, length), 1) + 1
    reduced = row_wave * col_wave % (2 * (length + 1))
    return (reduced.astype(jnp.float32) * (math.pi / (length + 1)), col_wave)


def sine_table(length):
    angles, col_wave = wave_grid(length)
    return math.sqrt(2.0 / (length + 1)) * jnp.sin(angles)


def eigen_line(length):
    wave_index = lax.broadcasted_iota(jnp.int32, (length,), 0).astype(jnp.float32) + 1.0
    return 2.0 - 2.0 * jnp.cos(wave_index * (math.pi / (length + 1)))


def basis_count(max_order):
    return (max_order + 1) * (max_order + 2) * (max_order + 3) * (max_order + 4) // 24


def lookup_fields(field_x, field_y, column_blocks, depth_blocks):
    columns = field_x.shape[0]
    depth_total = field_x.shape[1]
    table = jnp.concatenate([field_x, field_y], axis=1)
    upper = table.astype(jnp.bfloat16)
    upper_wide = lax.optimization_barrier(upper).astype(jnp.float32)
    lower = (table - upper_wide).astype(jnp.bfloat16)
    column_ids = lax.broadcasted_iota(jnp.int32, (1, columns), 1)
    depth_ids = lax.broadcasted_iota(jnp.int32, (1, depth_total), 1)

    def pick(carry, element):
        block_column, block_depth = element
        picked = (block_column[:, None] == column_ids).astype(jnp.bfloat16)
        rows_found = jnp.dot(picked, upper, preferred_element_type=jnp.float32)
        rows_found = rows_found + jnp.dot(picked, lower, preferred_element_type=jnp.float32)
        chosen = block_depth[:, None] == depth_ids
        value_x = jnp.sum(jnp.where(chosen, rows_found[:, :depth_total], 0.0), axis=1)
        value_y = jnp.sum(jnp.where(chosen, rows_found[:, depth_total:], 0.0), axis=1)
        return (carry, (value_x, value_y))

    unused, (found_x, found_y) = lax.scan(
        pick, jnp.zeros((), jnp.float32), (column_blocks, depth_blocks)
    )
    return (found_x, found_y)


def body(particle_phase, particle_weight, cell_column, cell_depth, slot_counts):
    row_count = lax.axis_size("row")
    col_count = lax.axis_size("col")
    devices = row_count * col_count
    slot_count = particle_weight.shape[-1]
    cells_x = NX // row_count
    cells_y = NY // col_count
    columns = cells_x * cells_y
    layers = NZ // devices
    both = ("row", "col")
    live_slot = lax.broadcasted_iota(jnp.int32, particle_weight.shape, 2) < slot_counts[:, :, None]
    live_mass = jnp.where(live_slot, particle_weight.astype(jnp.float32), 0.0)
    packed = jnp.concatenate(
        [
            particle_phase,
            live_mass[:, :, None, :],
            cell_column.astype(jnp.float32)[:, :, None, :],
            cell_depth.astype(jnp.float32)[:, :, None, :],
        ],
        axis=2,
    ).reshape(devices, 7, slot_count)
    arrived = lax.all_to_all(packed, both, 0, 0, tiled=True)
    phase_in = arrived[:, 0:4, :]
    mass_in = arrived[:, 4, :]
    column_in = arrived[:, 5, :].astype(jnp.int32)
    depth_in = arrived[:, 6, :].astype(jnp.int32)
    sources = devices
    group_size = math.gcd(sources, max(1, 2048 // slot_count))
    step_count = sources // group_size
    block_rows = group_size * slot_count
    column_blocks = column_in.reshape(step_count, block_rows)
    depth_blocks = depth_in.reshape(step_count, block_rows)
    mass_blocks = mass_in.reshape(step_count, block_rows)
    column_ids = lax.broadcasted_iota(jnp.int32, (1, columns), 1)
    depth_ids = lax.broadcasted_iota(jnp.int32, (1, NZ), 1)

    def deposit(running, element):
        block_column, block_depth, block_mass = element
        picked = (block_column[:, None] == column_ids).astype(jnp.bfloat16)
        spread = jnp.where(
            block_depth[:, None] == depth_ids,
            block_mass.astype(jnp.bfloat16)[:, None],
            jnp.zeros((), jnp.bfloat16),
        )
        added = lax.dot_general(
            picked, spread, (((0,), (0,)), ((), ())), preferred_element_type=jnp.float32
        )
        return (running + added, None)

    density, unused = lax.scan(
        deposit, jnp.zeros((columns, NZ), jnp.float32), (column_blocks, depth_blocks, mass_blocks)
    )
    sine_x = sine_table(NX)
    sine_y = sine_table(NY)
    sine_z = sine_table(NZ)
    chunk_count = 4 if layers % 4 == 0 else 1
    chunk_layers = layers // chunk_count
    slab_index = lax.axis_index("row") * col_count + lax.axis_index("col")
    sine_z_slabs = sine_z.reshape(NZ, devices, layers)
    line_field = jnp.zeros((columns, NZ), jnp.float32)
    sine_z_parts = []
    sends = []
    for chunk in range(chunk_count):
        lower_layer = chunk * chunk_layers
        sine_z_part = sine_z_slabs[:, :, lower_layer : lower_layer + chunk_layers]
        sine_z_parts.append(sine_z_part)
        sends.append(
            lax.dot_general(sine_z_part, density, (((0,), (1,)), ((), ())), precision=high)
        )
    arrivals = [lax.all_to_all(sends[0], both, 0, 0, tiled=True)]
    if chunk_count > 1:
        arrivals.append(lax.all_to_all(sends[1], both, 0, 0, tiled=True))
    for chunk in range(chunk_count):
        lower_layer = chunk * chunk_layers
        slab_field = arrivals[chunk].reshape(row_count, col_count, chunk_layers, cells_x, cells_y)
        sine_y_blocks = sine_y.reshape(col_count, cells_y, NY)
        sine_x_blocks = sine_x.reshape(row_count, cells_x, NX)
        mixed = jnp.einsum("rczxy,cyl->zrxl", slab_field, sine_y_blocks, precision=high)
        mixed = jnp.einsum("zrxl,rxk->zkl", mixed, sine_x_blocks, precision=high)
        depth_wave = (
            slab_index * layers
            + lower_layer
            + lax.broadcasted_iota(jnp.int32, (chunk_layers,), 0)
        )
        depth_eigen = 2.0 - 2.0 * jnp.cos(
            (depth_wave.astype(jnp.float32) + 1.0) * (math.pi / (NZ + 1))
        )
        eigen_sum = (
            eigen_line(NX)[None, :, None]
            + eigen_line(NY)[None, None, :]
            + depth_eigen[:, None, None]
        )
        scaled = mixed / eigen_sum
        potential = jnp.einsum("zkl,rxk->zrxl", scaled, sine_x_blocks, precision=high)
        potential = jnp.einsum("zrxl,cyl->rczxy", potential, sine_y_blocks, precision=high)
        outgoing = potential.reshape(devices, chunk_layers, columns)
        returned = lax.all_to_all(outgoing, both, 0, 0, tiled=True)
        if chunk + 2 < chunk_count:
            upcoming, returned = lax.optimization_barrier((sends[chunk + 2], returned))
            arrivals.append(lax.all_to_all(upcoming, both, 0, 0, tiled=True))
        line_field = line_field + lax.dot_general(
            returned, sine_z_parts[chunk], (((0, 1), (1, 2)), ((), ())), precision=high
        )
    padded = with_halo(line_field.reshape(cells_x, cells_y, NZ), (("row", 0), ("col", 1)), 1)
    field_x = (-0.5 * (padded[2:, 1:-1] - padded[:-2, 1:-1])).reshape(columns, NZ)
    field_y = (-0.5 * (padded[1:-1, 2:] - padded[1:-1, :-2])).reshape(columns, NZ)
    found_x, found_y = lookup_fields(field_x, field_y, column_blocks, depth_blocks)
    momentum_x = phase_in[:, 1, :] + kick_strength * found_x.reshape(sources, slot_count)
    momentum_y = phase_in[:, 3, :] + kick_strength * found_y.reshape(sources, slot_count)
    kicked = jnp.stack([momentum_x, momentum_y], axis=1).reshape(
        row_count, col_count, 2, slot_count
    )
    coord_blocks = (
        phase_in[:, 0, :].reshape(step_count, block_rows),
        momentum_x.reshape(step_count, block_rows),
        phase_in[:, 2, :].reshape(step_count, block_rows),
        momentum_y.reshape(step_count, block_rows),
    )
    slice_blocks = (depth_in // (NZ // SLICES)).reshape(step_count, block_rows)
    slice_ids = lax.broadcasted_iota(jnp.int32, (1, SLICES), 1)

    def gather_moments(running, element):
        coord_one, coord_two, coord_three, coord_four, block_slice, block_mass = element
        weighted_slices = jnp.where(block_slice[:, None] == slice_ids, block_mass[:, None], 0.0)
        basis = monomials([coord_one, coord_two, coord_three, coord_four], ORDER)
        moment_part = jnp.dot(
            basis, weighted_slices, precision=highest, preferred_element_type=jnp.float32
        )
        square_part = jnp.sum(weighted_slices * block_mass[:, None], axis=0)
        return ((running[0] + moment_part, running[1] + square_part), None)

    start_state = (
        jnp.zeros((basis_count(ORDER), SLICES), jnp.float32),
        jnp.zeros((SLICES,), jnp.float32),
    )
    (moment_sum, square_sum), unused_too = lax.scan(
        gather_moments, start_state, coord_blocks + (slice_blocks, mass_blocks)
    )
    flat_totals = jnp.concatenate([moment_sum.reshape(-1), square_sum])
    piece = -(-flat_totals.shape[0] // devices)
    flat_totals = jnp.pad(flat_totals, (0, piece * devices - flat_totals.shape[0]))
    own_piece = jnp.sum(
        lax.all_to_all(flat_totals.reshape(devices, piece), both, 0, 0, tiled=True), axis=0
    )
    totals = lax.all_to_all(
        jnp.broadcast_to(own_piece[None, :], (devices, piece)), both, 0, 0, tiled=True
    ).reshape(-1)
    moment_count = moment_sum.shape[0] * SLICES
    moment_total = totals[:moment_count].reshape(moment_sum.shape)
    square_total = totals[moment_count : moment_count + SLICES]
    slice_moments = moment_total / jnp.sqrt(square_total + epsilon)[None, :]
    return (kicked, slice_moments)


def momentum_shape(phase_in):
    return (phase_in.shape[0], phase_in.shape[1], phase_in.shape[3])


def solution(mesh):
    placed = (
        P(("row", "col"), None, None, None),
        P(("row", "col"), None, None),
        P(("row", "col"), None, None),
        P(("row", "col"), None, None),
        P(("row", "col"), None),
    )
    return jax.shard_map(
        body,
        mesh=mesh,
        in_specs=placed,
        out_specs=(P(("row", "col"), None, None, None), P()),
        check_vma=False,
    )
```

```python
import math

import jax
import jax.numpy as jnp
from jax import lax
from jax.sharding import PartitionSpec as P

NX = 256
NY = 256
NZ = 512
SLICES = 64
ORDER = 6


kick_strength = 8.0
epsilon = 1e-06
highest = lax.Precision.HIGHEST
high = lax.Precision.HIGH


def with_halo(block, sides, width):
    for axis, dim in sides:
        count = lax.axis_size(axis)
        forward = [(i, i + 1) for i in range(count - 1)]
        backward = [(target, source) for source, target in forward]
        low = lax.ppermute(
            lax.slice_in_dim(block, block.shape[dim] - width, None, axis=dim), axis, forward
        )
        high = lax.ppermute(lax.slice_in_dim(block, 0, width, axis=dim), axis, backward)
        block = jnp.concatenate([low, block, high], axis=dim)
    return block


def exponent_table(max_order):
    listing = []
    for power_one in range(max_order + 1):
        for power_two in range(max_order + 1):
            for power_three in range(max_order + 1):
                for power_four in range(max_order + 1):
                    if power_one + power_two + power_three + power_four <= max_order:
                        listing.append([power_one, power_two, power_three, power_four])
    return listing


def monomials(coords, max_order):
    power_lists = []
    for position in range(4):
        variable = coords[position]
        powers = [jnp.ones_like(variable)]
        for degree in range(max_order):
            powers.append(powers[-1] * variable)
        power_lists.append(powers)
    terms = []
    for entry in exponent_table(max_order):
        product = power_lists[0][entry[0]]
        for position in range(1, 4):
            product = product * power_lists[position][entry[position]]
        terms.append(product)
    return jnp.stack(terms)


def wave_grid(length):
    row_wave = lax.broadcasted_iota(jnp.int32, (length, length), 0) + 1
    col_wave = lax.broadcasted_iota(jnp.int32, (length, length), 1) + 1
    reduced = row_wave * col_wave % (2 * (length + 1))
    return (reduced.astype(jnp.float32) * (math.pi / (length + 1)), col_wave)


def sine_table(length):
    angles, col_wave = wave_grid(length)
    return math.sqrt(2.0 / (length + 1)) * jnp.sin(angles)


def eigen_line(length):
    wave_index = lax.broadcasted_iota(jnp.int32, (length,), 0).astype(jnp.float32) + 1.0
    return 2.0 - 2.0 * jnp.cos(wave_index * (math.pi / (length + 1)))


def basis_count(max_order):
    return (max_order + 1) * (max_order + 2) * (max_order + 3) * (max_order + 4) // 24


def lookup_fields(field_x, field_y, column_blocks, depth_blocks):
    columns = field_x.shape[0]
    depth_total = field_x.shape[1]
    table = jnp.concatenate([field_x, field_y], axis=1)
    upper = table.astype(jnp.bfloat16)
    upper_wide = lax.optimization_barrier(upper).astype(jnp.float32)
    lower = (table - upper_wide).astype(jnp.bfloat16)
    column_ids = lax.broadcasted_iota(jnp.int32, (1, columns), 1)
    depth_ids = lax.broadcasted_iota(jnp.int32, (1, depth_total), 1)

    def pick(carry, element):
        block_column, block_depth = element
        picked = (block_column[:, None] == column_ids).astype(jnp.bfloat16)
        rows_found = jnp.dot(picked, upper, preferred_element_type=jnp.float32)
        rows_found = rows_found + jnp.dot(picked, lower, preferred_element_type=jnp.float32)
        chosen = block_depth[:, None] == depth_ids
        value_x = jnp.sum(jnp.where(chosen, rows_found[:, :depth_total], 0.0), axis=1)
        value_y = jnp.sum(jnp.where(chosen, rows_found[:, depth_total:], 0.0), axis=1)
        return (carry, (value_x, value_y))

    unused, (found_x, found_y) = lax.scan(
        pick, jnp.zeros((), jnp.float32), (column_blocks, depth_blocks)
    )
    return (found_x, found_y)


def body(particle_phase, particle_weight, cell_column, cell_depth, slot_counts):
    row_count = lax.axis_size("row")
    col_count = lax.axis_size("col")
    devices = row_count * col_count
    slot_count = particle_weight.shape[-1]
    cells_x = NX // row_count
    cells_y = NY // col_count
    columns = cells_x * cells_y
    layers = NZ // devices
    both = ("row", "col")
    live_slot = lax.broadcasted_iota(jnp.int32, particle_weight.shape, 2) < slot_counts[:, :, None]
    live_mass = jnp.where(live_slot, particle_weight.astype(jnp.float32), 0.0)
    packed = jnp.concatenate(
        [
            particle_phase,
            live_mass[:, :, None, :],
            cell_column.astype(jnp.float32)[:, :, None, :],
            cell_depth.astype(jnp.float32)[:, :, None, :],
        ],
        axis=2,
    ).reshape(devices, 7, slot_count)
    arrived = lax.all_to_all(packed, both, 0, 0, tiled=True)
    phase_in = arrived[:, 0:4, :]
    mass_in = arrived[:, 4, :]
    column_in = arrived[:, 5, :].astype(jnp.int32)
    depth_in = arrived[:, 6, :].astype(jnp.int32)
    sources = devices
    group_size = math.gcd(sources, max(1, 2048 // slot_count))
    step_count = sources // group_size
    block_rows = group_size * slot_count
    column_blocks = column_in.reshape(step_count, block_rows)
    depth_blocks = depth_in.reshape(step_count, block_rows)
    mass_blocks = mass_in.reshape(step_count, block_rows)
    column_ids = lax.broadcasted_iota(jnp.int32, (1, columns), 1)
    depth_ids = lax.broadcasted_iota(jnp.int32, (1, NZ), 1)

    def deposit(running, element):
        block_column, block_depth, block_mass = element
        picked = (block_column[:, None] == column_ids).astype(jnp.bfloat16)
        spread = jnp.where(
            block_depth[:, None] == depth_ids,
            block_mass.astype(jnp.bfloat16)[:, None],
            jnp.zeros((), jnp.bfloat16),
        )
        added = lax.dot_general(
            picked, spread, (((0,), (0,)), ((), ())), preferred_element_type=jnp.float32
        )
        return (running + added, None)

    density, unused = lax.scan(
        deposit, jnp.zeros((columns, NZ), jnp.float32), (column_blocks, depth_blocks, mass_blocks)
    )
    sine_x = sine_table(NX)
    sine_y = sine_table(NY)
    sine_z = sine_table(NZ)
    chunk_count = 2 if layers % 2 == 0 else 1
    chunk_layers = layers // chunk_count
    slab_index = lax.axis_index("row") * col_count + lax.axis_index("col")
    sine_z_slabs = sine_z.reshape(NZ, devices, layers)
    line_field = jnp.zeros((columns, NZ), jnp.float32)
    sine_z_parts = []
    sends = []
    for chunk in range(chunk_count):
        lower_layer = chunk * chunk_layers
        sine_z_part = sine_z_slabs[:, :, lower_layer : lower_layer + chunk_layers]
        sine_z_parts.append(sine_z_part)
        sends.append(
            lax.dot_general(sine_z_part, density, (((0,), (1,)), ((), ())), precision=high)
        )
    arrivals = [lax.all_to_all(sends[0], both, 0, 0, tiled=True)]
    if chunk_count > 1:
        arrivals.append(lax.all_to_all(sends[1], both, 0, 0, tiled=True))
    for chunk in range(chunk_count):
        lower_layer = chunk * chunk_layers
        slab_field = arrivals[chunk].reshape(row_count, col_count, chunk_layers, cells_x, cells_y)
        sine_y_blocks = sine_y.reshape(col_count, cells_y, NY)
        sine_x_blocks = sine_x.reshape(row_count, cells_x, NX)
        mixed = jnp.einsum("rczxy,cyl->zrxl", slab_field, sine_y_blocks, precision=high)
        mixed = jnp.einsum("zrxl,rxk->zkl", mixed, sine_x_blocks, precision=high)
        depth_wave = (
            slab_index * layers
            + lower_layer
            + lax.broadcasted_iota(jnp.int32, (chunk_layers,), 0)
        )
        depth_eigen = 2.0 - 2.0 * jnp.cos(
            (depth_wave.astype(jnp.float32) + 1.0) * (math.pi / (NZ + 1))
        )
        eigen_sum = (
            eigen_line(NX)[None, :, None]
            + eigen_line(NY)[None, None, :]
            + depth_eigen[:, None, None]
        )
        scaled = mixed / eigen_sum
        potential = jnp.einsum("zkl,rxk->zrxl", scaled, sine_x_blocks, precision=high)
        potential = jnp.einsum("zrxl,cyl->rczxy", potential, sine_y_blocks, precision=high)
        outgoing = potential.reshape(devices, chunk_layers, columns)
        returned = lax.all_to_all(outgoing, both, 0, 0, tiled=True)
        if chunk + 2 < chunk_count:
            upcoming, returned = lax.optimization_barrier((sends[chunk + 2], returned))
            arrivals.append(lax.all_to_all(upcoming, both, 0, 0, tiled=True))
        line_field = line_field + lax.dot_general(
            returned, sine_z_parts[chunk], (((0, 1), (1, 2)), ((), ())), precision=high
        )
    line_grid = line_field.reshape(cells_x, cells_y, NZ)
    padded_x = with_halo(line_grid, (("row", 0),), 1)
    padded_y = with_halo(line_grid, (("col", 1),), 1)
    field_x = (-0.5 * (padded_x[2:] - padded_x[:-2])).reshape(columns, NZ)
    field_y = (-0.5 * (padded_y[:, 2:] - padded_y[:, :-2])).reshape(columns, NZ)
    found_x, found_y = lookup_fields(field_x, field_y, column_blocks, depth_blocks)
    momentum_x = phase_in[:, 1, :] + kick_strength * found_x.reshape(sources, slot_count)
    momentum_y = phase_in[:, 3, :] + kick_strength * found_y.reshape(sources, slot_count)
    kicked = jnp.stack([momentum_x, momentum_y], axis=1).reshape(
        row_count, col_count, 2, slot_count
    )
    coord_blocks = (
        phase_in[:, 0, :].reshape(step_count, block_rows),
        momentum_x.reshape(step_count, block_rows),
        phase_in[:, 2, :].reshape(step_count, block_rows),
        momentum_y.reshape(step_count, block_rows),
    )
    slice_blocks = (depth_in // (NZ // SLICES)).reshape(step_count, block_rows)
    slice_ids = lax.broadcasted_iota(jnp.int32, (1, SLICES), 1)

    def gather_moments(running, element):
        coord_one, coord_two, coord_three, coord_four, block_slice, block_mass = element
        weighted_slices = jnp.where(block_slice[:, None] == slice_ids, block_mass[:, None], 0.0)
        basis = monomials([coord_one, coord_two, coord_three, coord_four], ORDER)
        moment_part = jnp.dot(
            basis, weighted_slices, precision=highest, preferred_element_type=jnp.float32
        )
        square_part = jnp.sum(weighted_slices * block_mass[:, None], axis=0)
        return ((running[0] + moment_part, running[1] + square_part), None)

    start_state = (
        jnp.zeros((basis_count(ORDER), SLICES), jnp.float32),
        jnp.zeros((SLICES,), jnp.float32),
    )
    (moment_sum, square_sum), unused_too = lax.scan(
        gather_moments, start_state, coord_blocks + (slice_blocks, mass_blocks)
    )
    flat_totals = jnp.concatenate([moment_sum.reshape(-1), square_sum])
    piece = -(-flat_totals.shape[0] // devices)
    flat_totals = jnp.pad(flat_totals, (0, piece * devices - flat_totals.shape[0]))
    own_piece = jnp.sum(
        lax.all_to_all(flat_totals.reshape(devices, piece), both, 0, 0, tiled=True), axis=0
    )
    totals = lax.all_to_all(
        jnp.broadcast_to(own_piece[None, :], (devices, piece)), both, 0, 0, tiled=True
    ).reshape(-1)
    moment_count = moment_sum.shape[0] * SLICES
    moment_total = totals[:moment_count].reshape(moment_sum.shape)
    square_total = totals[moment_count : moment_count + SLICES]
    slice_moments = moment_total / jnp.sqrt(square_total + epsilon)[None, :]
    return (kicked, slice_moments)


def momentum_shape(phase_in):
    return (phase_in.shape[0], phase_in.shape[1], phase_in.shape[3])


def solution(mesh):
    placed = (
        P(("row", "col"), None, None, None),
        P(("row", "col"), None, None),
        P(("row", "col"), None, None),
        P(("row", "col"), None, None),
        P(("row", "col"), None),
    )
    return jax.shard_map(
        body,
        mesh=mesh,
        in_specs=placed,
        out_specs=(P(("row", "col"), None, None, None), P()),
        check_vma=False,
    )
```

```python
import math

import jax
import jax.numpy as jnp
from jax import lax
from jax.sharding import PartitionSpec as P

NX = 256
NY = 256
NZ = 512
SLICES = 64
ORDER = 6


kick_strength = 8.0
epsilon = 1e-06
highest = lax.Precision.HIGHEST
high = lax.Precision.HIGH


def with_halo(block, sides, width):
    for axis, dim in sides:
        count = lax.axis_size(axis)
        forward = [(i, i + 1) for i in range(count - 1)]
        backward = [(target, source) for source, target in forward]
        low = lax.ppermute(
            lax.slice_in_dim(block, block.shape[dim] - width, None, axis=dim), axis, forward
        )
        high = lax.ppermute(lax.slice_in_dim(block, 0, width, axis=dim), axis, backward)
        block = jnp.concatenate([low, block, high], axis=dim)
    return block


def exponent_table(max_order):
    listing = []
    for power_one in range(max_order + 1):
        for power_two in range(max_order + 1):
            for power_three in range(max_order + 1):
                for power_four in range(max_order + 1):
                    if power_one + power_two + power_three + power_four <= max_order:
                        listing.append([power_one, power_two, power_three, power_four])
    return listing


def monomials(coords, max_order):
    power_lists = []
    for position in range(4):
        variable = coords[position]
        powers = [jnp.ones_like(variable)]
        for degree in range(max_order):
            powers.append(powers[-1] * variable)
        power_lists.append(powers)
    terms = []
    for entry in exponent_table(max_order):
        product = power_lists[0][entry[0]]
        for position in range(1, 4):
            product = product * power_lists[position][entry[position]]
        terms.append(product)
    return jnp.stack(terms)


def wave_grid(length):
    row_wave = lax.broadcasted_iota(jnp.int32, (length, length), 0) + 1
    col_wave = lax.broadcasted_iota(jnp.int32, (length, length), 1) + 1
    reduced = row_wave * col_wave % (2 * (length + 1))
    return (reduced.astype(jnp.float32) * (math.pi / (length + 1)), col_wave)


def sine_table(length):
    angles, col_wave = wave_grid(length)
    return math.sqrt(2.0 / (length + 1)) * jnp.sin(angles)


def eigen_line(length):
    wave_index = lax.broadcasted_iota(jnp.int32, (length,), 0).astype(jnp.float32) + 1.0
    return 2.0 - 2.0 * jnp.cos(wave_index * (math.pi / (length + 1)))


def basis_count(max_order):
    return (max_order + 1) * (max_order + 2) * (max_order + 3) * (max_order + 4) // 24


def lookup_fields(field_x, field_y, column_blocks, depth_blocks):
    columns = field_x.shape[0]
    depth_total = field_x.shape[1]
    table = jnp.concatenate([field_x, field_y], axis=1)
    upper = table.astype(jnp.bfloat16)
    upper_wide = lax.optimization_barrier(upper).astype(jnp.float32)
    lower = (table - upper_wide).astype(jnp.bfloat16)
    column_ids = lax.broadcasted_iota(jnp.int32, (1, columns), 1)
    depth_ids = lax.broadcasted_iota(jnp.int32, (1, depth_total), 1)

    def pick(carry, element):
        block_column, block_depth = element
        picked = (block_column[:, None] == column_ids).astype(jnp.bfloat16)
        rows_found = jnp.dot(picked, upper, preferred_element_type=jnp.float32)
        rows_found = rows_found + jnp.dot(picked, lower, preferred_element_type=jnp.float32)
        chosen = block_depth[:, None] == depth_ids
        value_x = jnp.sum(jnp.where(chosen, rows_found[:, :depth_total], 0.0), axis=1)
        value_y = jnp.sum(jnp.where(chosen, rows_found[:, depth_total:], 0.0), axis=1)
        return (carry, (value_x, value_y))

    unused, (found_x, found_y) = lax.scan(
        pick, jnp.zeros((), jnp.float32), (column_blocks, depth_blocks)
    )
    return (found_x, found_y)


def body(particle_phase, particle_weight, cell_column, cell_depth, slot_counts):
    row_count = lax.axis_size("row")
    col_count = lax.axis_size("col")
    devices = row_count * col_count
    slot_count = particle_weight.shape[-1]
    cells_x = NX // row_count
    cells_y = NY // col_count
    columns = cells_x * cells_y
    layers = NZ // devices
    both = ("row", "col")
    live_slot = lax.broadcasted_iota(jnp.int32, particle_weight.shape, 2) < slot_counts[:, :, None]
    live_mass = jnp.where(live_slot, particle_weight.astype(jnp.float32), 0.0)
    packed = jnp.concatenate(
        [
            particle_phase,
            live_mass[:, :, None, :],
            cell_column.astype(jnp.float32)[:, :, None, :],
            cell_depth.astype(jnp.float32)[:, :, None, :],
        ],
        axis=2,
    ).reshape(devices, 7, slot_count)
    arrived = lax.all_to_all(packed, both, 0, 0, tiled=True)
    phase_in = arrived[:, 0:4, :]
    mass_in = arrived[:, 4, :]
    column_in = arrived[:, 5, :].astype(jnp.int32)
    depth_in = arrived[:, 6, :].astype(jnp.int32)
    sources = devices
    group_size = math.gcd(sources, max(1, 2048 // slot_count))
    step_count = sources // group_size
    block_rows = group_size * slot_count
    column_blocks = column_in.reshape(step_count, block_rows)
    depth_blocks = depth_in.reshape(step_count, block_rows)
    mass_blocks = mass_in.reshape(step_count, block_rows)
    column_ids = lax.broadcasted_iota(jnp.int32, (1, columns), 1)
    depth_ids = lax.broadcasted_iota(jnp.int32, (1, NZ), 1)

    def deposit(running, element):
        block_column, block_depth, block_mass = element
        picked = (block_column[:, None] == column_ids).astype(jnp.bfloat16)
        spread = jnp.where(
            block_depth[:, None] == depth_ids,
            block_mass.astype(jnp.bfloat16)[:, None],
            jnp.zeros((), jnp.bfloat16),
        )
        added = lax.dot_general(
            picked, spread, (((0,), (0,)), ((), ())), preferred_element_type=jnp.float32
        )
        return (running + added, None)

    density, unused = lax.scan(
        deposit, jnp.zeros((columns, NZ), jnp.float32), (column_blocks, depth_blocks, mass_blocks)
    )
    sine_x = sine_table(NX)
    sine_y = sine_table(NY)
    sine_z = sine_table(NZ)
    chunk_count = 2 if layers % 2 == 0 else 1
    chunk_layers = layers // chunk_count
    slab_index = lax.axis_index("row") * col_count + lax.axis_index("col")
    sine_z_slabs = sine_z.reshape(NZ, devices, layers)
    line_field = jnp.zeros((columns, NZ), jnp.float32)
    sine_z_parts = []
    sends = []
    for chunk in range(chunk_count):
        lower_layer = chunk * chunk_layers
        sine_z_part = sine_z_slabs[:, :, lower_layer : lower_layer + chunk_layers]
        sine_z_parts.append(sine_z_part)
        sends.append(
            lax.dot_general(sine_z_part, density, (((0,), (1,)), ((), ())), precision=high)
        )
    arrivals = [lax.all_to_all(sends[0], both, 0, 0, tiled=True)]
    if chunk_count > 1:
        arrivals.append(lax.all_to_all(sends[1], both, 0, 0, tiled=True))
    for chunk in range(chunk_count):
        lower_layer = chunk * chunk_layers
        slab_field = arrivals[chunk].reshape(row_count, col_count, chunk_layers, cells_x, cells_y)
        sine_y_blocks = sine_y.reshape(col_count, cells_y, NY)
        sine_x_blocks = sine_x.reshape(row_count, cells_x, NX)
        mixed = jnp.einsum("rczxy,cyl->zrxl", slab_field, sine_y_blocks, precision=high)
        mixed = jnp.einsum("zrxl,rxk->zkl", mixed, sine_x_blocks, precision=high)
        depth_wave = (
            slab_index * layers
            + lower_layer
            + lax.broadcasted_iota(jnp.int32, (chunk_layers,), 0)
        )
        depth_eigen = 2.0 - 2.0 * jnp.cos(
            (depth_wave.astype(jnp.float32) + 1.0) * (math.pi / (NZ + 1))
        )
        eigen_sum = (
            eigen_line(NX)[None, :, None]
            + eigen_line(NY)[None, None, :]
            + depth_eigen[:, None, None]
        )
        scaled = mixed / eigen_sum
        potential = jnp.einsum("zkl,rxk->zrxl", scaled, sine_x_blocks, precision=high)
        potential = jnp.einsum("zrxl,cyl->rczxy", potential, sine_y_blocks, precision=high)
        outgoing = potential.reshape(devices, chunk_layers, columns)
        returned = lax.all_to_all(outgoing, both, 0, 0, tiled=True)
        if chunk + 2 < chunk_count:
            upcoming, returned = lax.optimization_barrier((sends[chunk + 2], returned))
            arrivals.append(lax.all_to_all(upcoming, both, 0, 0, tiled=True))
        line_field = line_field + lax.dot_general(
            returned, sine_z_parts[chunk], (((0, 1), (1, 2)), ((), ())), precision=high
        )
    line_grid = line_field.reshape(cells_x, cells_y, NZ)
    padded_x = with_halo(line_grid, (("row", 0),), 1)
    padded_y = with_halo(line_grid, (("col", 1),), 1)
    field_x = (-0.5 * (padded_x[2:] - padded_x[:-2])).reshape(columns, NZ)
    field_y = (-0.5 * (padded_y[:, 2:] - padded_y[:, :-2])).reshape(columns, NZ)
    found_x, found_y = lookup_fields(field_x, field_y, column_blocks, depth_blocks)
    momentum_x = phase_in[:, 1, :] + kick_strength * found_x.reshape(sources, slot_count)
    momentum_y = phase_in[:, 3, :] + kick_strength * found_y.reshape(sources, slot_count)
    kicked = jnp.stack([momentum_x, momentum_y], axis=1).reshape(
        row_count, col_count, 2, slot_count
    )
    coord_blocks = (
        phase_in[:, 0, :].reshape(step_count, block_rows),
        momentum_x.reshape(step_count, block_rows),
        phase_in[:, 2, :].reshape(step_count, block_rows),
        momentum_y.reshape(step_count, block_rows),
    )
    slice_blocks = (depth_in // (NZ // SLICES)).reshape(step_count, block_rows)
    slice_ids = lax.broadcasted_iota(jnp.int32, (1, SLICES), 1)

    def gather_moments(running, element):
        coord_one, coord_two, coord_three, coord_four, block_slice, block_mass = element
        weighted_slices = jnp.where(block_slice[:, None] == slice_ids, block_mass[:, None], 0.0)
        basis = monomials([coord_one, coord_two, coord_three, coord_four], ORDER)
        moment_part = jnp.dot(
            basis, weighted_slices, precision=highest, preferred_element_type=jnp.float32
        )
        square_part = jnp.sum(weighted_slices * block_mass[:, None], axis=0)
        return ((running[0] + moment_part, running[1] + square_part), None)

    start_state = (
        jnp.zeros((basis_count(ORDER), SLICES), jnp.float32),
        jnp.zeros((SLICES,), jnp.float32),
    )
    (moment_sum, square_sum), unused_too = lax.scan(
        gather_moments, start_state, coord_blocks + (slice_blocks, mass_blocks)
    )
    flat_totals = jnp.concatenate([moment_sum.reshape(-1), square_sum])
    totals = lax.psum(lax.psum(flat_totals, "row"), "col")
    moment_count = moment_sum.shape[0] * SLICES
    moment_total = totals[:moment_count].reshape(moment_sum.shape)
    square_total = totals[moment_count : moment_count + SLICES]
    slice_moments = moment_total / jnp.sqrt(square_total + epsilon)[None, :]
    return (kicked, slice_moments)


def momentum_shape(phase_in):
    return (phase_in.shape[0], phase_in.shape[1], phase_in.shape[3])


def solution(mesh):
    placed = (
        P(("row", "col"), None, None, None),
        P(("row", "col"), None, None),
        P(("row", "col"), None, None),
        P(("row", "col"), None, None),
        P(("row", "col"), None),
    )
    return jax.shard_map(
        body,
        mesh=mesh,
        in_specs=placed,
        out_specs=(P(("row", "col"), None, None, None), P()),
        check_vma=False,
    )
```

```python
import math

import jax
import jax.numpy as jnp
from jax import lax
from jax.sharding import PartitionSpec as P

NX = 256
NY = 256
NZ = 512
SLICES = 64
ORDER = 6


kick_strength = 8.0
epsilon = 1e-06
highest = lax.Precision.HIGHEST
high = lax.Precision.HIGH


def with_halo(block, sides, width):
    for axis, dim in sides:
        count = lax.axis_size(axis)
        forward = [(i, i + 1) for i in range(count - 1)]
        backward = [(target, source) for source, target in forward]
        low = lax.ppermute(
            lax.slice_in_dim(block, block.shape[dim] - width, None, axis=dim), axis, forward
        )
        high = lax.ppermute(lax.slice_in_dim(block, 0, width, axis=dim), axis, backward)
        block = jnp.concatenate([low, block, high], axis=dim)
    return block


def exponent_table(max_order):
    listing = []
    for power_one in range(max_order + 1):
        for power_two in range(max_order + 1):
            for power_three in range(max_order + 1):
                for power_four in range(max_order + 1):
                    if power_one + power_two + power_three + power_four <= max_order:
                        listing.append([power_one, power_two, power_three, power_four])
    return listing


def monomials(coords, max_order):
    power_lists = []
    for position in range(4):
        variable = coords[position]
        powers = [jnp.ones_like(variable)]
        for degree in range(max_order):
            powers.append(powers[-1] * variable)
        power_lists.append(powers)
    terms = []
    for entry in exponent_table(max_order):
        product = power_lists[0][entry[0]]
        for position in range(1, 4):
            product = product * power_lists[position][entry[position]]
        terms.append(product)
    return jnp.stack(terms)


def wave_grid(length):
    row_wave = lax.broadcasted_iota(jnp.int32, (length, length), 0) + 1
    col_wave = lax.broadcasted_iota(jnp.int32, (length, length), 1) + 1
    reduced = row_wave * col_wave % (2 * (length + 1))
    return (reduced.astype(jnp.float32) * (math.pi / (length + 1)), col_wave)


def sine_table(length):
    angles, col_wave = wave_grid(length)
    return math.sqrt(2.0 / (length + 1)) * jnp.sin(angles)


def eigen_line(length):
    wave_index = lax.broadcasted_iota(jnp.int32, (length,), 0).astype(jnp.float32) + 1.0
    return 2.0 - 2.0 * jnp.cos(wave_index * (math.pi / (length + 1)))


def basis_count(max_order):
    return (max_order + 1) * (max_order + 2) * (max_order + 3) * (max_order + 4) // 24


def lookup_fields(field_x, field_y, column_blocks, depth_blocks):
    columns = field_x.shape[0]
    depth_total = field_x.shape[1]
    table = jnp.concatenate([field_x, field_y], axis=1)
    upper = table.astype(jnp.bfloat16)
    upper_wide = lax.optimization_barrier(upper).astype(jnp.float32)
    lower = (table - upper_wide).astype(jnp.bfloat16)
    column_ids = lax.broadcasted_iota(jnp.int32, (1, columns), 1)
    depth_ids = lax.broadcasted_iota(jnp.int32, (1, depth_total), 1)

    def pick(carry, element):
        block_column, block_depth = element
        picked = (block_column[:, None] == column_ids).astype(jnp.bfloat16)
        rows_found = jnp.dot(picked, upper, preferred_element_type=jnp.float32)
        rows_found = rows_found + jnp.dot(picked, lower, preferred_element_type=jnp.float32)
        chosen = block_depth[:, None] == depth_ids
        value_x = jnp.sum(jnp.where(chosen, rows_found[:, :depth_total], 0.0), axis=1)
        value_y = jnp.sum(jnp.where(chosen, rows_found[:, depth_total:], 0.0), axis=1)
        return (carry, (value_x, value_y))

    unused, (found_x, found_y) = lax.scan(
        pick, jnp.zeros((), jnp.float32), (column_blocks, depth_blocks)
    )
    return (found_x, found_y)


def shift_along(block, axis, forward):
    count = lax.axis_size(axis)
    pairs = [(i, i + 1) for i in range(count - 1)]
    if not forward:
        pairs = [(target, source) for source, target in pairs]
    return lax.ppermute(block, axis, pairs)


def lookup_faces(faces, column_blocks, depth_blocks, cells_x, cells_y):
    depth_total = faces.shape[1]
    upper = faces.astype(jnp.bfloat16)
    upper_wide = lax.optimization_barrier(upper).astype(jnp.float32)
    lower = (faces - upper_wide).astype(jnp.bfloat16)
    face_ids = lax.broadcasted_iota(jnp.int32, (1, faces.shape[0]), 1)
    depth_ids = lax.broadcasted_iota(jnp.int32, (1, depth_total), 1)
    half = jnp.asarray(0.5, jnp.bfloat16)
    zero = jnp.zeros((), jnp.bfloat16)

    def pick(carry, element):
        block_column, block_depth = element
        cx = (block_column // cells_y)[:, None]
        cy = (block_column % cells_y)[:, None]
        weight_x = jnp.where((face_ids == cy) & (cx == 0), half, zero) - jnp.where(
            (face_ids == cells_y + cy) & (cx == cells_x - 1), half, zero
        )
        weight_y = jnp.where(
            (face_ids == 2 * cells_y + cx) & (cy == 0), half, zero
        ) - jnp.where((face_ids == 2 * cells_y + cells_x + cx) & (cy == cells_y - 1), half, zero)
        weights = jnp.concatenate([weight_x, weight_y], axis=0)
        rows = jnp.dot(weights, upper, preferred_element_type=jnp.float32)
        rows = rows + jnp.dot(weights, lower, preferred_element_type=jnp.float32)
        count = block_column.shape[0]
        chosen = (block_depth[:, None] == depth_ids)[None]
        values = jnp.sum(jnp.where(chosen, rows.reshape(2, count, depth_total), 0.0), axis=2)
        return (carry, (values[0], values[1]))

    unused, (found_x, found_y) = lax.scan(
        pick, jnp.zeros((), jnp.float32), (column_blocks, depth_blocks)
    )
    return (found_x, found_y)


def body(particle_phase, particle_weight, cell_column, cell_depth, slot_counts):
    row_count = lax.axis_size("row")
    col_count = lax.axis_size("col")
    devices = row_count * col_count
    slot_count = particle_weight.shape[-1]
    cells_x = NX // row_count
    cells_y = NY // col_count
    columns = cells_x * cells_y
    layers = NZ // devices
    both = ("row", "col")
    live_slot = lax.broadcasted_iota(jnp.int32, particle_weight.shape, 2) < slot_counts[:, :, None]
    live_mass = jnp.where(live_slot, particle_weight.astype(jnp.float32), 0.0)
    packed = jnp.concatenate(
        [
            particle_phase,
            live_mass[:, :, None, :],
            cell_column.astype(jnp.float32)[:, :, None, :],
            cell_depth.astype(jnp.float32)[:, :, None, :],
        ],
        axis=2,
    ).reshape(devices, 7, slot_count)
    arrived = lax.all_to_all(packed, both, 0, 0, tiled=True)
    phase_in = arrived[:, 0:4, :]
    mass_in = arrived[:, 4, :]
    column_in = arrived[:, 5, :].astype(jnp.int32)
    depth_in = arrived[:, 6, :].astype(jnp.int32)
    sources = devices
    group_size = math.gcd(sources, max(1, 2048 // slot_count))
    step_count = sources // group_size
    block_rows = group_size * slot_count
    column_blocks = column_in.reshape(step_count, block_rows)
    depth_blocks = depth_in.reshape(step_count, block_rows)
    mass_blocks = mass_in.reshape(step_count, block_rows)
    column_ids = lax.broadcasted_iota(jnp.int32, (1, columns), 1)
    depth_ids = lax.broadcasted_iota(jnp.int32, (1, NZ), 1)

    def deposit(running, element):
        block_column, block_depth, block_mass = element
        picked = (block_column[:, None] == column_ids).astype(jnp.bfloat16)
        spread = jnp.where(
            block_depth[:, None] == depth_ids,
            block_mass.astype(jnp.bfloat16)[:, None],
            jnp.zeros((), jnp.bfloat16),
        )
        added = lax.dot_general(
            picked, spread, (((0,), (0,)), ((), ())), preferred_element_type=jnp.float32
        )
        return (running + added, None)

    density, unused = lax.scan(
        deposit, jnp.zeros((columns, NZ), jnp.float32), (column_blocks, depth_blocks, mass_blocks)
    )
    sine_x = sine_table(NX)
    sine_y = sine_table(NY)
    sine_z = sine_table(NZ)
    chunk_count = 2 if layers % 2 == 0 else 1
    chunk_layers = layers // chunk_count
    slab_index = lax.axis_index("row") * col_count + lax.axis_index("col")
    sine_z_slabs = sine_z.reshape(NZ, devices, layers)
    line_field = jnp.zeros((columns, NZ), jnp.float32)
    sine_z_parts = []
    sends = []
    for chunk in range(chunk_count):
        lower_layer = chunk * chunk_layers
        sine_z_part = sine_z_slabs[:, :, lower_layer : lower_layer + chunk_layers]
        sine_z_parts.append(sine_z_part)
        sends.append(
            lax.dot_general(sine_z_part, density, (((0,), (1,)), ((), ())), precision=high)
        )
    arrivals = [lax.all_to_all(sends[0], both, 0, 0, tiled=True)]
    if chunk_count > 1:
        arrivals.append(lax.all_to_all(sends[1], both, 0, 0, tiled=True))
    for chunk in range(chunk_count):
        lower_layer = chunk * chunk_layers
        slab_field = arrivals[chunk].reshape(row_count, col_count, chunk_layers, cells_x, cells_y)
        sine_y_blocks = sine_y.reshape(col_count, cells_y, NY)
        sine_x_blocks = sine_x.reshape(row_count, cells_x, NX)
        mixed = jnp.einsum("rczxy,cyl->zrxl", slab_field, sine_y_blocks, precision=high)
        mixed = jnp.einsum("zrxl,rxk->zkl", mixed, sine_x_blocks, precision=high)
        depth_wave = (
            slab_index * layers
            + lower_layer
            + lax.broadcasted_iota(jnp.int32, (chunk_layers,), 0)
        )
        depth_eigen = 2.0 - 2.0 * jnp.cos(
            (depth_wave.astype(jnp.float32) + 1.0) * (math.pi / (NZ + 1))
        )
        eigen_sum = (
            eigen_line(NX)[None, :, None]
            + eigen_line(NY)[None, None, :]
            + depth_eigen[:, None, None]
        )
        scaled = mixed / eigen_sum
        potential = jnp.einsum("zkl,rxk->zrxl", scaled, sine_x_blocks, precision=high)
        potential = jnp.einsum("zrxl,cyl->rczxy", potential, sine_y_blocks, precision=high)
        outgoing = potential.reshape(devices, chunk_layers, columns)
        returned = lax.all_to_all(outgoing, both, 0, 0, tiled=True)
        if chunk + 2 < chunk_count:
            upcoming, returned = lax.optimization_barrier((sends[chunk + 2], returned))
            arrivals.append(lax.all_to_all(upcoming, both, 0, 0, tiled=True))
        line_field = line_field + lax.dot_general(
            returned, sine_z_parts[chunk], (((0, 1), (1, 2)), ((), ())), precision=high
        )
    line_grid = line_field.reshape(cells_x, cells_y, NZ)
    faces = jnp.concatenate(
        [
            shift_along(line_grid[cells_x - 1], "row", True),
            shift_along(line_grid[0], "row", False),
            shift_along(line_grid[:, cells_y - 1], "col", True),
            shift_along(line_grid[:, 0], "col", False),
        ],
        axis=0,
    )
    zero_x = jnp.pad(line_grid, ((1, 1), (0, 0), (0, 0)))
    zero_y = jnp.pad(line_grid, ((0, 0), (1, 1), (0, 0)))
    field_x = (-0.5 * (zero_x[2:] - zero_x[:-2])).reshape(columns, NZ)
    field_y = (-0.5 * (zero_y[:, 2:] - zero_y[:, :-2])).reshape(columns, NZ)
    inner_x, inner_y = lookup_fields(field_x, field_y, column_blocks, depth_blocks)
    edge_x, edge_y = lookup_faces(faces, column_blocks, depth_blocks, cells_x, cells_y)
    found_x = inner_x + edge_x
    found_y = inner_y + edge_y
    momentum_x = phase_in[:, 1, :] + kick_strength * found_x.reshape(sources, slot_count)
    momentum_y = phase_in[:, 3, :] + kick_strength * found_y.reshape(sources, slot_count)
    kicked = jnp.stack([momentum_x, momentum_y], axis=1).reshape(
        row_count, col_count, 2, slot_count
    )
    coord_blocks = (
        phase_in[:, 0, :].reshape(step_count, block_rows),
        momentum_x.reshape(step_count, block_rows),
        phase_in[:, 2, :].reshape(step_count, block_rows),
        momentum_y.reshape(step_count, block_rows),
    )
    slice_blocks = (depth_in // (NZ // SLICES)).reshape(step_count, block_rows)
    slice_ids = lax.broadcasted_iota(jnp.int32, (1, SLICES), 1)

    def gather_moments(running, element):
        coord_one, coord_two, coord_three, coord_four, block_slice, block_mass = element
        weighted_slices = jnp.where(block_slice[:, None] == slice_ids, block_mass[:, None], 0.0)
        basis = monomials([coord_one, coord_two, coord_three, coord_four], ORDER)
        moment_part = jnp.dot(
            basis, weighted_slices, precision=highest, preferred_element_type=jnp.float32
        )
        square_part = jnp.sum(weighted_slices * block_mass[:, None], axis=0)
        return ((running[0] + moment_part, running[1] + square_part), None)

    start_state = (
        jnp.zeros((basis_count(ORDER), SLICES), jnp.float32),
        jnp.zeros((SLICES,), jnp.float32),
    )
    (moment_sum, square_sum), unused_too = lax.scan(
        gather_moments, start_state, coord_blocks + (slice_blocks, mass_blocks)
    )
    flat_totals = jnp.concatenate([moment_sum.reshape(-1), square_sum])
    piece = -(-flat_totals.shape[0] // devices)
    flat_totals = jnp.pad(flat_totals, (0, piece * devices - flat_totals.shape[0]))
    own_piece = jnp.sum(
        lax.all_to_all(flat_totals.reshape(devices, piece), both, 0, 0, tiled=True), axis=0
    )
    totals = lax.all_to_all(
        jnp.broadcast_to(own_piece[None, :], (devices, piece)), both, 0, 0, tiled=True
    ).reshape(-1)
    moment_count = moment_sum.shape[0] * SLICES
    moment_total = totals[:moment_count].reshape(moment_sum.shape)
    square_total = totals[moment_count : moment_count + SLICES]
    slice_moments = moment_total / jnp.sqrt(square_total + epsilon)[None, :]
    return (kicked, slice_moments)


def momentum_shape(phase_in):
    return (phase_in.shape[0], phase_in.shape[1], phase_in.shape[3])


def solution(mesh):
    placed = (
        P(("row", "col"), None, None, None),
        P(("row", "col"), None, None),
        P(("row", "col"), None, None),
        P(("row", "col"), None, None),
        P(("row", "col"), None),
    )
    return jax.shard_map(
        body,
        mesh=mesh,
        in_specs=placed,
        out_specs=(P(("row", "col"), None, None, None), P()),
        check_vma=False,
    )
```

```python
import math

import jax
import jax.numpy as jnp
from jax import lax
from jax.sharding import PartitionSpec as P

NX = 256
NY = 256
NZ = 512
SLICES = 64
ORDER = 6


kick_strength = 8.0
epsilon = 1e-06
highest = lax.Precision.HIGHEST
high = lax.Precision.HIGH


def with_halo(block, sides, width):
    for axis, dim in sides:
        count = lax.axis_size(axis)
        forward = [(i, i + 1) for i in range(count - 1)]
        backward = [(target, source) for source, target in forward]
        low = lax.ppermute(
            lax.slice_in_dim(block, block.shape[dim] - width, None, axis=dim), axis, forward
        )
        high = lax.ppermute(lax.slice_in_dim(block, 0, width, axis=dim), axis, backward)
        block = jnp.concatenate([low, block, high], axis=dim)
    return block


def exponent_table(max_order):
    listing = []
    for power_one in range(max_order + 1):
        for power_two in range(max_order + 1):
            for power_three in range(max_order + 1):
                for power_four in range(max_order + 1):
                    if power_one + power_two + power_three + power_four <= max_order:
                        listing.append([power_one, power_two, power_three, power_four])
    return listing


def monomials(coords, max_order):
    power_lists = []
    for position in range(4):
        variable = coords[position]
        powers = [jnp.ones_like(variable)]
        for degree in range(max_order):
            powers.append(powers[-1] * variable)
        power_lists.append(powers)
    terms = []
    for entry in exponent_table(max_order):
        product = power_lists[0][entry[0]]
        for position in range(1, 4):
            product = product * power_lists[position][entry[position]]
        terms.append(product)
    return jnp.stack(terms)


def wave_grid(length):
    row_wave = lax.broadcasted_iota(jnp.int32, (length, length), 0) + 1
    col_wave = lax.broadcasted_iota(jnp.int32, (length, length), 1) + 1
    reduced = row_wave * col_wave % (2 * (length + 1))
    return (reduced.astype(jnp.float32) * (math.pi / (length + 1)), col_wave)


def sine_table(length):
    angles, col_wave = wave_grid(length)
    return math.sqrt(2.0 / (length + 1)) * jnp.sin(angles)


def eigen_line(length):
    wave_index = lax.broadcasted_iota(jnp.int32, (length,), 0).astype(jnp.float32) + 1.0
    return 2.0 - 2.0 * jnp.cos(wave_index * (math.pi / (length + 1)))


def basis_count(max_order):
    return (max_order + 1) * (max_order + 2) * (max_order + 3) * (max_order + 4) // 24


def lookup_fields(field_x, field_y, column_blocks, depth_blocks):
    columns = field_x.shape[0]
    depth_total = field_x.shape[1]
    table = jnp.concatenate([field_x, field_y], axis=1)
    upper = table.astype(jnp.bfloat16)
    upper_wide = lax.optimization_barrier(upper).astype(jnp.float32)
    lower = (table - upper_wide).astype(jnp.bfloat16)
    column_ids = lax.broadcasted_iota(jnp.int32, (1, columns), 1)
    depth_ids = lax.broadcasted_iota(jnp.int32, (1, depth_total), 1)

    def pick(carry, element):
        block_column, block_depth = element
        picked = (block_column[:, None] == column_ids).astype(jnp.bfloat16)
        rows_found = jnp.dot(picked, upper, preferred_element_type=jnp.float32)
        rows_found = rows_found + jnp.dot(picked, lower, preferred_element_type=jnp.float32)
        chosen = block_depth[:, None] == depth_ids
        value_x = jnp.sum(jnp.where(chosen, rows_found[:, :depth_total], 0.0), axis=1)
        value_y = jnp.sum(jnp.where(chosen, rows_found[:, depth_total:], 0.0), axis=1)
        return (carry, (value_x, value_y))

    unused, (found_x, found_y) = lax.scan(
        pick, jnp.zeros((), jnp.float32), (column_blocks, depth_blocks)
    )
    return (found_x, found_y)


def shift_along(block, axis, forward):
    count = lax.axis_size(axis)
    pairs = [(i, i + 1) for i in range(count - 1)]
    if not forward:
        pairs = [(target, source) for source, target in pairs]
    return lax.ppermute(block, axis, pairs)


def body(particle_phase, particle_weight, cell_column, cell_depth, slot_counts):
    row_count = lax.axis_size("row")
    col_count = lax.axis_size("col")
    devices = row_count * col_count
    slot_count = particle_weight.shape[-1]
    cells_x = NX // row_count
    cells_y = NY // col_count
    columns = cells_x * cells_y
    layers = NZ // devices
    both = ("row", "col")
    live_slot = lax.broadcasted_iota(jnp.int32, particle_weight.shape, 2) < slot_counts[:, :, None]
    live_mass = jnp.where(live_slot, particle_weight.astype(jnp.float32), 0.0)
    packed = jnp.concatenate(
        [
            particle_phase,
            live_mass[:, :, None, :],
            cell_column.astype(jnp.float32)[:, :, None, :],
            cell_depth.astype(jnp.float32)[:, :, None, :],
        ],
        axis=2,
    ).reshape(devices, 7, slot_count)
    arrived = lax.all_to_all(packed, both, 0, 0, tiled=True)
    phase_in = arrived[:, 0:4, :]
    mass_in = arrived[:, 4, :]
    column_in = arrived[:, 5, :].astype(jnp.int32)
    depth_in = arrived[:, 6, :].astype(jnp.int32)
    sources = devices
    group_size = math.gcd(sources, max(1, 2048 // slot_count))
    step_count = sources // group_size
    block_rows = group_size * slot_count
    column_blocks = column_in.reshape(step_count, block_rows)
    depth_blocks = depth_in.reshape(step_count, block_rows)
    mass_blocks = mass_in.reshape(step_count, block_rows)
    column_ids = lax.broadcasted_iota(jnp.int32, (1, columns), 1)
    depth_ids = lax.broadcasted_iota(jnp.int32, (1, NZ), 1)

    def deposit(running, element):
        block_column, block_depth, block_mass = element
        picked = (block_column[:, None] == column_ids).astype(jnp.bfloat16)
        spread = jnp.where(
            block_depth[:, None] == depth_ids,
            block_mass.astype(jnp.bfloat16)[:, None],
            jnp.zeros((), jnp.bfloat16),
        )
        added = lax.dot_general(
            picked, spread, (((0,), (0,)), ((), ())), preferred_element_type=jnp.float32
        )
        return (running + added, None)

    density, unused = lax.scan(
        deposit, jnp.zeros((columns, NZ), jnp.float32), (column_blocks, depth_blocks, mass_blocks)
    )
    sine_x = sine_table(NX)
    sine_y = sine_table(NY)
    sine_z = sine_table(NZ)
    chunk_count = 2 if layers % 2 == 0 else 1
    chunk_layers = layers // chunk_count
    slab_index = lax.axis_index("row") * col_count + lax.axis_index("col")
    sine_z_slabs = sine_z.reshape(NZ, devices, layers)
    line_parts = []
    sine_z_parts = []
    sends = []
    for chunk in range(chunk_count):
        lower_layer = chunk * chunk_layers
        sine_z_part = sine_z_slabs[:, :, lower_layer : lower_layer + chunk_layers]
        sine_z_parts.append(sine_z_part)
        sends.append(
            lax.dot_general(sine_z_part, density, (((0,), (1,)), ((), ())), precision=high)
        )
    arrivals = [lax.all_to_all(sends[0], both, 0, 0, tiled=True)]
    if chunk_count > 1:
        arrivals.append(lax.all_to_all(sends[1], both, 0, 0, tiled=True))
    for chunk in range(chunk_count):
        lower_layer = chunk * chunk_layers
        slab_field = arrivals[chunk].reshape(row_count, col_count, chunk_layers, cells_x, cells_y)
        sine_y_blocks = sine_y.reshape(col_count, cells_y, NY)
        sine_x_blocks = sine_x.reshape(row_count, cells_x, NX)
        mixed = jnp.einsum("rczxy,cyl->zrxl", slab_field, sine_y_blocks, precision=high)
        mixed = jnp.einsum("zrxl,rxk->zkl", mixed, sine_x_blocks, precision=high)
        depth_wave = (
            slab_index * layers
            + lower_layer
            + lax.broadcasted_iota(jnp.int32, (chunk_layers,), 0)
        )
        depth_eigen = 2.0 - 2.0 * jnp.cos(
            (depth_wave.astype(jnp.float32) + 1.0) * (math.pi / (NZ + 1))
        )
        eigen_sum = (
            eigen_line(NX)[None, :, None]
            + eigen_line(NY)[None, None, :]
            + depth_eigen[:, None, None]
        )
        scaled = mixed / eigen_sum
        potential = jnp.einsum("zkl,rxk->zrxl", scaled, sine_x_blocks, precision=high)
        potential = jnp.einsum("zrxl,cyl->rczxy", potential, sine_y_blocks, precision=high)
        outgoing = potential.reshape(devices, chunk_layers, columns)
        returned = lax.all_to_all(outgoing, both, 0, 0, tiled=True)
        if chunk + 2 < chunk_count:
            upcoming, returned = lax.optimization_barrier((sends[chunk + 2], returned))
            arrivals.append(lax.all_to_all(upcoming, both, 0, 0, tiled=True))
        line_parts.append(
            lax.dot_general(
                returned, sine_z_parts[chunk], (((0, 1), (1, 2)), ((), ())), precision=high
            ).reshape(cells_x, cells_y, NZ)
        )
    def face(pick):
        return sum([pick(part) for part in line_parts[1:]], pick(line_parts[0]))

    line_grid = sum(line_parts[1:], line_parts[0])
    padded_x = jnp.concatenate(
        [
            shift_along(face(lambda part: part[cells_x - 1 :]), "row", True),
            line_grid,
            shift_along(face(lambda part: part[:1]), "row", False),
        ],
        axis=0,
    )
    padded_y = jnp.concatenate(
        [
            shift_along(face(lambda part: part[:, cells_y - 1 :]), "col", True),
            line_grid,
            shift_along(face(lambda part: part[:, :1]), "col", False),
        ],
        axis=1,
    )
    field_x = (-0.5 * (padded_x[2:] - padded_x[:-2])).reshape(columns, NZ)
    field_y = (-0.5 * (padded_y[:, 2:] - padded_y[:, :-2])).reshape(columns, NZ)
    found_x, found_y = lookup_fields(field_x, field_y, column_blocks, depth_blocks)
    momentum_x = phase_in[:, 1, :] + kick_strength * found_x.reshape(sources, slot_count)
    momentum_y = phase_in[:, 3, :] + kick_strength * found_y.reshape(sources, slot_count)
    kicked = jnp.stack([momentum_x, momentum_y], axis=1).reshape(
        row_count, col_count, 2, slot_count
    )
    coord_blocks = (
        phase_in[:, 0, :].reshape(step_count, block_rows),
        momentum_x.reshape(step_count, block_rows),
        phase_in[:, 2, :].reshape(step_count, block_rows),
        momentum_y.reshape(step_count, block_rows),
    )
    slice_blocks = (depth_in // (NZ // SLICES)).reshape(step_count, block_rows)
    slice_ids = lax.broadcasted_iota(jnp.int32, (1, SLICES), 1)

    def gather_moments(running, element):
        coord_one, coord_two, coord_three, coord_four, block_slice, block_mass = element
        weighted_slices = jnp.where(block_slice[:, None] == slice_ids, block_mass[:, None], 0.0)
        basis = monomials([coord_one, coord_two, coord_three, coord_four], ORDER)
        moment_part = jnp.dot(
            basis, weighted_slices, precision=highest, preferred_element_type=jnp.float32
        )
        square_part = jnp.sum(weighted_slices * block_mass[:, None], axis=0)
        return ((running[0] + moment_part, running[1] + square_part), None)

    start_state = (
        jnp.zeros((basis_count(ORDER), SLICES), jnp.float32),
        jnp.zeros((SLICES,), jnp.float32),
    )
    (moment_sum, square_sum), unused_too = lax.scan(
        gather_moments, start_state, coord_blocks + (slice_blocks, mass_blocks)
    )
    flat_totals = jnp.concatenate([moment_sum.reshape(-1), square_sum])
    piece = -(-flat_totals.shape[0] // devices)
    flat_totals = jnp.pad(flat_totals, (0, piece * devices - flat_totals.shape[0]))
    own_piece = jnp.sum(
        lax.all_to_all(flat_totals.reshape(devices, piece), both, 0, 0, tiled=True), axis=0
    )
    totals = lax.all_to_all(
        jnp.broadcast_to(own_piece[None, :], (devices, piece)), both, 0, 0, tiled=True
    ).reshape(-1)
    moment_count = moment_sum.shape[0] * SLICES
    moment_total = totals[:moment_count].reshape(moment_sum.shape)
    square_total = totals[moment_count : moment_count + SLICES]
    slice_moments = moment_total / jnp.sqrt(square_total + epsilon)[None, :]
    return (kicked, slice_moments)


def momentum_shape(phase_in):
    return (phase_in.shape[0], phase_in.shape[1], phase_in.shape[3])


def solution(mesh):
    placed = (
        P(("row", "col"), None, None, None),
        P(("row", "col"), None, None),
        P(("row", "col"), None, None),
        P(("row", "col"), None, None),
        P(("row", "col"), None),
    )
    return jax.shard_map(
        body,
        mesh=mesh,
        in_specs=placed,
        out_specs=(P(("row", "col"), None, None, None), P()),
        check_vma=False,
    )
```

```python
import math

import jax
import jax.numpy as jnp
from jax import lax
from jax.sharding import PartitionSpec as P

NX = 256
NY = 256
NZ = 512
SLICES = 64
ORDER = 6


kick_strength = 8.0
epsilon = 1e-06
highest = lax.Precision.HIGHEST
high = lax.Precision.HIGH


def with_halo(block, sides, width):
    for axis, dim in sides:
        count = lax.axis_size(axis)
        forward = [(i, i + 1) for i in range(count - 1)]
        backward = [(target, source) for source, target in forward]
        low = lax.ppermute(
            lax.slice_in_dim(block, block.shape[dim] - width, None, axis=dim), axis, forward
        )
        high = lax.ppermute(lax.slice_in_dim(block, 0, width, axis=dim), axis, backward)
        block = jnp.concatenate([low, block, high], axis=dim)
    return block


def exponent_table(max_order):
    listing = []
    for power_one in range(max_order + 1):
        for power_two in range(max_order + 1):
            for power_three in range(max_order + 1):
                for power_four in range(max_order + 1):
                    if power_one + power_two + power_three + power_four <= max_order:
                        listing.append([power_one, power_two, power_three, power_four])
    return listing


def monomials(coords, max_order):
    power_lists = []
    for position in range(4):
        variable = coords[position]
        powers = [jnp.ones_like(variable)]
        for degree in range(max_order):
            powers.append(powers[-1] * variable)
        power_lists.append(powers)
    terms = []
    for entry in exponent_table(max_order):
        product = power_lists[0][entry[0]]
        for position in range(1, 4):
            product = product * power_lists[position][entry[position]]
        terms.append(product)
    return jnp.stack(terms)


def wave_grid(length):
    row_wave = lax.broadcasted_iota(jnp.int32, (length, length), 0) + 1
    col_wave = lax.broadcasted_iota(jnp.int32, (length, length), 1) + 1
    reduced = row_wave * col_wave % (2 * (length + 1))
    return (reduced.astype(jnp.float32) * (math.pi / (length + 1)), col_wave)


def sine_table(length):
    angles, col_wave = wave_grid(length)
    return math.sqrt(2.0 / (length + 1)) * jnp.sin(angles)


def eigen_line(length):
    wave_index = lax.broadcasted_iota(jnp.int32, (length,), 0).astype(jnp.float32) + 1.0
    return 2.0 - 2.0 * jnp.cos(wave_index * (math.pi / (length + 1)))


def basis_count(max_order):
    return (max_order + 1) * (max_order + 2) * (max_order + 3) * (max_order + 4) // 24


def lookup_fields(field_x, field_y, column_blocks, depth_blocks):
    columns = field_x.shape[0]
    depth_total = field_x.shape[1]
    table = jnp.concatenate([field_x, field_y], axis=1)
    upper = table.astype(jnp.bfloat16)
    upper_wide = lax.optimization_barrier(upper).astype(jnp.float32)
    lower = (table - upper_wide).astype(jnp.bfloat16)
    column_ids = lax.broadcasted_iota(jnp.int32, (1, columns), 1)
    depth_ids = lax.broadcasted_iota(jnp.int32, (1, depth_total), 1)

    def pick(carry, element):
        block_column, block_depth = element
        picked = (block_column[:, None] == column_ids).astype(jnp.bfloat16)
        rows_found = jnp.dot(picked, upper, preferred_element_type=jnp.float32)
        rows_found = rows_found + jnp.dot(picked, lower, preferred_element_type=jnp.float32)
        chosen = block_depth[:, None] == depth_ids
        value_x = jnp.sum(jnp.where(chosen, rows_found[:, :depth_total], 0.0), axis=1)
        value_y = jnp.sum(jnp.where(chosen, rows_found[:, depth_total:], 0.0), axis=1)
        return (carry, (value_x, value_y))

    unused, (found_x, found_y) = lax.scan(
        pick, jnp.zeros((), jnp.float32), (column_blocks, depth_blocks)
    )
    return (found_x, found_y)


def shift_along(block, axis, forward):
    count = lax.axis_size(axis)
    pairs = [(i, i + 1) for i in range(count - 1)]
    if not forward:
        pairs = [(target, source) for source, target in pairs]
    return lax.ppermute(block, axis, pairs)


def body(particle_phase, particle_weight, cell_column, cell_depth, slot_counts):
    row_count = lax.axis_size("row")
    col_count = lax.axis_size("col")
    devices = row_count * col_count
    slot_count = particle_weight.shape[-1]
    cells_x = NX // row_count
    cells_y = NY // col_count
    columns = cells_x * cells_y
    layers = NZ // devices
    both = ("row", "col")
    live_slot = lax.broadcasted_iota(jnp.int32, particle_weight.shape, 2) < slot_counts[:, :, None]
    live_mass = jnp.where(live_slot, particle_weight.astype(jnp.float32), 0.0)
    packed = jnp.concatenate(
        [
            particle_phase,
            live_mass[:, :, None, :],
            cell_column.astype(jnp.float32)[:, :, None, :],
            cell_depth.astype(jnp.float32)[:, :, None, :],
        ],
        axis=2,
    ).reshape(devices, 7, slot_count)
    arrived = lax.all_to_all(packed, both, 0, 0, tiled=True)
    phase_in = arrived[:, 0:4, :]
    mass_in = arrived[:, 4, :]
    column_in = arrived[:, 5, :].astype(jnp.int32)
    depth_in = arrived[:, 6, :].astype(jnp.int32)
    sources = devices
    group_size = math.gcd(sources, max(1, 2048 // slot_count))
    step_count = sources // group_size
    block_rows = group_size * slot_count
    column_blocks = column_in.reshape(step_count, block_rows)
    depth_blocks = depth_in.reshape(step_count, block_rows)
    mass_blocks = mass_in.reshape(step_count, block_rows)
    column_ids = lax.broadcasted_iota(jnp.int32, (1, columns), 1)
    depth_ids = lax.broadcasted_iota(jnp.int32, (1, NZ), 1)

    def deposit(running, element):
        block_column, block_depth, block_mass = element
        picked = (block_column[:, None] == column_ids).astype(jnp.bfloat16)
        spread = jnp.where(
            block_depth[:, None] == depth_ids,
            block_mass.astype(jnp.bfloat16)[:, None],
            jnp.zeros((), jnp.bfloat16),
        )
        added = lax.dot_general(
            picked, spread, (((0,), (0,)), ((), ())), preferred_element_type=jnp.float32
        )
        return (running + added, None)

    density, unused = lax.scan(
        deposit, jnp.zeros((columns, NZ), jnp.float32), (column_blocks, depth_blocks, mass_blocks)
    )
    sine_x = sine_table(NX)
    sine_y = sine_table(NY)
    sine_z = sine_table(NZ)
    chunk_count = 2 if layers % 2 == 0 else 1
    chunk_layers = layers // chunk_count
    slab_index = lax.axis_index("row") * col_count + lax.axis_index("col")
    sine_z_slabs = sine_z.reshape(NZ, devices, layers)
    line_parts = []
    wave_parts = []
    sine_z_parts = []
    sends = []
    for chunk in range(chunk_count):
        lower_layer = chunk * chunk_layers
        sine_z_part = sine_z_slabs[:, :, lower_layer : lower_layer + chunk_layers]
        sine_z_parts.append(sine_z_part)
        sends.append(
            lax.dot_general(sine_z_part, density, (((0,), (1,)), ((), ())), precision=high)
        )
    arrivals = [lax.all_to_all(sends[0], both, 0, 0, tiled=True)]
    if chunk_count > 1:
        arrivals.append(lax.all_to_all(sends[1], both, 0, 0, tiled=True))
    for chunk in range(chunk_count):
        lower_layer = chunk * chunk_layers
        slab_field = arrivals[chunk].reshape(row_count, col_count, chunk_layers, cells_x, cells_y)
        sine_y_blocks = sine_y.reshape(col_count, cells_y, NY)
        sine_x_blocks = sine_x.reshape(row_count, cells_x, NX)
        mixed = jnp.einsum("rczxy,cyl->zrxl", slab_field, sine_y_blocks, precision=high)
        mixed = jnp.einsum("zrxl,rxk->zkl", mixed, sine_x_blocks, precision=high)
        depth_wave = (
            slab_index * layers
            + lower_layer
            + lax.broadcasted_iota(jnp.int32, (chunk_layers,), 0)
        )
        depth_eigen = 2.0 - 2.0 * jnp.cos(
            (depth_wave.astype(jnp.float32) + 1.0) * (math.pi / (NZ + 1))
        )
        eigen_sum = (
            eigen_line(NX)[None, :, None]
            + eigen_line(NY)[None, None, :]
            + depth_eigen[:, None, None]
        )
        scaled = mixed / eigen_sum
        potential = jnp.einsum("zkl,rxk->zrxl", scaled, sine_x_blocks, precision=high)
        potential = jnp.einsum("zrxl,cyl->rczxy", potential, sine_y_blocks, precision=high)
        outgoing = potential.reshape(devices, chunk_layers, columns)
        returned = lax.all_to_all(outgoing, both, 0, 0, tiled=True)
        if chunk + 2 < chunk_count:
            upcoming, returned = lax.optimization_barrier((sends[chunk + 2], returned))
            arrivals.append(lax.all_to_all(upcoming, both, 0, 0, tiled=True))
        wave_parts.append(returned.reshape(devices, chunk_layers, cells_x, cells_y))
        line_parts.append(
            lax.dot_general(
                returned, sine_z_parts[chunk], (((0, 1), (1, 2)), ((), ())), precision=high
            ).reshape(cells_x, cells_y, NZ)
        )
    def face(pick):
        dims = (((0, 1), (1, 2)), ((), ()))
        pieces = [
            lax.dot_general(pick(wave), sine, dims, precision=high)
            for wave, sine in zip(wave_parts, sine_z_parts)
        ]
        return sum(pieces[1:], pieces[0])

    line_grid = sum(line_parts[1:], line_parts[0])
    padded_x = jnp.concatenate(
        [
            shift_along(face(lambda wave: wave[:, :, cells_x - 1])[None], "row", True),
            line_grid,
            shift_along(face(lambda wave: wave[:, :, 0])[None], "row", False),
        ],
        axis=0,
    )
    padded_y = jnp.concatenate(
        [
            shift_along(face(lambda wave: wave[:, :, :, cells_y - 1])[:, None], "col", True),
            line_grid,
            shift_along(face(lambda wave: wave[:, :, :, 0])[:, None], "col", False),
        ],
        axis=1,
    )
    field_x = (-0.5 * (padded_x[2:] - padded_x[:-2])).reshape(columns, NZ)
    field_y = (-0.5 * (padded_y[:, 2:] - padded_y[:, :-2])).reshape(columns, NZ)
    found_x, found_y = lookup_fields(field_x, field_y, column_blocks, depth_blocks)
    momentum_x = phase_in[:, 1, :] + kick_strength * found_x.reshape(sources, slot_count)
    momentum_y = phase_in[:, 3, :] + kick_strength * found_y.reshape(sources, slot_count)
    kicked = jnp.stack([momentum_x, momentum_y], axis=1).reshape(
        row_count, col_count, 2, slot_count
    )
    coord_blocks = (
        phase_in[:, 0, :].reshape(step_count, block_rows),
        momentum_x.reshape(step_count, block_rows),
        phase_in[:, 2, :].reshape(step_count, block_rows),
        momentum_y.reshape(step_count, block_rows),
    )
    slice_blocks = (depth_in // (NZ // SLICES)).reshape(step_count, block_rows)
    slice_ids = lax.broadcasted_iota(jnp.int32, (1, SLICES), 1)

    def gather_moments(running, element):
        coord_one, coord_two, coord_three, coord_four, block_slice, block_mass = element
        weighted_slices = jnp.where(block_slice[:, None] == slice_ids, block_mass[:, None], 0.0)
        basis = monomials([coord_one, coord_two, coord_three, coord_four], ORDER)
        moment_part = jnp.dot(
            basis, weighted_slices, precision=highest, preferred_element_type=jnp.float32
        )
        square_part = jnp.sum(weighted_slices * block_mass[:, None], axis=0)
        return ((running[0] + moment_part, running[1] + square_part), None)

    start_state = (
        jnp.zeros((basis_count(ORDER), SLICES), jnp.float32),
        jnp.zeros((SLICES,), jnp.float32),
    )
    (moment_sum, square_sum), unused_too = lax.scan(
        gather_moments, start_state, coord_blocks + (slice_blocks, mass_blocks)
    )
    flat_totals = jnp.concatenate([moment_sum.reshape(-1), square_sum])
    piece = -(-flat_totals.shape[0] // devices)
    flat_totals = jnp.pad(flat_totals, (0, piece * devices - flat_totals.shape[0]))
    own_piece = jnp.sum(
        lax.all_to_all(flat_totals.reshape(devices, piece), both, 0, 0, tiled=True), axis=0
    )
    totals = lax.all_to_all(
        jnp.broadcast_to(own_piece[None, :], (devices, piece)), both, 0, 0, tiled=True
    ).reshape(-1)
    moment_count = moment_sum.shape[0] * SLICES
    moment_total = totals[:moment_count].reshape(moment_sum.shape)
    square_total = totals[moment_count : moment_count + SLICES]
    slice_moments = moment_total / jnp.sqrt(square_total + epsilon)[None, :]
    return (kicked, slice_moments)


def momentum_shape(phase_in):
    return (phase_in.shape[0], phase_in.shape[1], phase_in.shape[3])


def solution(mesh):
    placed = (
        P(("row", "col"), None, None, None),
        P(("row", "col"), None, None),
        P(("row", "col"), None, None),
        P(("row", "col"), None, None),
        P(("row", "col"), None),
    )
    return jax.shard_map(
        body,
        mesh=mesh,
        in_specs=placed,
        out_specs=(P(("row", "col"), None, None, None), P()),
        check_vma=False,
    )
```

```python
import math

import jax
import jax.numpy as jnp
from jax import lax
from jax.sharding import PartitionSpec as P

NX = 256
NY = 256
NZ = 512
SLICES = 64
ORDER = 6


kick_strength = 8.0
epsilon = 1e-06
highest = lax.Precision.HIGHEST
high = lax.Precision.HIGH


def with_halo(block, sides, width):
    for axis, dim in sides:
        count = lax.axis_size(axis)
        forward = [(i, i + 1) for i in range(count - 1)]
        backward = [(target, source) for source, target in forward]
        low = lax.ppermute(
            lax.slice_in_dim(block, block.shape[dim] - width, None, axis=dim), axis, forward
        )
        high = lax.ppermute(lax.slice_in_dim(block, 0, width, axis=dim), axis, backward)
        block = jnp.concatenate([low, block, high], axis=dim)
    return block


def exponent_table(max_order):
    listing = []
    for power_one in range(max_order + 1):
        for power_two in range(max_order + 1):
            for power_three in range(max_order + 1):
                for power_four in range(max_order + 1):
                    if power_one + power_two + power_three + power_four <= max_order:
                        listing.append([power_one, power_two, power_three, power_four])
    return listing


def monomials(coords, max_order):
    power_lists = []
    for position in range(4):
        variable = coords[position]
        powers = [jnp.ones_like(variable)]
        for degree in range(max_order):
            powers.append(powers[-1] * variable)
        power_lists.append(powers)
    terms = []
    for entry in exponent_table(max_order):
        product = power_lists[0][entry[0]]
        for position in range(1, 4):
            product = product * power_lists[position][entry[position]]
        terms.append(product)
    return jnp.stack(terms)


def wave_grid(length):
    row_wave = lax.broadcasted_iota(jnp.int32, (length, length), 0) + 1
    col_wave = lax.broadcasted_iota(jnp.int32, (length, length), 1) + 1
    reduced = row_wave * col_wave % (2 * (length + 1))
    return (reduced.astype(jnp.float32) * (math.pi / (length + 1)), col_wave)


def sine_table(length):
    angles, col_wave = wave_grid(length)
    return math.sqrt(2.0 / (length + 1)) * jnp.sin(angles)


def eigen_line(length):
    wave_index = lax.broadcasted_iota(jnp.int32, (length,), 0).astype(jnp.float32) + 1.0
    return 2.0 - 2.0 * jnp.cos(wave_index * (math.pi / (length + 1)))


def basis_count(max_order):
    return (max_order + 1) * (max_order + 2) * (max_order + 3) * (max_order + 4) // 24


def lookup_fields(field_x, field_y, column_blocks, depth_blocks):
    columns = field_x.shape[0]
    depth_total = field_x.shape[1]
    table = jnp.concatenate([field_x, field_y], axis=1)
    upper = table.astype(jnp.bfloat16)
    upper_wide = lax.optimization_barrier(upper).astype(jnp.float32)
    lower = (table - upper_wide).astype(jnp.bfloat16)
    column_ids = lax.broadcasted_iota(jnp.int32, (1, columns), 1)
    depth_ids = lax.broadcasted_iota(jnp.int32, (1, depth_total), 1)

    def pick(carry, element):
        block_column, block_depth = element
        picked = (block_column[:, None] == column_ids).astype(jnp.bfloat16)
        rows_found = jnp.dot(picked, upper, preferred_element_type=jnp.float32)
        rows_found = rows_found + jnp.dot(picked, lower, preferred_element_type=jnp.float32)
        chosen = block_depth[:, None] == depth_ids
        value_x = jnp.sum(jnp.where(chosen, rows_found[:, :depth_total], 0.0), axis=1)
        value_y = jnp.sum(jnp.where(chosen, rows_found[:, depth_total:], 0.0), axis=1)
        return (carry, (value_x, value_y))

    unused, (found_x, found_y) = lax.scan(
        pick, jnp.zeros((), jnp.float32), (column_blocks, depth_blocks)
    )
    return (found_x, found_y)


def shift_along(block, axis, forward):
    count = lax.axis_size(axis)
    pairs = [(i, i + 1) for i in range(count - 1)]
    if not forward:
        pairs = [(target, source) for source, target in pairs]
    return lax.ppermute(block, axis, pairs)


def body(particle_phase, particle_weight, cell_column, cell_depth, slot_counts):
    row_count = lax.axis_size("row")
    col_count = lax.axis_size("col")
    devices = row_count * col_count
    slot_count = particle_weight.shape[-1]
    cells_x = NX // row_count
    cells_y = NY // col_count
    columns = cells_x * cells_y
    layers = NZ // devices
    both = ("row", "col")
    live_slot = lax.broadcasted_iota(jnp.int32, particle_weight.shape, 2) < slot_counts[:, :, None]
    live_mass = jnp.where(live_slot, particle_weight.astype(jnp.float32), 0.0)
    packed = jnp.concatenate(
        [
            particle_phase,
            live_mass[:, :, None, :],
            cell_column.astype(jnp.float32)[:, :, None, :],
            cell_depth.astype(jnp.float32)[:, :, None, :],
        ],
        axis=2,
    ).reshape(devices, 7, slot_count)
    arrived = lax.all_to_all(packed, both, 0, 0, tiled=True)
    phase_in = arrived[:, 0:4, :]
    mass_in = arrived[:, 4, :]
    column_in = arrived[:, 5, :].astype(jnp.int32)
    depth_in = arrived[:, 6, :].astype(jnp.int32)
    sources = devices
    group_size = math.gcd(sources, max(1, 2048 // slot_count))
    step_count = sources // group_size
    block_rows = group_size * slot_count
    column_blocks = column_in.reshape(step_count, block_rows)
    depth_blocks = depth_in.reshape(step_count, block_rows)
    mass_blocks = mass_in.reshape(step_count, block_rows)
    column_ids = lax.broadcasted_iota(jnp.int32, (1, columns), 1)
    depth_ids = lax.broadcasted_iota(jnp.int32, (1, NZ), 1)

    def deposit(running, element):
        block_column, block_depth, block_mass = element
        picked = (block_column[:, None] == column_ids).astype(jnp.bfloat16)
        spread = jnp.where(
            block_depth[:, None] == depth_ids,
            block_mass.astype(jnp.bfloat16)[:, None],
            jnp.zeros((), jnp.bfloat16),
        )
        added = lax.dot_general(
            picked, spread, (((0,), (0,)), ((), ())), preferred_element_type=jnp.float32
        )
        return (running + added, None)

    density, unused = lax.scan(
        deposit, jnp.zeros((columns, NZ), jnp.float32), (column_blocks, depth_blocks, mass_blocks)
    )
    sine_x = sine_table(NX)
    sine_y = sine_table(NY)
    sine_z = sine_table(NZ)
    chunk_count = 2 if layers % 2 == 0 else 1
    chunk_layers = layers // chunk_count
    slab_index = lax.axis_index("row") * col_count + lax.axis_index("col")
    sine_z_slabs = sine_z.reshape(NZ, devices, layers)
    line_parts = []
    sine_z_parts = []
    sends = []
    for chunk in range(chunk_count):
        lower_layer = chunk * chunk_layers
        sine_z_part = sine_z_slabs[:, :, lower_layer : lower_layer + chunk_layers]
        sine_z_parts.append(sine_z_part)
        sends.append(
            lax.dot_general(sine_z_part, density, (((0,), (1,)), ((), ())), precision=high)
        )
    arrivals = [lax.all_to_all(sends[0], both, 0, 0, tiled=True)]
    if chunk_count > 1:
        arrivals.append(lax.all_to_all(sends[1], both, 0, 0, tiled=True))
    for chunk in range(chunk_count):
        lower_layer = chunk * chunk_layers
        slab_field = arrivals[chunk].reshape(row_count, col_count, chunk_layers, cells_x, cells_y)
        sine_y_blocks = sine_y.reshape(col_count, cells_y, NY)
        sine_x_blocks = sine_x.reshape(row_count, cells_x, NX)
        mixed = jnp.einsum("rczxy,cyl->zrxl", slab_field, sine_y_blocks, precision=high)
        mixed = jnp.einsum("zrxl,rxk->zkl", mixed, sine_x_blocks, precision=high)
        depth_wave = (
            slab_index * layers
            + lower_layer
            + lax.broadcasted_iota(jnp.int32, (chunk_layers,), 0)
        )
        depth_eigen = 2.0 - 2.0 * jnp.cos(
            (depth_wave.astype(jnp.float32) + 1.0) * (math.pi / (NZ + 1))
        )
        eigen_sum = (
            eigen_line(NX)[None, :, None]
            + eigen_line(NY)[None, None, :]
            + depth_eigen[:, None, None]
        )
        scaled = mixed / eigen_sum
        potential = jnp.einsum("zkl,rxk->zrxl", scaled, sine_x_blocks, precision=high)
        potential = jnp.einsum("zrxl,cyl->rczxy", potential, sine_y_blocks, precision=high)
        outgoing = potential.reshape(devices, chunk_layers, columns)
        returned = lax.all_to_all(outgoing, both, 0, 0, tiled=True)
        if chunk + 2 < chunk_count:
            upcoming, returned = lax.optimization_barrier((sends[chunk + 2], returned))
            arrivals.append(lax.all_to_all(upcoming, both, 0, 0, tiled=True))
        line_parts.append(
            lax.dot_general(
                returned, sine_z_parts[chunk], (((0, 1), (1, 2)), ((), ())), precision=high
            ).reshape(cells_x, cells_y, NZ)
        )
    def face(pick):
        return sum([pick(part) for part in line_parts[1:]], pick(line_parts[0]))

    line_grid = sum(line_parts[1:], line_parts[0])
    padded_x = jnp.concatenate(
        [
            shift_along(face(lambda part: part[cells_x - 1 :]), "row", True),
            line_grid,
            shift_along(face(lambda part: part[:1]), "row", False),
        ],
        axis=0,
    )
    padded_y = jnp.concatenate(
        [
            shift_along(face(lambda part: part[:, cells_y - 1 :]), "col", True),
            line_grid,
            shift_along(face(lambda part: part[:, :1]), "col", False),
        ],
        axis=1,
    )
    field_x = (-0.5 * (padded_x[2:] - padded_x[:-2])).reshape(columns, NZ)
    field_y = (-0.5 * (padded_y[:, 2:] - padded_y[:, :-2])).reshape(columns, NZ)
    found_x, found_y = lookup_fields(field_x, field_y, column_blocks, depth_blocks)
    momentum_x = phase_in[:, 1, :] + kick_strength * found_x.reshape(sources, slot_count)
    momentum_y = phase_in[:, 3, :] + kick_strength * found_y.reshape(sources, slot_count)
    kicked = jnp.stack([momentum_x, momentum_y], axis=1).reshape(
        row_count, col_count, 2, slot_count
    )
    coord_blocks = (
        phase_in[:, 0, :].reshape(step_count, block_rows),
        momentum_x.reshape(step_count, block_rows),
        phase_in[:, 2, :].reshape(step_count, block_rows),
        momentum_y.reshape(step_count, block_rows),
    )
    slice_blocks = (depth_in // (NZ // SLICES)).reshape(step_count, block_rows)
    slice_ids = lax.broadcasted_iota(jnp.int32, (1, SLICES), 1)

    def gather_moments(running, element):
        coord_one, coord_two, coord_three, coord_four, block_slice, block_mass = element
        weighted_slices = jnp.where(block_slice[:, None] == slice_ids, block_mass[:, None], 0.0)
        basis = monomials([coord_one, coord_two, coord_three, coord_four], ORDER)
        moment_part = jnp.dot(
            basis, weighted_slices, precision=highest, preferred_element_type=jnp.float32
        )
        square_part = jnp.sum(weighted_slices * block_mass[:, None], axis=0)
        return ((running[0] + moment_part, running[1] + square_part), None)

    start_state = (
        jnp.zeros((basis_count(ORDER), SLICES), jnp.float32),
        jnp.zeros((SLICES,), jnp.float32),
    )
    (moment_sum, square_sum), unused_too = lax.scan(
        gather_moments, start_state, coord_blocks + (slice_blocks, mass_blocks)
    )
    flat_totals = jnp.concatenate([moment_sum.reshape(-1), square_sum])
    piece = -(-flat_totals.shape[0] // (devices * 128)) * 128
    flat_totals = jnp.pad(flat_totals, (0, piece * devices - flat_totals.shape[0]))
    own_piece = jnp.sum(
        lax.all_to_all(flat_totals.reshape(devices, piece), both, 0, 0, tiled=True), axis=0
    )
    totals = lax.all_to_all(
        jnp.broadcast_to(own_piece[None, :], (devices, piece)), both, 0, 0, tiled=True
    ).reshape(-1)
    moment_count = moment_sum.shape[0] * SLICES
    moment_total = totals[:moment_count].reshape(moment_sum.shape)
    square_total = totals[moment_count : moment_count + SLICES]
    slice_moments = moment_total / jnp.sqrt(square_total + epsilon)[None, :]
    return (kicked, slice_moments)


def momentum_shape(phase_in):
    return (phase_in.shape[0], phase_in.shape[1], phase_in.shape[3])


def solution(mesh):
    placed = (
        P(("row", "col"), None, None, None),
        P(("row", "col"), None, None),
        P(("row", "col"), None, None),
        P(("row", "col"), None, None),
        P(("row", "col"), None),
    )
    return jax.shard_map(
        body,
        mesh=mesh,
        in_specs=placed,
        out_specs=(P(("row", "col"), None, None, None), P()),
        check_vma=False,
    )
```

```python
import math

import jax
import jax.numpy as jnp
from jax import lax
from jax.sharding import PartitionSpec as P

NX = 256
NY = 256
NZ = 512
SLICES = 64
ORDER = 6


kick_strength = 8.0
epsilon = 1e-06
highest = lax.Precision.HIGHEST
high = lax.Precision.HIGH


def with_halo(block, sides, width):
    for axis, dim in sides:
        count = lax.axis_size(axis)
        forward = [(i, i + 1) for i in range(count - 1)]
        backward = [(target, source) for source, target in forward]
        low = lax.ppermute(
            lax.slice_in_dim(block, block.shape[dim] - width, None, axis=dim), axis, forward
        )
        high = lax.ppermute(lax.slice_in_dim(block, 0, width, axis=dim), axis, backward)
        block = jnp.concatenate([low, block, high], axis=dim)
    return block


def exponent_table(max_order):
    listing = []
    for power_one in range(max_order + 1):
        for power_two in range(max_order + 1):
            for power_three in range(max_order + 1):
                for power_four in range(max_order + 1):
                    if power_one + power_two + power_three + power_four <= max_order:
                        listing.append([power_one, power_two, power_three, power_four])
    return listing


def monomials(coords, max_order):
    power_lists = []
    for position in range(4):
        variable = coords[position]
        powers = [jnp.ones_like(variable)]
        for degree in range(max_order):
            powers.append(powers[-1] * variable)
        power_lists.append(powers)
    terms = []
    for entry in exponent_table(max_order):
        product = power_lists[0][entry[0]]
        for position in range(1, 4):
            product = product * power_lists[position][entry[position]]
        terms.append(product)
    return jnp.stack(terms)


def wave_grid(length):
    row_wave = lax.broadcasted_iota(jnp.int32, (length, length), 0) + 1
    col_wave = lax.broadcasted_iota(jnp.int32, (length, length), 1) + 1
    reduced = row_wave * col_wave % (2 * (length + 1))
    return (reduced.astype(jnp.float32) * (math.pi / (length + 1)), col_wave)


def sine_table(length):
    angles, col_wave = wave_grid(length)
    return math.sqrt(2.0 / (length + 1)) * jnp.sin(angles)


def eigen_line(length):
    wave_index = lax.broadcasted_iota(jnp.int32, (length,), 0).astype(jnp.float32) + 1.0
    return 2.0 - 2.0 * jnp.cos(wave_index * (math.pi / (length + 1)))


def basis_count(max_order):
    return (max_order + 1) * (max_order + 2) * (max_order + 3) * (max_order + 4) // 24


def lookup_fields(field_x, field_y, column_blocks, depth_blocks):
    columns = field_x.shape[0]
    depth_total = field_x.shape[1]
    table = jnp.concatenate([field_x, field_y], axis=1)
    upper = table.astype(jnp.bfloat16)
    upper_wide = lax.optimization_barrier(upper).astype(jnp.float32)
    lower = (table - upper_wide).astype(jnp.bfloat16)
    column_ids = lax.broadcasted_iota(jnp.int32, (1, columns), 1)
    depth_ids = lax.broadcasted_iota(jnp.int32, (1, depth_total), 1)

    def pick(carry, element):
        block_column, block_depth = element
        picked = (block_column[:, None] == column_ids).astype(jnp.bfloat16)
        rows_found = jnp.dot(picked, upper, preferred_element_type=jnp.float32)
        rows_found = rows_found + jnp.dot(picked, lower, preferred_element_type=jnp.float32)
        chosen = block_depth[:, None] == depth_ids
        value_x = jnp.sum(jnp.where(chosen, rows_found[:, :depth_total], 0.0), axis=1)
        value_y = jnp.sum(jnp.where(chosen, rows_found[:, depth_total:], 0.0), axis=1)
        return (carry, (value_x, value_y))

    unused, (found_x, found_y) = lax.scan(
        pick, jnp.zeros((), jnp.float32), (column_blocks, depth_blocks)
    )
    return (found_x, found_y)


def shift_along(block, axis, forward):
    count = lax.axis_size(axis)
    pairs = [(i, i + 1) for i in range(count - 1)]
    if not forward:
        pairs = [(target, source) for source, target in pairs]
    return lax.ppermute(block, axis, pairs)


def column_face(grid, offset):
    rows, width, depth = grid.shape
    wanted = lax.broadcasted_iota(jnp.int32, (rows, rows * width), 0) * width + offset
    chosen = (lax.broadcasted_iota(jnp.int32, (rows, rows * width), 1) == wanted).astype(
        jnp.float32
    )
    return jnp.dot(
        chosen,
        grid.reshape(rows * width, depth),
        precision=lax.Precision.HIGHEST,
        preferred_element_type=jnp.float32,
    )


def body(particle_phase, particle_weight, cell_column, cell_depth, slot_counts):
    row_count = lax.axis_size("row")
    col_count = lax.axis_size("col")
    devices = row_count * col_count
    slot_count = particle_weight.shape[-1]
    cells_x = NX // row_count
    cells_y = NY // col_count
    columns = cells_x * cells_y
    layers = NZ // devices
    both = ("row", "col")
    live_slot = lax.broadcasted_iota(jnp.int32, particle_weight.shape, 2) < slot_counts[:, :, None]
    live_mass = jnp.where(live_slot, particle_weight.astype(jnp.float32), 0.0)
    packed = jnp.concatenate(
        [
            particle_phase,
            live_mass[:, :, None, :],
            cell_column.astype(jnp.float32)[:, :, None, :],
            cell_depth.astype(jnp.float32)[:, :, None, :],
        ],
        axis=2,
    ).reshape(devices, 7, slot_count)
    arrived = lax.all_to_all(packed, both, 0, 0, tiled=True)
    phase_in = arrived[:, 0:4, :]
    mass_in = arrived[:, 4, :]
    column_in = arrived[:, 5, :].astype(jnp.int32)
    depth_in = arrived[:, 6, :].astype(jnp.int32)
    sources = devices
    group_size = math.gcd(sources, max(1, 2048 // slot_count))
    step_count = sources // group_size
    block_rows = group_size * slot_count
    column_blocks = column_in.reshape(step_count, block_rows)
    depth_blocks = depth_in.reshape(step_count, block_rows)
    mass_blocks = mass_in.reshape(step_count, block_rows)
    column_ids = lax.broadcasted_iota(jnp.int32, (1, columns), 1)
    depth_ids = lax.broadcasted_iota(jnp.int32, (1, NZ), 1)

    def deposit(running, element):
        block_column, block_depth, block_mass = element
        picked = (block_column[:, None] == column_ids).astype(jnp.bfloat16)
        spread = jnp.where(
            block_depth[:, None] == depth_ids,
            block_mass.astype(jnp.bfloat16)[:, None],
            jnp.zeros((), jnp.bfloat16),
        )
        added = lax.dot_general(
            picked, spread, (((0,), (0,)), ((), ())), preferred_element_type=jnp.float32
        )
        return (running + added, None)

    density, unused = lax.scan(
        deposit, jnp.zeros((columns, NZ), jnp.float32), (column_blocks, depth_blocks, mass_blocks)
    )
    sine_x = sine_table(NX)
    sine_y = sine_table(NY)
    sine_z = sine_table(NZ)
    chunk_count = 2 if layers % 2 == 0 else 1
    chunk_layers = layers // chunk_count
    slab_index = lax.axis_index("row") * col_count + lax.axis_index("col")
    sine_z_slabs = sine_z.reshape(NZ, devices, layers)
    line_parts = []
    sine_z_parts = []
    sends = []
    for chunk in range(chunk_count):
        lower_layer = chunk * chunk_layers
        sine_z_part = sine_z_slabs[:, :, lower_layer : lower_layer + chunk_layers]
        sine_z_parts.append(sine_z_part)
        sends.append(
            lax.dot_general(sine_z_part, density, (((0,), (1,)), ((), ())), precision=high)
        )
    arrivals = [lax.all_to_all(sends[0], both, 0, 0, tiled=True)]
    if chunk_count > 1:
        arrivals.append(lax.all_to_all(sends[1], both, 0, 0, tiled=True))
    for chunk in range(chunk_count):
        lower_layer = chunk * chunk_layers
        slab_field = arrivals[chunk].reshape(row_count, col_count, chunk_layers, cells_x, cells_y)
        sine_y_blocks = sine_y.reshape(col_count, cells_y, NY)
        sine_x_blocks = sine_x.reshape(row_count, cells_x, NX)
        mixed = jnp.einsum("rczxy,cyl->zrxl", slab_field, sine_y_blocks, precision=high)
        mixed = jnp.einsum("zrxl,rxk->zkl", mixed, sine_x_blocks, precision=high)
        depth_wave = (
            slab_index * layers
            + lower_layer
            + lax.broadcasted_iota(jnp.int32, (chunk_layers,), 0)
        )
        depth_eigen = 2.0 - 2.0 * jnp.cos(
            (depth_wave.astype(jnp.float32) + 1.0) * (math.pi / (NZ + 1))
        )
        eigen_sum = (
            eigen_line(NX)[None, :, None]
            + eigen_line(NY)[None, None, :]
            + depth_eigen[:, None, None]
        )
        scaled = mixed / eigen_sum
        potential = jnp.einsum("zkl,rxk->zrxl", scaled, sine_x_blocks, precision=high)
        potential = jnp.einsum("zrxl,cyl->rczxy", potential, sine_y_blocks, precision=high)
        outgoing = potential.reshape(devices, chunk_layers, columns)
        returned = lax.all_to_all(outgoing, both, 0, 0, tiled=True)
        if chunk + 2 < chunk_count:
            upcoming, returned = lax.optimization_barrier((sends[chunk + 2], returned))
            arrivals.append(lax.all_to_all(upcoming, both, 0, 0, tiled=True))
        line_parts.append(
            lax.dot_general(
                returned, sine_z_parts[chunk], (((0, 1), (1, 2)), ((), ())), precision=high
            ).reshape(cells_x, cells_y, NZ)
        )
    def face(pick):
        return sum([pick(part) for part in line_parts[1:]], pick(line_parts[0]))

    line_grid = sum(line_parts[1:], line_parts[0])
    padded_x = jnp.concatenate(
        [
            shift_along(face(lambda part: part[cells_x - 1 :]), "row", True),
            line_grid,
            shift_along(face(lambda part: part[:1]), "row", False),
        ],
        axis=0,
    )
    padded_y = jnp.concatenate(
        [
            shift_along(column_face(line_grid, cells_y - 1)[:, None], "col", True),
            line_grid,
            shift_along(column_face(line_grid, 0)[:, None], "col", False),
        ],
        axis=1,
    )
    field_x = (-0.5 * (padded_x[2:] - padded_x[:-2])).reshape(columns, NZ)
    field_y = (-0.5 * (padded_y[:, 2:] - padded_y[:, :-2])).reshape(columns, NZ)
    found_x, found_y = lookup_fields(field_x, field_y, column_blocks, depth_blocks)
    momentum_x = phase_in[:, 1, :] + kick_strength * found_x.reshape(sources, slot_count)
    momentum_y = phase_in[:, 3, :] + kick_strength * found_y.reshape(sources, slot_count)
    kicked = jnp.stack([momentum_x, momentum_y], axis=1).reshape(
        row_count, col_count, 2, slot_count
    )
    coord_blocks = (
        phase_in[:, 0, :].reshape(step_count, block_rows),
        momentum_x.reshape(step_count, block_rows),
        phase_in[:, 2, :].reshape(step_count, block_rows),
        momentum_y.reshape(step_count, block_rows),
    )
    slice_blocks = (depth_in // (NZ // SLICES)).reshape(step_count, block_rows)
    slice_ids = lax.broadcasted_iota(jnp.int32, (1, SLICES), 1)

    def gather_moments(running, element):
        coord_one, coord_two, coord_three, coord_four, block_slice, block_mass = element
        weighted_slices = jnp.where(block_slice[:, None] == slice_ids, block_mass[:, None], 0.0)
        basis = monomials([coord_one, coord_two, coord_three, coord_four], ORDER)
        moment_part = jnp.dot(
            basis, weighted_slices, precision=highest, preferred_element_type=jnp.float32
        )
        square_part = jnp.sum(weighted_slices * block_mass[:, None], axis=0)
        return ((running[0] + moment_part, running[1] + square_part), None)

    start_state = (
        jnp.zeros((basis_count(ORDER), SLICES), jnp.float32),
        jnp.zeros((SLICES,), jnp.float32),
    )
    (moment_sum, square_sum), unused_too = lax.scan(
        gather_moments, start_state, coord_blocks + (slice_blocks, mass_blocks)
    )
    flat_totals = jnp.concatenate([moment_sum.reshape(-1), square_sum])
    piece = -(-flat_totals.shape[0] // (devices * 128)) * 128
    flat_totals = jnp.pad(flat_totals, (0, piece * devices - flat_totals.shape[0]))
    own_piece = jnp.sum(
        lax.all_to_all(flat_totals.reshape(devices, piece), both, 0, 0, tiled=True), axis=0
    )
    totals = lax.all_to_all(
        jnp.broadcast_to(own_piece[None, :], (devices, piece)), both, 0, 0, tiled=True
    ).reshape(-1)
    moment_count = moment_sum.shape[0] * SLICES
    moment_total = totals[:moment_count].reshape(moment_sum.shape)
    square_total = totals[moment_count : moment_count + SLICES]
    slice_moments = moment_total / jnp.sqrt(square_total + epsilon)[None, :]
    return (kicked, slice_moments)


def momentum_shape(phase_in):
    return (phase_in.shape[0], phase_in.shape[1], phase_in.shape[3])


def solution(mesh):
    placed = (
        P(("row", "col"), None, None, None),
        P(("row", "col"), None, None),
        P(("row", "col"), None, None),
        P(("row", "col"), None, None),
        P(("row", "col"), None),
    )
    return jax.shard_map(
        body,
        mesh=mesh,
        in_specs=placed,
        out_specs=(P(("row", "col"), None, None, None), P()),
        check_vma=False,
    )
```

```python
import math

import jax
import jax.numpy as jnp
from jax import lax
from jax.sharding import PartitionSpec as P

NX = 256
NY = 256
NZ = 512
SLICES = 64
ORDER = 6


kick_strength = 8.0
epsilon = 1e-06
highest = lax.Precision.HIGHEST
high = lax.Precision.HIGH


def with_halo(block, sides, width):
    for axis, dim in sides:
        count = lax.axis_size(axis)
        forward = [(i, i + 1) for i in range(count - 1)]
        backward = [(target, source) for source, target in forward]
        low = lax.ppermute(
            lax.slice_in_dim(block, block.shape[dim] - width, None, axis=dim), axis, forward
        )
        high = lax.ppermute(lax.slice_in_dim(block, 0, width, axis=dim), axis, backward)
        block = jnp.concatenate([low, block, high], axis=dim)
    return block


def exponent_table(max_order):
    listing = []
    for power_one in range(max_order + 1):
        for power_two in range(max_order + 1):
            for power_three in range(max_order + 1):
                for power_four in range(max_order + 1):
                    if power_one + power_two + power_three + power_four <= max_order:
                        listing.append([power_one, power_two, power_three, power_four])
    return listing


def monomials(coords, max_order):
    power_lists = []
    for position in range(4):
        variable = coords[position]
        powers = [jnp.ones_like(variable)]
        for degree in range(max_order):
            powers.append(powers[-1] * variable)
        power_lists.append(powers)
    terms = []
    for entry in exponent_table(max_order):
        product = power_lists[0][entry[0]]
        for position in range(1, 4):
            product = product * power_lists[position][entry[position]]
        terms.append(product)
    return jnp.stack(terms)


def wave_grid(length):
    row_wave = lax.broadcasted_iota(jnp.int32, (length, length), 0) + 1
    col_wave = lax.broadcasted_iota(jnp.int32, (length, length), 1) + 1
    reduced = row_wave * col_wave % (2 * (length + 1))
    return (reduced.astype(jnp.float32) * (math.pi / (length + 1)), col_wave)


def sine_table(length):
    angles, col_wave = wave_grid(length)
    return math.sqrt(2.0 / (length + 1)) * jnp.sin(angles)


def eigen_line(length):
    wave_index = lax.broadcasted_iota(jnp.int32, (length,), 0).astype(jnp.float32) + 1.0
    return 2.0 - 2.0 * jnp.cos(wave_index * (math.pi / (length + 1)))


def basis_count(max_order):
    return (max_order + 1) * (max_order + 2) * (max_order + 3) * (max_order + 4) // 24


def lookup_fields(field_x, field_y, column_blocks, depth_blocks):
    columns = field_x.shape[0]
    depth_total = field_x.shape[1]
    table = jnp.concatenate([field_x, field_y], axis=1)
    upper = table.astype(jnp.bfloat16)
    upper_wide = lax.optimization_barrier(upper).astype(jnp.float32)
    lower = (table - upper_wide).astype(jnp.bfloat16)
    stacked = jnp.concatenate([upper, lower], axis=1)
    column_ids = lax.broadcasted_iota(jnp.int32, (1, columns), 1)
    depth_ids = lax.broadcasted_iota(jnp.int32, (1, depth_total), 1)

    def pick(carry, element):
        block_column, block_depth = element
        picked = (block_column[:, None] == column_ids).astype(jnp.bfloat16)
        both_found = jnp.dot(picked, stacked, preferred_element_type=jnp.float32)
        rows_found = both_found[:, : 2 * depth_total] + both_found[:, 2 * depth_total :]
        chosen = block_depth[:, None] == depth_ids
        value_x = jnp.sum(jnp.where(chosen, rows_found[:, :depth_total], 0.0), axis=1)
        value_y = jnp.sum(jnp.where(chosen, rows_found[:, depth_total:], 0.0), axis=1)
        return (carry, (value_x, value_y))

    unused, (found_x, found_y) = lax.scan(
        pick, jnp.zeros((), jnp.float32), (column_blocks, depth_blocks)
    )
    return (found_x, found_y)


def shift_along(block, axis, forward):
    count = lax.axis_size(axis)
    pairs = [(i, i + 1) for i in range(count - 1)]
    if not forward:
        pairs = [(target, source) for source, target in pairs]
    return lax.ppermute(block, axis, pairs)


def body(particle_phase, particle_weight, cell_column, cell_depth, slot_counts):
    row_count = lax.axis_size("row")
    col_count = lax.axis_size("col")
    devices = row_count * col_count
    slot_count = particle_weight.shape[-1]
    cells_x = NX // row_count
    cells_y = NY // col_count
    columns = cells_x * cells_y
    layers = NZ // devices
    both = ("row", "col")
    live_slot = lax.broadcasted_iota(jnp.int32, particle_weight.shape, 2) < slot_counts[:, :, None]
    live_mass = jnp.where(live_slot, particle_weight.astype(jnp.float32), 0.0)
    packed = jnp.concatenate(
        [
            particle_phase,
            live_mass[:, :, None, :],
            cell_column.astype(jnp.float32)[:, :, None, :],
            cell_depth.astype(jnp.float32)[:, :, None, :],
        ],
        axis=2,
    ).reshape(devices, 7, slot_count)
    arrived = lax.all_to_all(packed, both, 0, 0, tiled=True)
    phase_in = arrived[:, 0:4, :]
    mass_in = arrived[:, 4, :]
    column_in = arrived[:, 5, :].astype(jnp.int32)
    depth_in = arrived[:, 6, :].astype(jnp.int32)
    sources = devices
    group_size = math.gcd(sources, max(1, 2048 // slot_count))
    step_count = sources // group_size
    block_rows = group_size * slot_count
    column_blocks = column_in.reshape(step_count, block_rows)
    depth_blocks = depth_in.reshape(step_count, block_rows)
    mass_blocks = mass_in.reshape(step_count, block_rows)
    column_ids = lax.broadcasted_iota(jnp.int32, (1, columns), 1)
    depth_ids = lax.broadcasted_iota(jnp.int32, (1, NZ), 1)

    def deposit(running, element):
        block_column, block_depth, block_mass = element
        picked = (block_column[:, None] == column_ids).astype(jnp.bfloat16)
        spread = jnp.where(
            block_depth[:, None] == depth_ids,
            block_mass.astype(jnp.bfloat16)[:, None],
            jnp.zeros((), jnp.bfloat16),
        )
        added = lax.dot_general(
            picked, spread, (((0,), (0,)), ((), ())), preferred_element_type=jnp.float32
        )
        return (running + added, None)

    density, unused = lax.scan(
        deposit, jnp.zeros((columns, NZ), jnp.float32), (column_blocks, depth_blocks, mass_blocks)
    )
    sine_x = sine_table(NX)
    sine_y = sine_table(NY)
    sine_z = sine_table(NZ)
    chunk_count = 2 if layers % 2 == 0 else 1
    chunk_layers = layers // chunk_count
    slab_index = lax.axis_index("row") * col_count + lax.axis_index("col")
    sine_z_slabs = sine_z.reshape(NZ, devices, layers)
    line_parts = []
    sine_z_parts = []
    sends = []
    for chunk in range(chunk_count):
        lower_layer = chunk * chunk_layers
        sine_z_part = sine_z_slabs[:, :, lower_layer : lower_layer + chunk_layers]
        sine_z_parts.append(sine_z_part)
        sends.append(
            lax.dot_general(sine_z_part, density, (((0,), (1,)), ((), ())), precision=high)
        )
    arrivals = [lax.all_to_all(sends[0], both, 0, 0, tiled=True)]
    if chunk_count > 1:
        arrivals.append(lax.all_to_all(sends[1], both, 0, 0, tiled=True))
    for chunk in range(chunk_count):
        lower_layer = chunk * chunk_layers
        slab_field = arrivals[chunk].reshape(row_count, col_count, chunk_layers, cells_x, cells_y)
        sine_y_blocks = sine_y.reshape(col_count, cells_y, NY)
        sine_x_blocks = sine_x.reshape(row_count, cells_x, NX)
        mixed = jnp.einsum("rczxy,cyl->zrxl", slab_field, sine_y_blocks, precision=high)
        mixed = jnp.einsum("zrxl,rxk->zkl", mixed, sine_x_blocks, precision=high)
        depth_wave = (
            slab_index * layers
            + lower_layer
            + lax.broadcasted_iota(jnp.int32, (chunk_layers,), 0)
        )
        depth_eigen = 2.0 - 2.0 * jnp.cos(
            (depth_wave.astype(jnp.float32) + 1.0) * (math.pi / (NZ + 1))
        )
        eigen_sum = (
            eigen_line(NX)[None, :, None]
            + eigen_line(NY)[None, None, :]
            + depth_eigen[:, None, None]
        )
        scaled = mixed / eigen_sum
        potential = jnp.einsum("zkl,rxk->zrxl", scaled, sine_x_blocks, precision=high)
        potential = jnp.einsum("zrxl,cyl->rczxy", potential, sine_y_blocks, precision=high)
        outgoing = potential.reshape(devices, chunk_layers, columns)
        returned = lax.all_to_all(outgoing, both, 0, 0, tiled=True)
        if chunk + 2 < chunk_count:
            upcoming, returned = lax.optimization_barrier((sends[chunk + 2], returned))
            arrivals.append(lax.all_to_all(upcoming, both, 0, 0, tiled=True))
        line_parts.append(
            lax.dot_general(
                returned, sine_z_parts[chunk], (((0, 1), (1, 2)), ((), ())), precision=high
            ).reshape(cells_x, cells_y, NZ)
        )
    def face(pick):
        return sum([pick(part) for part in line_parts[1:]], pick(line_parts[0]))

    line_grid = sum(line_parts[1:], line_parts[0])
    padded_x = jnp.concatenate(
        [
            shift_along(face(lambda part: part[cells_x - 1 :]), "row", True),
            line_grid,
            shift_along(face(lambda part: part[:1]), "row", False),
        ],
        axis=0,
    )
    padded_y = jnp.concatenate(
        [
            shift_along(face(lambda part: part[:, cells_y - 1 :]), "col", True),
            line_grid,
            shift_along(face(lambda part: part[:, :1]), "col", False),
        ],
        axis=1,
    )
    field_x = (-0.5 * (padded_x[2:] - padded_x[:-2])).reshape(columns, NZ)
    field_y = (-0.5 * (padded_y[:, 2:] - padded_y[:, :-2])).reshape(columns, NZ)
    found_x, found_y = lookup_fields(field_x, field_y, column_blocks, depth_blocks)
    momentum_x = phase_in[:, 1, :] + kick_strength * found_x.reshape(sources, slot_count)
    momentum_y = phase_in[:, 3, :] + kick_strength * found_y.reshape(sources, slot_count)
    kicked = jnp.stack([momentum_x, momentum_y], axis=1).reshape(
        row_count, col_count, 2, slot_count
    )
    coord_blocks = (
        phase_in[:, 0, :].reshape(step_count, block_rows),
        momentum_x.reshape(step_count, block_rows),
        phase_in[:, 2, :].reshape(step_count, block_rows),
        momentum_y.reshape(step_count, block_rows),
    )
    slice_blocks = (depth_in // (NZ // SLICES)).reshape(step_count, block_rows)
    slice_ids = lax.broadcasted_iota(jnp.int32, (1, SLICES), 1)

    def gather_moments(running, element):
        coord_one, coord_two, coord_three, coord_four, block_slice, block_mass = element
        weighted_slices = jnp.where(block_slice[:, None] == slice_ids, block_mass[:, None], 0.0)
        basis = monomials([coord_one, coord_two, coord_three, coord_four], ORDER)
        moment_part = jnp.dot(
            basis, weighted_slices, precision=highest, preferred_element_type=jnp.float32
        )
        square_part = jnp.sum(weighted_slices * block_mass[:, None], axis=0)
        return ((running[0] + moment_part, running[1] + square_part), None)

    start_state = (
        jnp.zeros((basis_count(ORDER), SLICES), jnp.float32),
        jnp.zeros((SLICES,), jnp.float32),
    )
    (moment_sum, square_sum), unused_too = lax.scan(
        gather_moments, start_state, coord_blocks + (slice_blocks, mass_blocks)
    )
    flat_totals = jnp.concatenate([moment_sum.reshape(-1), square_sum])
    piece = -(-flat_totals.shape[0] // (devices * 128)) * 128
    flat_totals = jnp.pad(flat_totals, (0, piece * devices - flat_totals.shape[0]))
    own_piece = jnp.sum(
        lax.all_to_all(flat_totals.reshape(devices, piece), both, 0, 0, tiled=True), axis=0
    )
    totals = lax.all_to_all(
        jnp.broadcast_to(own_piece[None, :], (devices, piece)), both, 0, 0, tiled=True
    ).reshape(-1)
    moment_count = moment_sum.shape[0] * SLICES
    moment_total = totals[:moment_count].reshape(moment_sum.shape)
    square_total = totals[moment_count : moment_count + SLICES]
    slice_moments = moment_total / jnp.sqrt(square_total + epsilon)[None, :]
    return (kicked, slice_moments)


def momentum_shape(phase_in):
    return (phase_in.shape[0], phase_in.shape[1], phase_in.shape[3])


def solution(mesh):
    placed = (
        P(("row", "col"), None, None, None),
        P(("row", "col"), None, None),
        P(("row", "col"), None, None),
        P(("row", "col"), None, None),
        P(("row", "col"), None),
    )
    return jax.shard_map(
        body,
        mesh=mesh,
        in_specs=placed,
        out_specs=(P(("row", "col"), None, None, None), P()),
        check_vma=False,
    )
```

```python
import math

import jax
import jax.numpy as jnp
from jax import lax
from jax.sharding import PartitionSpec as P

NX = 256
NY = 256
NZ = 512
SLICES = 64
ORDER = 6


kick_strength = 8.0
epsilon = 1e-06
highest = lax.Precision.HIGHEST
high = lax.Precision.HIGH


def with_halo(block, sides, width):
    for axis, dim in sides:
        count = lax.axis_size(axis)
        forward = [(i, i + 1) for i in range(count - 1)]
        backward = [(target, source) for source, target in forward]
        low = lax.ppermute(
            lax.slice_in_dim(block, block.shape[dim] - width, None, axis=dim), axis, forward
        )
        high = lax.ppermute(lax.slice_in_dim(block, 0, width, axis=dim), axis, backward)
        block = jnp.concatenate([low, block, high], axis=dim)
    return block


def exponent_table(max_order):
    listing = []
    for power_one in range(max_order + 1):
        for power_two in range(max_order + 1):
            for power_three in range(max_order + 1):
                for power_four in range(max_order + 1):
                    if power_one + power_two + power_three + power_four <= max_order:
                        listing.append([power_one, power_two, power_three, power_four])
    return listing


def monomials(coords, max_order):
    power_lists = []
    for position in range(4):
        variable = coords[position]
        powers = [jnp.ones_like(variable)]
        for degree in range(max_order):
            powers.append(powers[-1] * variable)
        power_lists.append(powers)
    terms = []
    for entry in exponent_table(max_order):
        product = power_lists[0][entry[0]]
        for position in range(1, 4):
            product = product * power_lists[position][entry[position]]
        terms.append(product)
    return jnp.stack(terms)


def wave_grid(length):
    row_wave = lax.broadcasted_iota(jnp.int32, (length, length), 0) + 1
    col_wave = lax.broadcasted_iota(jnp.int32, (length, length), 1) + 1
    reduced = row_wave * col_wave % (2 * (length + 1))
    return (reduced.astype(jnp.float32) * (math.pi / (length + 1)), col_wave)


def sine_table(length):
    angles, col_wave = wave_grid(length)
    return math.sqrt(2.0 / (length + 1)) * jnp.sin(angles)


def eigen_line(length):
    wave_index = lax.broadcasted_iota(jnp.int32, (length,), 0).astype(jnp.float32) + 1.0
    return 2.0 - 2.0 * jnp.cos(wave_index * (math.pi / (length + 1)))


def basis_count(max_order):
    return (max_order + 1) * (max_order + 2) * (max_order + 3) * (max_order + 4) // 24


def lookup_fields(field_x, field_y, column_blocks, depth_blocks):
    columns = field_x.shape[0]
    depth_total = field_x.shape[1]
    table = jnp.concatenate([field_x, field_y], axis=1)
    upper = table.astype(jnp.bfloat16)
    upper_wide = lax.optimization_barrier(upper).astype(jnp.float32)
    lower = (table - upper_wide).astype(jnp.bfloat16)
    column_ids = lax.broadcasted_iota(jnp.int32, (1, columns), 1)
    depth_ids = lax.broadcasted_iota(jnp.int32, (1, depth_total), 1)

    def pick(carry, element):
        block_column, block_depth = element
        picked = (block_column[:, None] == column_ids).astype(jnp.bfloat16)
        rows_found = jnp.dot(picked, upper, preferred_element_type=jnp.float32)
        rows_found = rows_found + jnp.dot(picked, lower, preferred_element_type=jnp.float32)
        chosen = block_depth[:, None] == depth_ids
        value_x = jnp.sum(jnp.where(chosen, rows_found[:, :depth_total], 0.0), axis=1)
        value_y = jnp.sum(jnp.where(chosen, rows_found[:, depth_total:], 0.0), axis=1)
        return (carry, (value_x, value_y))

    unused, (found_x, found_y) = lax.scan(
        pick, jnp.zeros((), jnp.float32), (column_blocks, depth_blocks)
    )
    return (found_x, found_y)


def shift_along(block, axis, forward):
    count = lax.axis_size(axis)
    pairs = [(i, i + 1) for i in range(count - 1)]
    if not forward:
        pairs = [(target, source) for source, target in pairs]
    return lax.ppermute(block, axis, pairs)


def body(particle_phase, particle_weight, cell_column, cell_depth, slot_counts):
    row_count = lax.axis_size("row")
    col_count = lax.axis_size("col")
    devices = row_count * col_count
    slot_count = particle_weight.shape[-1]
    cells_x = NX // row_count
    cells_y = NY // col_count
    columns = cells_x * cells_y
    layers = NZ // devices
    both = ("row", "col")
    live_slot = lax.broadcasted_iota(jnp.int32, particle_weight.shape, 2) < slot_counts[:, :, None]
    live_mass = jnp.where(live_slot, particle_weight.astype(jnp.float32), 0.0)
    packed = jnp.concatenate(
        [
            particle_phase,
            live_mass[:, :, None, :],
            cell_column.astype(jnp.float32)[:, :, None, :],
            cell_depth.astype(jnp.float32)[:, :, None, :],
            jnp.zeros_like(live_mass)[:, :, None, :],
        ],
        axis=2,
    ).reshape(devices, 8, slot_count)
    arrived = lax.all_to_all(packed, both, 0, 0, tiled=True)
    phase_in = arrived[:, 0:4, :]
    mass_in = arrived[:, 4, :]
    column_in = arrived[:, 5, :].astype(jnp.int32)
    depth_in = arrived[:, 6, :].astype(jnp.int32)
    sources = devices
    group_size = math.gcd(sources, max(1, 2048 // slot_count))
    step_count = sources // group_size
    block_rows = group_size * slot_count
    column_blocks = column_in.reshape(step_count, block_rows)
    depth_blocks = depth_in.reshape(step_count, block_rows)
    mass_blocks = mass_in.reshape(step_count, block_rows)
    column_ids = lax.broadcasted_iota(jnp.int32, (1, columns), 1)
    depth_ids = lax.broadcasted_iota(jnp.int32, (1, NZ), 1)

    def deposit(running, element):
        block_column, block_depth, block_mass = element
        picked = (block_column[:, None] == column_ids).astype(jnp.bfloat16)
        spread = jnp.where(
            block_depth[:, None] == depth_ids,
            block_mass.astype(jnp.bfloat16)[:, None],
            jnp.zeros((), jnp.bfloat16),
        )
        added = lax.dot_general(
            picked, spread, (((0,), (0,)), ((), ())), preferred_element_type=jnp.float32
        )
        return (running + added, None)

    density, unused = lax.scan(
        deposit, jnp.zeros((columns, NZ), jnp.float32), (column_blocks, depth_blocks, mass_blocks)
    )
    sine_x = sine_table(NX)
    sine_y = sine_table(NY)
    sine_z = sine_table(NZ)
    chunk_count = 2 if layers % 2 == 0 else 1
    chunk_layers = layers // chunk_count
    slab_index = lax.axis_index("row") * col_count + lax.axis_index("col")
    sine_z_slabs = sine_z.reshape(NZ, devices, layers)
    line_parts = []
    sine_z_parts = []
    sends = []
    for chunk in range(chunk_count):
        lower_layer = chunk * chunk_layers
        sine_z_part = sine_z_slabs[:, :, lower_layer : lower_layer + chunk_layers]
        sine_z_parts.append(sine_z_part)
        sends.append(
            lax.dot_general(sine_z_part, density, (((0,), (1,)), ((), ())), precision=high)
        )
    arrivals = [lax.all_to_all(sends[0], both, 0, 0, tiled=True)]
    if chunk_count > 1:
        arrivals.append(lax.all_to_all(sends[1], both, 0, 0, tiled=True))
    for chunk in range(chunk_count):
        lower_layer = chunk * chunk_layers
        slab_field = arrivals[chunk].reshape(row_count, col_count, chunk_layers, cells_x, cells_y)
        sine_y_blocks = sine_y.reshape(col_count, cells_y, NY)
        sine_x_blocks = sine_x.reshape(row_count, cells_x, NX)
        mixed = jnp.einsum("rczxy,cyl->zrxl", slab_field, sine_y_blocks, precision=high)
        mixed = jnp.einsum("zrxl,rxk->zkl", mixed, sine_x_blocks, precision=high)
        depth_wave = (
            slab_index * layers
            + lower_layer
            + lax.broadcasted_iota(jnp.int32, (chunk_layers,), 0)
        )
        depth_eigen = 2.0 - 2.0 * jnp.cos(
            (depth_wave.astype(jnp.float32) + 1.0) * (math.pi / (NZ + 1))
        )
        eigen_sum = (
            eigen_line(NX)[None, :, None]
            + eigen_line(NY)[None, None, :]
            + depth_eigen[:, None, None]
        )
        scaled = mixed / eigen_sum
        potential = jnp.einsum("zkl,rxk->zrxl", scaled, sine_x_blocks, precision=high)
        potential = jnp.einsum("zrxl,cyl->rczxy", potential, sine_y_blocks, precision=high)
        outgoing = potential.reshape(devices, chunk_layers, columns)
        returned = lax.all_to_all(outgoing, both, 0, 0, tiled=True)
        if chunk + 2 < chunk_count:
            upcoming, returned = lax.optimization_barrier((sends[chunk + 2], returned))
            arrivals.append(lax.all_to_all(upcoming, both, 0, 0, tiled=True))
        line_parts.append(
            lax.dot_general(
                returned, sine_z_parts[chunk], (((0, 1), (1, 2)), ((), ())), precision=high
            ).reshape(cells_x, cells_y, NZ)
        )
    def face(pick):
        return sum([pick(part) for part in line_parts[1:]], pick(line_parts[0]))

    line_grid = sum(line_parts[1:], line_parts[0])
    padded_x = jnp.concatenate(
        [
            shift_along(face(lambda part: part[cells_x - 1 :]), "row", True),
            line_grid,
            shift_along(face(lambda part: part[:1]), "row", False),
        ],
        axis=0,
    )
    padded_y = jnp.concatenate(
        [
            shift_along(face(lambda part: part[:, cells_y - 1 :]), "col", True),
            line_grid,
            shift_along(face(lambda part: part[:, :1]), "col", False),
        ],
        axis=1,
    )
    field_x = (-0.5 * (padded_x[2:] - padded_x[:-2])).reshape(columns, NZ)
    field_y = (-0.5 * (padded_y[:, 2:] - padded_y[:, :-2])).reshape(columns, NZ)
    found_x, found_y = lookup_fields(field_x, field_y, column_blocks, depth_blocks)
    momentum_x = phase_in[:, 1, :] + kick_strength * found_x.reshape(sources, slot_count)
    momentum_y = phase_in[:, 3, :] + kick_strength * found_y.reshape(sources, slot_count)
    kicked = jnp.stack([momentum_x, momentum_y], axis=1).reshape(
        row_count, col_count, 2, slot_count
    )
    coord_blocks = (
        phase_in[:, 0, :].reshape(step_count, block_rows),
        momentum_x.reshape(step_count, block_rows),
        phase_in[:, 2, :].reshape(step_count, block_rows),
        momentum_y.reshape(step_count, block_rows),
    )
    slice_blocks = (depth_in // (NZ // SLICES)).reshape(step_count, block_rows)
    slice_ids = lax.broadcasted_iota(jnp.int32, (1, SLICES), 1)

    def gather_moments(running, element):
        coord_one, coord_two, coord_three, coord_four, block_slice, block_mass = element
        weighted_slices = jnp.where(block_slice[:, None] == slice_ids, block_mass[:, None], 0.0)
        basis = monomials([coord_one, coord_two, coord_three, coord_four], ORDER)
        moment_part = jnp.dot(
            basis, weighted_slices, precision=highest, preferred_element_type=jnp.float32
        )
        square_part = jnp.sum(weighted_slices * block_mass[:, None], axis=0)
        return ((running[0] + moment_part, running[1] + square_part), None)

    start_state = (
        jnp.zeros((basis_count(ORDER), SLICES), jnp.float32),
        jnp.zeros((SLICES,), jnp.float32),
    )
    (moment_sum, square_sum), unused_too = lax.scan(
        gather_moments, start_state, coord_blocks + (slice_blocks, mass_blocks)
    )
    flat_totals = jnp.concatenate([moment_sum.reshape(-1), square_sum])
    piece = -(-flat_totals.shape[0] // (devices * 128)) * 128
    flat_totals = jnp.pad(flat_totals, (0, piece * devices - flat_totals.shape[0]))
    own_piece = jnp.sum(
        lax.all_to_all(flat_totals.reshape(devices, piece), both, 0, 0, tiled=True), axis=0
    )
    totals = lax.all_to_all(
        jnp.broadcast_to(own_piece[None, :], (devices, piece)), both, 0, 0, tiled=True
    ).reshape(-1)
    moment_count = moment_sum.shape[0] * SLICES
    moment_total = totals[:moment_count].reshape(moment_sum.shape)
    square_total = totals[moment_count : moment_count + SLICES]
    slice_moments = moment_total / jnp.sqrt(square_total + epsilon)[None, :]
    return (kicked, slice_moments)


def momentum_shape(phase_in):
    return (phase_in.shape[0], phase_in.shape[1], phase_in.shape[3])


def solution(mesh):
    placed = (
        P(("row", "col"), None, None, None),
        P(("row", "col"), None, None),
        P(("row", "col"), None, None),
        P(("row", "col"), None, None),
        P(("row", "col"), None),
    )
    return jax.shard_map(
        body,
        mesh=mesh,
        in_specs=placed,
        out_specs=(P(("row", "col"), None, None, None), P()),
        check_vma=False,
    )
```

```python
import math

import jax
import jax.numpy as jnp
from jax import lax
from jax.sharding import PartitionSpec as P

NX = 256
NY = 256
NZ = 512
SLICES = 64
ORDER = 6


kick_strength = 8.0
epsilon = 1e-06
highest = lax.Precision.HIGHEST
high = lax.Precision.HIGH


def with_halo(block, sides, width):
    for axis, dim in sides:
        count = lax.axis_size(axis)
        forward = [(i, i + 1) for i in range(count - 1)]
        backward = [(target, source) for source, target in forward]
        low = lax.ppermute(
            lax.slice_in_dim(block, block.shape[dim] - width, None, axis=dim), axis, forward
        )
        high = lax.ppermute(lax.slice_in_dim(block, 0, width, axis=dim), axis, backward)
        block = jnp.concatenate([low, block, high], axis=dim)
    return block


def exponent_table(max_order):
    listing = []
    for power_one in range(max_order + 1):
        for power_two in range(max_order + 1):
            for power_three in range(max_order + 1):
                for power_four in range(max_order + 1):
                    if power_one + power_two + power_three + power_four <= max_order:
                        listing.append([power_one, power_two, power_three, power_four])
    return listing


def monomials(coords, max_order):
    power_lists = []
    for position in range(4):
        variable = coords[position]
        powers = [jnp.ones_like(variable)]
        for degree in range(max_order):
            powers.append(powers[-1] * variable)
        power_lists.append(powers)
    terms = []
    for entry in exponent_table(max_order):
        product = power_lists[0][entry[0]]
        for position in range(1, 4):
            product = product * power_lists[position][entry[position]]
        terms.append(product)
    return jnp.stack(terms)


def wave_grid(length):
    row_wave = lax.broadcasted_iota(jnp.int32, (length, length), 0) + 1
    col_wave = lax.broadcasted_iota(jnp.int32, (length, length), 1) + 1
    reduced = row_wave * col_wave % (2 * (length + 1))
    return (reduced.astype(jnp.float32) * (math.pi / (length + 1)), col_wave)


def sine_table(length):
    angles, col_wave = wave_grid(length)
    return math.sqrt(2.0 / (length + 1)) * jnp.sin(angles)


def eigen_line(length):
    wave_index = lax.broadcasted_iota(jnp.int32, (length,), 0).astype(jnp.float32) + 1.0
    return 2.0 - 2.0 * jnp.cos(wave_index * (math.pi / (length + 1)))


def basis_count(max_order):
    return (max_order + 1) * (max_order + 2) * (max_order + 3) * (max_order + 4) // 24


def lookup_fields(field_x, field_y, column_blocks, depth_blocks):
    columns = field_x.shape[0]
    depth_total = field_x.shape[1]
    table = jnp.concatenate([field_x, field_y], axis=1)
    upper = table.astype(jnp.bfloat16)
    upper_wide = lax.optimization_barrier(upper).astype(jnp.float32)
    lower = (table - upper_wide).astype(jnp.bfloat16)
    stacked = jnp.concatenate([upper, lower], axis=1)
    column_ids = lax.broadcasted_iota(jnp.int32, (1, columns), 1)
    depth_ids = lax.broadcasted_iota(jnp.int32, (1, depth_total), 1)

    def pick(carry, element):
        block_column, block_depth = element
        picked = (block_column[:, None] == column_ids).astype(jnp.bfloat16)
        both_found = jnp.dot(picked, stacked, preferred_element_type=jnp.float32)
        rows_found = both_found[:, : 2 * depth_total] + both_found[:, 2 * depth_total :]
        chosen = block_depth[:, None] == depth_ids
        value_x = jnp.sum(jnp.where(chosen, rows_found[:, :depth_total], 0.0), axis=1)
        value_y = jnp.sum(jnp.where(chosen, rows_found[:, depth_total:], 0.0), axis=1)
        return (carry, (value_x, value_y))

    unused, (found_x, found_y) = lax.scan(
        pick, jnp.zeros((), jnp.float32), (column_blocks, depth_blocks)
    )
    return (found_x, found_y)


def shift_along(block, axis, forward):
    count = lax.axis_size(axis)
    pairs = [(i, i + 1) for i in range(count - 1)]
    if not forward:
        pairs = [(target, source) for source, target in pairs]
    return lax.ppermute(block, axis, pairs)


def body(particle_phase, particle_weight, cell_column, cell_depth, slot_counts):
    row_count = lax.axis_size("row")
    col_count = lax.axis_size("col")
    devices = row_count * col_count
    slot_count = particle_weight.shape[-1]
    cells_x = NX // row_count
    cells_y = NY // col_count
    columns = cells_x * cells_y
    layers = NZ // devices
    both = ("row", "col")
    live_slot = lax.broadcasted_iota(jnp.int32, particle_weight.shape, 2) < slot_counts[:, :, None]
    live_mass = jnp.where(live_slot, particle_weight.astype(jnp.float32), 0.0)
    packed = jnp.concatenate(
        [
            particle_phase,
            live_mass[:, :, None, :],
            cell_column.astype(jnp.float32)[:, :, None, :],
            cell_depth.astype(jnp.float32)[:, :, None, :],
            jnp.zeros_like(live_mass)[:, :, None, :],
        ],
        axis=2,
    ).reshape(devices, 8, slot_count)
    arrived = lax.all_to_all(packed, both, 0, 0, tiled=True)
    phase_in = arrived[:, 0:4, :]
    mass_in = arrived[:, 4, :]
    column_in = arrived[:, 5, :].astype(jnp.int32)
    depth_in = arrived[:, 6, :].astype(jnp.int32)
    sources = devices
    group_size = math.gcd(sources, max(1, 2048 // slot_count))
    step_count = sources // group_size
    block_rows = group_size * slot_count
    column_blocks = column_in.reshape(step_count, block_rows)
    depth_blocks = depth_in.reshape(step_count, block_rows)
    mass_blocks = mass_in.reshape(step_count, block_rows)
    column_ids = lax.broadcasted_iota(jnp.int32, (1, columns), 1)
    depth_ids = lax.broadcasted_iota(jnp.int32, (1, NZ), 1)

    def deposit(running, element):
        block_column, block_depth, block_mass = element
        picked = (block_column[:, None] == column_ids).astype(jnp.bfloat16)
        spread = jnp.where(
            block_depth[:, None] == depth_ids,
            block_mass.astype(jnp.bfloat16)[:, None],
            jnp.zeros((), jnp.bfloat16),
        )
        added = lax.dot_general(
            picked, spread, (((0,), (0,)), ((), ())), preferred_element_type=jnp.float32
        )
        return (running + added, None)

    density, unused = lax.scan(
        deposit, jnp.zeros((columns, NZ), jnp.float32), (column_blocks, depth_blocks, mass_blocks)
    )
    sine_x = sine_table(NX)
    sine_y = sine_table(NY)
    sine_z = sine_table(NZ)
    chunk_count = 2 if layers % 2 == 0 else 1
    chunk_layers = layers // chunk_count
    slab_index = lax.axis_index("row") * col_count + lax.axis_index("col")
    sine_z_slabs = sine_z.reshape(NZ, devices, layers)
    line_parts = []
    sine_z_parts = []
    sends = []
    for chunk in range(chunk_count):
        lower_layer = chunk * chunk_layers
        sine_z_part = sine_z_slabs[:, :, lower_layer : lower_layer + chunk_layers]
        sine_z_parts.append(sine_z_part)
        sends.append(
            lax.dot_general(sine_z_part, density, (((0,), (1,)), ((), ())), precision=high)
        )
    arrivals = [lax.all_to_all(sends[0], both, 0, 0, tiled=True)]
    if chunk_count > 1:
        arrivals.append(lax.all_to_all(sends[1], both, 0, 0, tiled=True))
    for chunk in range(chunk_count):
        lower_layer = chunk * chunk_layers
        slab_field = arrivals[chunk].reshape(row_count, col_count, chunk_layers, cells_x, cells_y)
        sine_y_blocks = sine_y.reshape(col_count, cells_y, NY)
        sine_x_blocks = sine_x.reshape(row_count, cells_x, NX)
        mixed = jnp.einsum("rczxy,cyl->zrxl", slab_field, sine_y_blocks, precision=high)
        mixed = jnp.einsum("zrxl,rxk->zkl", mixed, sine_x_blocks, precision=high)
        depth_wave = (
            slab_index * layers
            + lower_layer
            + lax.broadcasted_iota(jnp.int32, (chunk_layers,), 0)
        )
        depth_eigen = 2.0 - 2.0 * jnp.cos(
            (depth_wave.astype(jnp.float32) + 1.0) * (math.pi / (NZ + 1))
        )
        eigen_sum = (
            eigen_line(NX)[None, :, None]
            + eigen_line(NY)[None, None, :]
            + depth_eigen[:, None, None]
        )
        scaled = mixed / eigen_sum
        potential = jnp.einsum("zkl,rxk->zrxl", scaled, sine_x_blocks, precision=high)
        potential = jnp.einsum("zrxl,cyl->rczxy", potential, sine_y_blocks, precision=high)
        outgoing = potential.reshape(devices, chunk_layers, columns)
        returned = lax.all_to_all(outgoing, both, 0, 0, tiled=True)
        if chunk + 2 < chunk_count:
            upcoming, returned = lax.optimization_barrier((sends[chunk + 2], returned))
            arrivals.append(lax.all_to_all(upcoming, both, 0, 0, tiled=True))
        line_parts.append(
            lax.dot_general(
                returned, sine_z_parts[chunk], (((0, 1), (1, 2)), ((), ())), precision=high
            ).reshape(cells_x, cells_y, NZ)
        )
    def face(pick):
        return sum([pick(part) for part in line_parts[1:]], pick(line_parts[0]))

    line_grid = sum(line_parts[1:], line_parts[0])
    padded_x = jnp.concatenate(
        [
            shift_along(face(lambda part: part[cells_x - 1 :]), "row", True),
            line_grid,
            shift_along(face(lambda part: part[:1]), "row", False),
        ],
        axis=0,
    )
    padded_y = jnp.concatenate(
        [
            shift_along(face(lambda part: part[:, cells_y - 1 :]), "col", True),
            line_grid,
            shift_along(face(lambda part: part[:, :1]), "col", False),
        ],
        axis=1,
    )
    field_x = (-0.5 * (padded_x[2:] - padded_x[:-2])).reshape(columns, NZ)
    field_y = (-0.5 * (padded_y[:, 2:] - padded_y[:, :-2])).reshape(columns, NZ)
    found_x, found_y = lookup_fields(field_x, field_y, column_blocks, depth_blocks)
    momentum_x = phase_in[:, 1, :] + kick_strength * found_x.reshape(sources, slot_count)
    momentum_y = phase_in[:, 3, :] + kick_strength * found_y.reshape(sources, slot_count)
    kicked = jnp.stack([momentum_x, momentum_y], axis=1).reshape(
        row_count, col_count, 2, slot_count
    )
    coord_blocks = (
        phase_in[:, 0, :].reshape(step_count, block_rows),
        momentum_x.reshape(step_count, block_rows),
        phase_in[:, 2, :].reshape(step_count, block_rows),
        momentum_y.reshape(step_count, block_rows),
    )
    slice_blocks = (depth_in // (NZ // SLICES)).reshape(step_count, block_rows)
    slice_ids = lax.broadcasted_iota(jnp.int32, (1, SLICES), 1)

    def gather_moments(running, element):
        coord_one, coord_two, coord_three, coord_four, block_slice, block_mass = element
        weighted_slices = jnp.where(block_slice[:, None] == slice_ids, block_mass[:, None], 0.0)
        basis = monomials([coord_one, coord_two, coord_three, coord_four], ORDER)
        moment_part = jnp.dot(
            basis, weighted_slices, precision=highest, preferred_element_type=jnp.float32
        )
        square_part = jnp.sum(weighted_slices * block_mass[:, None], axis=0)
        return ((running[0] + moment_part, running[1] + square_part), None)

    start_state = (
        jnp.zeros((basis_count(ORDER), SLICES), jnp.float32),
        jnp.zeros((SLICES,), jnp.float32),
    )
    (moment_sum, square_sum), unused_too = lax.scan(
        gather_moments, start_state, coord_blocks + (slice_blocks, mass_blocks)
    )
    flat_totals = jnp.concatenate([moment_sum.reshape(-1), square_sum])
    piece = -(-flat_totals.shape[0] // (devices * 128)) * 128
    flat_totals = jnp.pad(flat_totals, (0, piece * devices - flat_totals.shape[0]))
    own_piece = jnp.sum(
        lax.all_to_all(flat_totals.reshape(devices, piece), both, 0, 0, tiled=True), axis=0
    )
    totals = lax.all_to_all(
        jnp.broadcast_to(own_piece[None, :], (devices, piece)), both, 0, 0, tiled=True
    ).reshape(-1)
    moment_count = moment_sum.shape[0] * SLICES
    moment_total = totals[:moment_count].reshape(moment_sum.shape)
    square_total = totals[moment_count : moment_count + SLICES]
    slice_moments = moment_total / jnp.sqrt(square_total + epsilon)[None, :]
    return (kicked, slice_moments)


def momentum_shape(phase_in):
    return (phase_in.shape[0], phase_in.shape[1], phase_in.shape[3])


def solution(mesh):
    placed = (
        P(("row", "col"), None, None, None),
        P(("row", "col"), None, None),
        P(("row", "col"), None, None),
        P(("row", "col"), None, None),
        P(("row", "col"), None),
    )
    return jax.shard_map(
        body,
        mesh=mesh,
        in_specs=placed,
        out_specs=(P(("row", "col"), None, None, None), P()),
        check_vma=False,
    )
```
